32 devices in a mesh: grp: 2 (over y), ctx: 2 (over core), tp: 8 (over z, x).
Axes of the slice: x: 2, y: 2, z: 4, core: 2. Of those that a mesh axis runs over, the one named last changes fastest.
Arguments:
- queries: bfloat16 [8192, 8, 192], P(('grp', 'ctx'), 'tp'), parts along dimension 0, may hold values from -70 to 70
- latent_rows: bfloat16 [8192, 576], P(('grp', 'ctx', 'tp')), parts along dimension 0, may hold values from -6 to 6
- doc_ids: int32 [8192], P(('grp', 'ctx', 'tp')), parts along dimension 0, may hold values from 0 to 7, as said below
- key_weight: bfloat16 [512, 1024], P(None, 'tp'), may hold values from -0.25 to 0.25
- value_weight: bfloat16 [512, 1024], P(None, 'tp'), may hold values from -0.25 to 0.25
Outputs:
- attended: bfloat16 [8192, 1024], P(('grp', 'ctx'), 'tp'), parts along dimension 0
The draws below stay inside these ranges and needn't reach their ends.
There are 2 independent parts, one for each index of `grp`. The reference program is written for one: setup_inputs(seed, part) draws one part's arguments, and reference() takes and returns one part's arrays. A program takes and returns all parts, laid end to end along the dimension named above; an argument that names none is the same for every part. Nothing has to cross between parts.
Inputs may be any that keep to these rules, and one draw needn't show every extreme that they name: `doc_ids`: never falling along the tokens.
All inputs are finite; a program needn't handle non-finite values.
Results may differ from the reference program's by a relative error of at most 0.0065.
Values may be sent and summed in bfloat16 or wider, within the bound.
No kernel may reach another device: no remote copies, remote signals or barrier semaphores. Data moves between devices by JAX's collectives and lax.ppermute only.
A program may use at most 64 MiB of HBM per device.

```python
import math
import jax
import jax.numpy as jnp
from jax import lax

KV_RANK = 512
ROPE_DIM = 64
NOPE_DIM = 128
V_DIM = 128
HEADS = 8
TOKENS = 4096
DOCS = 8


def draw_queries(key, part):
    shape = (TOKENS, HEADS, NOPE_DIM + ROPE_DIM)
    values = jnp.clip(jax.random.normal(jax.random.fold_in(key, 13), shape, jnp.float32), -4.0, 4.0)
    return values.astype(jnp.bfloat16)


def draw_latent_rows(key, part):
    shape = (TOKENS, KV_RANK + ROPE_DIM)
    values = jnp.clip(jax.random.normal(jax.random.fold_in(key, 23), shape, jnp.float32), -5.5, 5.5)
    return values.astype(jnp.bfloat16)


def draw_doc_ids(key, part):
    cuts = TOKENS // 4 + jax.random.randint(jax.random.fold_in(key, 31), (DOCS - 1,), 0, TOKENS - TOKENS // 4)
    index = jnp.arange(TOKENS, dtype=jnp.int32)
    return jnp.sum((index[:, None] >= cuts[None, :]).astype(jnp.int32), axis=1).astype(jnp.int32)


def steps_of(key, dims, shards, low, high):
    gain, own = 1.0, jax.random.fold_in(key, 6)
    for axis_at, shards_of in shards:
        steps = jnp.exp(jax.random.uniform(jax.random.fold_in(own, axis_at), (shards_of,), jnp.float32, low / len(shards), high / len(shards)))
        gain = gain * jnp.repeat(steps, dims[axis_at] // shards_of).reshape([-1 if axis == axis_at else 1 for axis in range(len(dims))])
    return gain


def normal_values(stream_key, dims, width, limit, split=(), kind=jnp.bfloat16):
    drawn = width * jax.random.normal(stream_key, dims, jnp.float32)
    if split:
        drawn = drawn * steps_of(stream_key, dims, split, -0.22, 0.18)
    return jnp.clip(drawn, -limit, limit).astype(kind)


def setup_inputs(seed: int = 0, part: int = 0) -> dict:
    streams_of = jax.random.split(jax.random.key(seed), 6)
    own_keys = jax.random.split(jax.random.fold_in(streams_of[5], part), 6)
    return {
        "queries": draw_queries(jax.random.fold_in(jax.random.fold_in(streams_of[5], part), 71), part),
        "latent_rows": draw_latent_rows(jax.random.fold_in(jax.random.fold_in(streams_of[5], part), 71), part),
        "doc_ids": draw_doc_ids(jax.random.fold_in(jax.random.fold_in(streams_of[5], part), 71), part),
        "key_weight": normal_values(streams_of[3], (KV_RANK, HEADS * NOPE_DIM), KV_RANK ** -0.5, 0.25, ((1, 8),)),
        "value_weight": normal_values(streams_of[4], (KV_RANK, HEADS * V_DIM), KV_RANK ** -0.5, 0.25, ((1, 8),)),
    }


def reference(queries, latent_rows, doc_ids, key_weight, value_weight):
    latent_part = latent_rows[:, :KV_RANK]
    rope_part = latent_rows[:, KV_RANK:]
    key_heads = jnp.dot(latent_part, key_weight, preferred_element_type=jnp.float32).astype(jnp.bfloat16)
    value_heads = jnp.dot(latent_part, value_weight, preferred_element_type=jnp.float32).astype(jnp.bfloat16)
    key_heads = jnp.transpose(key_heads.reshape(TOKENS, HEADS, NOPE_DIM), (1, 0, 2))
    value_heads = jnp.transpose(value_heads.reshape(TOKENS, HEADS, V_DIM), (1, 0, 2))
    query_heads = jnp.transpose(queries, (1, 0, 2))
    position = jnp.arange(TOKENS, dtype=jnp.int32)
    visible = (position[None, :] <= position[:, None]) & (doc_ids[None, :] == doc_ids[:, None])
    factor = 1.0 / math.sqrt(NOPE_DIM + ROPE_DIM)

    def per_head(packed):
        query_one, key_one, value_one = packed
        scores = jnp.dot(query_one[:, :NOPE_DIM], key_one.T, preferred_element_type=jnp.float32)
        scores = scores + jnp.dot(query_one[:, NOPE_DIM:], rope_part.T, preferred_element_type=jnp.float32)
        scores = scores * factor
        scores = jnp.where(visible, scores, jnp.float32(-1e+30))
        maxima = lax.optimization_barrier(jnp.max(scores, axis=1, keepdims=True))
        weights = jnp.where(visible, jnp.exp(scores - maxima), jnp.float32(0.0))
        totals = lax.optimization_barrier(jnp.sum(weights, axis=1))
        summed = jnp.dot(weights.astype(jnp.bfloat16), value_one, preferred_element_type=jnp.float32)
        return (summed / totals[:, None]).astype(jnp.bfloat16)
    result = lax.map(per_head, (query_heads, key_heads, value_heads))
    return jnp.transpose(result, (1, 0, 2)).reshape(TOKENS, HEADS * V_DIM)
```

```python
import functools
import math

import jax
import jax.numpy as jnp
from jax import lax
from jax.experimental import pallas as pl
from jax.experimental.pallas import tpu as pltpu
from jax.sharding import PartitionSpec as P

KV_RANK = 512
ROPE_DIM = 64
NOPE_DIM = 128
BLOCK_Q = 512
BLOCK_K = 512
FAR = 1 << 30


def passed_along(block, axis, distance):
    devices = range(lax.axis_size(axis))
    route = [(i - distance, i) for i in devices if i - distance in devices]
    return lax.ppermute(block, axis, route)


def flash_kernel(
    lo_ref, hi_ref, qpos_ref, kpos_ref, qdl_ref, kdf_ref,
    q_ref, k_ref, r_ref, v_ref, qd_ref, kd_ref,
    o_ref,
    m_sc, l_sc, acc_sc,
    *, steps, factor,
):
    qt = pl.program_id(1)
    s = pl.program_id(2)
    lo = lo_ref[qt]
    hi = hi_ref[qt]
    kt = jnp.minimum(lo + s, hi)
    bq = q_ref.shape[0]
    bk = k_ref.shape[0]

    @pl.when(s == 0)
    def _():
        m_sc[...] = jnp.full(m_sc.shape, -1e30, jnp.float32)
        l_sc[...] = jnp.zeros(l_sc.shape, jnp.float32)
        acc_sc[...] = jnp.zeros(acc_sc.shape, jnp.float32)

    def tile(masked):
        q = q_ref[...]
        nt = (((1,), (1,)), ((), ()))
        scores = lax.dot_general(
            q[:, :NOPE_DIM], k_ref[...], nt, preferred_element_type=jnp.float32
        )
        scores = scores + lax.dot_general(
            q[:, NOPE_DIM:], r_ref[...], nt, preferred_element_type=jnp.float32
        )
        scores = scores * factor
        if masked:
            qpos = qpos_ref[qt] + lax.broadcasted_iota(jnp.int32, (bq, 1), 0)
            kpos = kpos_ref[kt] + lax.broadcasted_iota(jnp.int32, (1, bk), 1)
            visible = (kpos <= qpos) & (kd_ref[...] == qd_ref[...])
            scores = jnp.where(visible, scores, jnp.float32(-1e30))
        m_prev = m_sc[...]
        m_new = jnp.maximum(m_prev, jnp.max(scores, axis=1, keepdims=True))
        alpha = jnp.exp(m_prev - m_new)
        weights = jnp.exp(scores - m_new)
        if masked:
            weights = jnp.where(visible, weights, jnp.float32(0.0))
        l_sc[...] = alpha * l_sc[...] + jnp.sum(weights, axis=1, keepdims=True)
        acc_sc[...] = alpha * acc_sc[...] + jnp.dot(
            weights.astype(jnp.bfloat16), v_ref[...], preferred_element_type=jnp.float32
        )
        m_sc[...] = m_new

    run = lo + s <= hi
    full = (kpos_ref[kt] + bk - 1 <= qpos_ref[qt]) & (kdf_ref[kt] == qdl_ref[qt])

    @pl.when(run & full)
    def _():
        tile(False)

    @pl.when(run & jnp.logical_not(full))
    def _():
        tile(True)

    @pl.when(s == steps - 1)
    def _():
        o_ref[...] = (acc_sc[...] / l_sc[...]).astype(o_ref.dtype)


def flash(query_heads, keys, ropes, values, query_docs, key_docs, qpos0, kpos0):
    heads_here, rows, _ = query_heads.shape
    count = keys.shape[0]
    value_width = values.shape[1] // heads_here
    bq = min(BLOCK_Q, rows)
    bk = min(BLOCK_K, count)
    q_tiles = rows // bq
    k_tiles = count // bk
    qdf = query_docs[::bq]
    qdl = query_docs[bq - 1 :: bq]
    kdf = key_docs[::bk]
    kdl = key_docs[bk - 1 :: bk]
    active = (kpos0[None, :] <= qpos0[:, None] + (bq - 1)) & (kdl[None, :] >= qdf[:, None])
    index = jnp.arange(k_tiles, dtype=jnp.int32)
    lo = jnp.min(jnp.where(active, index[None, :], k_tiles), axis=1).astype(jnp.int32)
    hi = jnp.max(jnp.where(active, index[None, :], -1), axis=1).astype(jnp.int32)

    def key_map(h, qt, s, lo_ref, hi_ref, *_):
        return (jnp.minimum(lo_ref[qt] + s, hi_ref[qt]), h)

    def rope_map(h, qt, s, lo_ref, hi_ref, *_):
        return (jnp.minimum(lo_ref[qt] + s, hi_ref[qt]), 0)

    def kdoc_map(h, qt, s, lo_ref, hi_ref, *_):
        return (0, jnp.minimum(lo_ref[qt] + s, hi_ref[qt]))

    kernel = functools.partial(
        flash_kernel, steps=k_tiles, factor=1.0 / math.sqrt(NOPE_DIM + ROPE_DIM)
    )
    grid_spec = pltpu.PrefetchScalarGridSpec(
        num_scalar_prefetch=6,
        grid=(heads_here, q_tiles, k_tiles),
        in_specs=[
            pl.BlockSpec((None, bq, query_heads.shape[2]), lambda h, qt, s, *_: (h, qt, 0)),
            pl.BlockSpec((bk, NOPE_DIM), key_map),
            pl.BlockSpec((bk, ROPE_DIM), rope_map),
            pl.BlockSpec((bk, value_width), key_map),
            pl.BlockSpec((bq, 1), lambda h, qt, s, *_: (qt, 0)),
            pl.BlockSpec((1, bk), kdoc_map),
        ],
        out_specs=pl.BlockSpec((bq, value_width), lambda h, qt, s, *_: (qt, h)),
        scratch_shapes=[
            pltpu.VMEM((bq, 1), jnp.float32),
            pltpu.VMEM((bq, 1), jnp.float32),
            pltpu.VMEM((bq, value_width), jnp.float32),
        ],
    )
    return pl.pallas_call(
        kernel,
        grid_spec=grid_spec,
        out_shape=jax.ShapeDtypeStruct((rows, heads_here * value_width), jnp.bfloat16),
        compiler_params=pltpu.CompilerParams(
            dimension_semantics=("arbitrary", "arbitrary", "arbitrary")
        ),
    )(
        lo, hi, qpos0, kpos0, qdl, kdf,
        query_heads, keys, ropes, values,
        query_docs.reshape(rows, 1), key_docs.reshape(1, count),
    )


def body(queries, latent_rows, doc_ids, key_weight, value_weight):
    block_rows = queries.shape[0]
    cycle_size = lax.axis_size("ctx")
    cycle_index = lax.axis_index("ctx")
    gathered, own_docs = (
        lax.all_gather(latent_rows, "tp", axis=0, tiled=True),
        lax.all_gather(doc_ids, "tp", axis=0, tiled=True),
    )
    latent_part = gathered[:, :KV_RANK]
    key_heads = jnp.dot(latent_part, key_weight, preferred_element_type=jnp.float32).astype(
        jnp.bfloat16
    )
    value_heads = jnp.dot(latent_part, value_weight, preferred_element_type=jnp.float32).astype(
        jnp.bfloat16
    )
    rope_keys = gathered[:, KV_RANK:]
    local = (key_heads, value_heads, rope_keys, own_docs)
    sets = []
    for distance in range(cycle_size - 1, 0, -1):
        sets.append(passed_along(local, "ctx", distance))
    sets.append(local)
    keys = jnp.concatenate([entry[0] for entry in sets], axis=0)
    values = jnp.concatenate([entry[1] for entry in sets], axis=0)
    ropes = jnp.concatenate([entry[2] for entry in sets], axis=0)
    key_docs = jnp.concatenate([entry[3] for entry in sets], axis=0)

    bq = min(BLOCK_Q, block_rows)
    bk = min(BLOCK_K, block_rows)
    qpos0 = cycle_index * block_rows + jnp.arange(0, block_rows, bq, dtype=jnp.int32)
    starts = []
    for number in range(cycle_size):
        source = cycle_index - (cycle_size - 1) + number
        tile_starts = source * block_rows + jnp.arange(0, block_rows, bk, dtype=jnp.int32)
        starts.append(jnp.where(source >= 0, tile_starts, FAR))
    kpos0 = jnp.concatenate(starts, axis=0)

    query_heads = jnp.transpose(queries, (1, 0, 2))
    return flash(query_heads, keys, ropes, values, own_docs, key_docs, qpos0, kpos0)


def solution(mesh):
    placed = (
        P(("grp", "ctx"), "tp", None),
        P(("grp", "ctx", "tp"), None),
        P(("grp", "ctx", "tp")),
        P(None, "tp"),
        P(None, "tp"),
    )
    return jax.shard_map(
        body, mesh=mesh, in_specs=placed, out_specs=P(("grp", "ctx"), "tp"), check_vma=False
    )
```

```python
import functools
import math

import jax
import numpy as np
import jax.numpy as jnp
from jax import lax
from jax.experimental import pallas as pl
from jax.experimental.pallas import tpu as pltpu
from jax.sharding import PartitionSpec as P

KV_RANK = 512
ROPE_DIM = 64
NOPE_DIM = 128
BLOCK_Q = 512
BLOCK_K = 512
FAR = 1 << 30


def passed_along(block, axis, distance):
    devices = range(lax.axis_size(axis))
    route = [(i - distance, i) for i in devices if i - distance in devices]
    return lax.ppermute(block, axis, route)


def flash_kernel(
    lo_ref, hi_ref, qpos_ref, kpos_ref, qdl_ref, kdf_ref,
    q_ref, k_ref, r_ref, v_ref, qd_ref, kd_ref,
    o_ref,
    m_sc, l_sc, acc_sc,
    *, steps, factor,
):
    qt = pl.program_id(1)
    s = pl.program_id(2)
    lo = lo_ref[qt]
    hi = hi_ref[qt]
    kt = jnp.minimum(lo + s, hi)
    bq = q_ref.shape[0]
    bk = k_ref.shape[0]

    @pl.when(s == 0)
    def _():
        m_sc[...] = jnp.full(m_sc.shape, -1e30, jnp.float32)
        l_sc[...] = jnp.zeros(l_sc.shape, jnp.float32)
        acc_sc[...] = jnp.zeros(acc_sc.shape, jnp.float32)

    def tile(masked):
        q = q_ref[...]
        nt = (((1,), (1,)), ((), ()))
        scores = lax.dot_general(
            q[:, :NOPE_DIM], k_ref[...], nt, preferred_element_type=jnp.float32
        )
        scores = scores + lax.dot_general(
            q[:, NOPE_DIM:], r_ref[...], nt, preferred_element_type=jnp.float32
        )
        scores = scores * factor
        if masked:
            qpos = qpos_ref[qt] + lax.broadcasted_iota(jnp.int32, (bq, 1), 0)
            kpos = kpos_ref[kt] + lax.broadcasted_iota(jnp.int32, (1, bk), 1)
            visible = (kpos <= qpos) & (kd_ref[...] == qd_ref[...])
            scores = jnp.where(visible, scores, jnp.float32(-1e30))
        m_prev = m_sc[...]
        m_new = jnp.maximum(m_prev, jnp.max(scores, axis=1, keepdims=True))
        alpha = jnp.exp(m_prev - m_new)
        weights = jnp.exp(scores - m_new)
        if masked:
            weights = jnp.where(visible, weights, jnp.float32(0.0))
        l_sc[...] = alpha * l_sc[...] + jnp.sum(weights, axis=1, keepdims=True)
        acc_sc[...] = alpha * acc_sc[...] + jnp.dot(
            weights.astype(jnp.bfloat16), v_ref[...], preferred_element_type=jnp.float32
        )
        m_sc[...] = m_new

    run = lo + s <= hi
    full = (kpos_ref[kt] + bk - 1 <= qpos_ref[qt]) & (kdf_ref[kt] == qdl_ref[qt])

    @pl.when(run & full)
    def _():
        tile(False)

    @pl.when(run & jnp.logical_not(full))
    def _():
        tile(True)

    @pl.when(s == steps - 1)
    def _():
        o_ref[...] = (acc_sc[...] / l_sc[...]).astype(o_ref.dtype)


def flash(query_heads, keys, ropes, values, query_docs, key_docs, qpos0, kpos0):
    heads_here, rows, _ = query_heads.shape
    count = keys.shape[0]
    value_width = values.shape[1] // heads_here
    bq = min(BLOCK_Q, rows)
    bk = min(BLOCK_K, count)
    q_tiles = rows // bq
    k_tiles = count // bk
    qdf = query_docs[::bq]
    qdl = query_docs[bq - 1 :: bq]
    kdf = key_docs[::bk]
    kdl = key_docs[bk - 1 :: bk]
    active = (kpos0[None, :] <= qpos0[:, None] + (bq - 1)) & (kdl[None, :] >= qdf[:, None])
    index = jnp.arange(k_tiles, dtype=jnp.int32)
    lo = jnp.min(jnp.where(active, index[None, :], k_tiles), axis=1).astype(jnp.int32)
    hi = jnp.max(jnp.where(active, index[None, :], -1), axis=1).astype(jnp.int32)

    def key_map(h, qt, s, lo_ref, hi_ref, *_):
        return (jnp.minimum(lo_ref[qt] + s, hi_ref[qt]), h)

    def rope_map(h, qt, s, lo_ref, hi_ref, *_):
        return (jnp.minimum(lo_ref[qt] + s, hi_ref[qt]), 0)

    def kdoc_map(h, qt, s, lo_ref, hi_ref, *_):
        return (0, jnp.minimum(lo_ref[qt] + s, hi_ref[qt]))

    kernel = functools.partial(
        flash_kernel, steps=k_tiles, factor=1.0 / math.sqrt(NOPE_DIM + ROPE_DIM)
    )
    grid_spec = pltpu.PrefetchScalarGridSpec(
        num_scalar_prefetch=6,
        grid=(heads_here, q_tiles, k_tiles),
        in_specs=[
            pl.BlockSpec((None, bq, query_heads.shape[2]), lambda h, qt, s, *_: (h, qt, 0)),
            pl.BlockSpec((bk, NOPE_DIM), key_map),
            pl.BlockSpec((bk, ROPE_DIM), rope_map),
            pl.BlockSpec((bk, value_width), key_map),
            pl.BlockSpec((bq, 1), lambda h, qt, s, *_: (qt, 0)),
            pl.BlockSpec((1, bk), kdoc_map),
        ],
        out_specs=pl.BlockSpec((bq, value_width), lambda h, qt, s, *_: (qt, h)),
        scratch_shapes=[
            pltpu.VMEM((bq, 1), jnp.float32),
            pltpu.VMEM((bq, 1), jnp.float32),
            pltpu.VMEM((bq, value_width), jnp.float32),
        ],
    )
    return pl.pallas_call(
        kernel,
        grid_spec=grid_spec,
        out_shape=jax.ShapeDtypeStruct((rows, heads_here * value_width), jnp.bfloat16),
        compiler_params=pltpu.CompilerParams(
            dimension_semantics=("arbitrary", "arbitrary", "arbitrary")
        ),
    )(
        lo, hi, qpos0, kpos0, qdl, kdf,
        query_heads, keys, ropes, values,
        query_docs.reshape(rows, 1), key_docs.reshape(1, count),
    )


def ring_gather(block, docs, order):
    count = len(order)
    place = {device: number for number, device in enumerate(order)}
    forward = [(order[i], order[(i + 1) % count]) for i in range(count)]
    backward = [(order[(i + 1) % count], order[i]) for i in range(count)]
    ahead = count // 2
    behind = count - 1 - ahead
    arrived = [(block, docs)]
    sources = [[device for device in range(count)]]
    moving_f = (block, docs)
    moving_b = (block, docs)
    for step in range(1, ahead + 1):
        moving_f = lax.ppermute(moving_f, "tp", forward)
        arrived.append(moving_f)
        sources.append([order[(place[d] - step) % count] for d in range(count)])
        if step <= behind:
            moving_b = lax.ppermute(moving_b, "tp", backward)
            arrived.append(moving_b)
            sources.append([order[(place[d] + step) % count] for d in range(count)])
    table = np.zeros((count, count), np.int32)
    for number, row in enumerate(sources):
        for device, source in enumerate(row):
            table[device, source] = number
    me = lax.axis_index("tp")
    pick = jnp.asarray(table)[me]
    stacked = jnp.stack([entry[0] for entry in arrived], axis=0)
    stacked_docs = jnp.stack([entry[1] for entry in arrived], axis=0)
    rows = block.shape[0]
    gathered = jnp.take(stacked, pick, axis=0).reshape(count * rows, block.shape[1])
    gathered_docs = jnp.take(stacked_docs, pick, axis=0).reshape(count * rows)
    return gathered, gathered_docs


def body(queries, latent_rows, doc_ids, key_weight, value_weight, *, order):
    block_rows = queries.shape[0]
    cycle_size = lax.axis_size("ctx")
    cycle_index = lax.axis_index("ctx")
    gathered, own_docs = ring_gather(latent_rows, doc_ids, order)
    latent_part = gathered[:, :KV_RANK]
    key_heads = jnp.dot(latent_part, key_weight, preferred_element_type=jnp.float32).astype(
        jnp.bfloat16
    )
    value_heads = jnp.dot(latent_part, value_weight, preferred_element_type=jnp.float32).astype(
        jnp.bfloat16
    )
    rope_keys = gathered[:, KV_RANK:]
    local = (key_heads, value_heads, rope_keys, own_docs)
    sets = []
    for distance in range(cycle_size - 1, 0, -1):
        sets.append(passed_along(local, "ctx", distance))
    sets.append(local)
    keys = jnp.concatenate([entry[0] for entry in sets], axis=0)
    values = jnp.concatenate([entry[1] for entry in sets], axis=0)
    ropes = jnp.concatenate([entry[2] for entry in sets], axis=0)
    key_docs = jnp.concatenate([entry[3] for entry in sets], axis=0)

    bq = min(BLOCK_Q, block_rows)
    bk = min(BLOCK_K, block_rows)
    qpos0 = cycle_index * block_rows + jnp.arange(0, block_rows, bq, dtype=jnp.int32)
    starts = []
    for number in range(cycle_size):
        source = cycle_index - (cycle_size - 1) + number
        tile_starts = source * block_rows + jnp.arange(0, block_rows, bk, dtype=jnp.int32)
        starts.append(jnp.where(source >= 0, tile_starts, FAR))
    kpos0 = jnp.concatenate(starts, axis=0)

    query_heads = jnp.transpose(queries, (1, 0, 2))
    return flash(query_heads, keys, ropes, values, own_docs, key_docs, qpos0, kpos0)


def ring_order(mesh):
    line = list(mesh.devices[(0,) * (mesh.devices.ndim - 1)].reshape(-1))
    try:
        where = {(d.coords[0], d.coords[2]): number for number, d in enumerate(line)}
        xs = sorted({key[0] for key in where})
        zs = sorted({key[1] for key in where})
        order = []
        for turn, x in enumerate(xs):
            for z in zs if turn % 2 == 0 else zs[::-1]:
                order.append(where[(x, z)])
    except (AttributeError, KeyError, IndexError, TypeError):
        return list(range(len(line)))
    if sorted(order) != list(range(len(line))):
        return list(range(len(line)))
    return order


def solution(mesh):
    placed = (
        P(("grp", "ctx"), "tp", None),
        P(("grp", "ctx", "tp"), None),
        P(("grp", "ctx", "tp")),
        P(None, "tp"),
        P(None, "tp"),
    )
    return jax.shard_map(
        functools.partial(body, order=ring_order(mesh)), mesh=mesh, in_specs=placed, out_specs=P(("grp", "ctx"), "tp"), check_vma=False
    )
```

```python
import functools
import math

import jax
import jax.numpy as jnp
import numpy as np
from jax import lax
from jax.experimental import pallas as pl
from jax.experimental.pallas import tpu as pltpu
from jax.sharding import PartitionSpec as P

KV_RANK = 512
ROPE_DIM = 64
NOPE_DIM = 128
LANES = 128
BLOCK_Q = 256
BLOCK_K = 256
FAR = 1 << 30


def flash_kernel(
    qbase_ref, qdf_ref, qdl_ref, kminp_ref, kmaxp_ref, kmind_ref, kmaxd_ref,
    q_ref, *rest, sets, tiles, factor,
):
    set_refs = [rest[5 * n : 5 * n + 5] for n in range(sets)]
    qd_ref, o_ref = rest[5 * sets], rest[5 * sets + 1]
    qt = pl.program_id(1)
    bq = q_ref.shape[0]
    bk = BLOCK_K
    first_pos = qbase_ref[0] + qt * bq
    last_pos = first_pos + (bq - 1)
    first_doc = qdf_ref[qt]
    last_doc = qdl_ref[qt]
    q = q_ref[...]
    q_nope = q[:, :NOPE_DIM]
    q_rope = q[:, NOPE_DIM:]
    q_pos = first_pos + lax.broadcasted_iota(jnp.int32, (bq, 1), 0)
    q_doc = qd_ref[...]
    nt = (((1,), (1,)), ((), ()))

    def make_step(number, k_ref, v_ref, r_ref, kp_ref, kd_ref):
        def tile(masked, t, carry):
            m_prev, l_prev, acc_prev = carry
            start = pl.multiple_of(t * bk, bk)
            keys = k_ref[pl.ds(start, bk), :]
            ropes = r_ref[pl.ds(start, bk), :]
            scores = lax.dot_general(q_nope, keys, nt, preferred_element_type=jnp.float32)
            scores = scores + lax.dot_general(
                q_rope, ropes[:, :ROPE_DIM], nt, preferred_element_type=jnp.float32
            )
            scores = scores * factor
            if masked:
                k_pos = kp_ref[:, pl.ds(start, bk)]
                k_doc = kd_ref[:, pl.ds(start, bk)]
                visible = (k_pos <= q_pos) & (k_doc == q_doc)
                scores = jnp.where(visible, scores, jnp.float32(-1e30))
            m_new = jnp.maximum(m_prev, jnp.max(scores, axis=1, keepdims=True))
            alpha = jnp.exp(m_prev - m_new)
            weights = jnp.exp(scores - m_new)
            if masked:
                weights = jnp.where(visible, weights, jnp.float32(0.0))
            l_new = alpha * l_prev + jnp.sum(weights, axis=1, keepdims=True)
            acc_new = alpha * acc_prev + jnp.dot(
                weights.astype(jnp.bfloat16),
                v_ref[pl.ds(start, bk), :],
                preferred_element_type=jnp.float32,
            )
            return (m_new, l_new, acc_new)

        def step(t, carry):
            at = number * tiles + t
            active = (
                (kminp_ref[at] <= last_pos)
                & (kmaxd_ref[at] >= first_doc)
                & (kmind_ref[at] <= last_doc)
            )
            full = (
                (kmaxp_ref[at] <= first_pos)
                & (kmind_ref[at] == last_doc)
                & (kmaxd_ref[at] == first_doc)
            )
            mode = jnp.where(active, jnp.where(full, 2, 1), 0)
            return lax.switch(
                mode,
                [
                    lambda t, c: c,
                    functools.partial(tile, True),
                    functools.partial(tile, False),
                ],
                t,
                carry,
            )

        return step

    carry = (
        jnp.full((bq, 1), -1e30, jnp.float32),
        jnp.zeros((bq, 1), jnp.float32),
        jnp.zeros((bq, o_ref.shape[1]), jnp.float32),
    )
    for number, refs in enumerate(set_refs):
        carry = lax.fori_loop(0, tiles, make_step(number, *refs), carry)
    _, totals, summed = carry
    o_ref[...] = (summed / totals).astype(o_ref.dtype)


def flash(query_heads, packs, positions, docs_rows, query_docs, query_base):
    heads_here, rows, _ = query_heads.shape
    count = packs[0].shape[0]
    bq = min(BLOCK_Q, rows)
    bk = BLOCK_K
    q_tiles = rows // bq
    tiles = count // bk
    sets = len(packs)
    qdf = query_docs[::bq]
    qdl = query_docs[bq - 1 :: bq]
    pos_tiles = jnp.concatenate(positions, axis=0).reshape(sets * tiles, bk)
    doc_tiles = jnp.concatenate(docs_rows, axis=0).reshape(sets * tiles, bk)
    kminp = jnp.min(pos_tiles, axis=1)
    kmaxp = jnp.max(pos_tiles, axis=1)
    kmind = jnp.min(doc_tiles, axis=1)
    kmaxd = jnp.max(doc_tiles, axis=1)

    whole = lambda width: pl.BlockSpec((count, width), lambda h, qt, *_: (0, 0))
    in_specs = [pl.BlockSpec((None, bq, query_heads.shape[2]), lambda h, qt, *_: (h, qt, 0))]
    operands = [query_heads]
    for pack, pos, doc in zip(packs, positions, docs_rows):
        in_specs += [
            pl.BlockSpec((count, LANES), lambda h, qt, *_: (0, h)),
            pl.BlockSpec((count, LANES), lambda h, qt, *_: (0, heads_here + h)),
            pl.BlockSpec((count, LANES), lambda h, qt, *_: (0, 2 * heads_here)),
            pl.BlockSpec((1, count), lambda h, qt, *_: (0, 0)),
            pl.BlockSpec((1, count), lambda h, qt, *_: (0, 0)),
        ]
        operands += [pack, pack, pack, pos.reshape(1, count), doc.reshape(1, count)]
    in_specs.append(pl.BlockSpec((bq, 1), lambda h, qt, *_: (qt, 0)))
    operands.append(query_docs.reshape(rows, 1))
    del whole

    kernel = functools.partial(
        flash_kernel, sets=sets, tiles=tiles, factor=1.0 / math.sqrt(NOPE_DIM + ROPE_DIM)
    )
    grid_spec = pltpu.PrefetchScalarGridSpec(
        num_scalar_prefetch=7,
        grid=(heads_here, q_tiles),
        in_specs=in_specs,
        out_specs=pl.BlockSpec((bq, LANES), lambda h, qt, *_: (qt, h)),
    )
    return pl.pallas_call(
        kernel,
        grid_spec=grid_spec,
        out_shape=jax.ShapeDtypeStruct((rows, heads_here * LANES), jnp.bfloat16),
        compiler_params=pltpu.CompilerParams(dimension_semantics=("arbitrary", "arbitrary")),
    )(query_base, qdf, qdl, kminp, kmaxp, kmind, kmaxd, *operands)


def ring_gather(block, order):
    count = len(order)
    place = {device: number for number, device in enumerate(order)}
    forward = [(order[i], order[(i + 1) % count]) for i in range(count)]
    backward = [(order[(i + 1) % count], order[i]) for i in range(count)]
    ahead = count // 2
    behind = count - 1 - ahead
    arrived = [block]
    sources = [list(range(count))]
    moving_f = block
    moving_b = block
    for step in range(1, ahead + 1):
        moving_f = lax.ppermute(moving_f, "tp", forward)
        arrived.append(moving_f)
        sources.append([order[(place[d] - step) % count] for d in range(count)])
        if step <= behind:
            moving_b = lax.ppermute(moving_b, "tp", backward)
            arrived.append(moving_b)
            sources.append([order[(place[d] + step) % count] for d in range(count)])
    source_of = np.zeros((count, count), np.int32)
    slot_of = np.zeros((count, count), np.int32)
    for number, row in enumerate(sources):
        for device, source in enumerate(row):
            source_of[device, number] = source
            slot_of[device, source] = number
    me = lax.axis_index("tp")
    return (
        jnp.concatenate(arrived, axis=0),
        jnp.asarray(source_of)[me],
        jnp.asarray(slot_of)[me],
    )


def body(queries, latent_rows, doc_ids, key_weight, value_weight, *, order):
    block_rows = queries.shape[0]
    chunk_rows = latent_rows.shape[0]
    chunks = block_rows // chunk_rows
    cycle_size = lax.axis_size("ctx")
    cycle_index = lax.axis_index("ctx")
    heads_here = key_weight.shape[1] // NOPE_DIM
    width = latent_rows.shape[1]
    pad = (-(width + 1)) % LANES
    doc_column = jnp.concatenate(
        [doc_ids.astype(jnp.bfloat16)[:, None], jnp.zeros((chunk_rows, pad), jnp.bfloat16)],
        axis=1,
    )
    chunk = jnp.concatenate([latent_rows, doc_column], axis=1)
    gathered, source_of, slot_of = ring_gather(chunk, order)
    latent_part = gathered[:, :KV_RANK]
    key_heads = jnp.dot(latent_part, key_weight, preferred_element_type=jnp.float32).astype(
        jnp.bfloat16
    )
    value_heads = jnp.dot(latent_part, value_weight, preferred_element_type=jnp.float32).astype(
        jnp.bfloat16
    )
    pack = jnp.concatenate([key_heads, value_heads, gathered[:, KV_RANK:]], axis=1)
    docs = gathered[:, width].astype(jnp.int32)
    offsets = (
        source_of[:, None] * chunk_rows + jnp.arange(chunk_rows, dtype=jnp.int32)[None, :]
    ).reshape(block_rows)
    query_docs = jnp.take(docs.reshape(chunks, chunk_rows), slot_of, axis=0).reshape(block_rows)

    packs, positions, docs_rows = [], [], []
    for distance in range(cycle_size - 1, 0, -1):
        route = [(i - distance, i) for i in range(cycle_size) if i - distance >= 0]
        moved = lax.ppermute(pack, "ctx", route)
        source = cycle_index - distance
        packs.append(moved)
        positions.append(jnp.where(source >= 0, source * block_rows + offsets, FAR))
        docs_rows.append(moved[:, 2 * heads_here * NOPE_DIM + ROPE_DIM].astype(jnp.int32))
    packs.append(pack)
    positions.append(cycle_index * block_rows + offsets)
    docs_rows.append(docs)

    query_heads = jnp.transpose(queries, (1, 0, 2))
    query_base = (cycle_index * block_rows).astype(jnp.int32).reshape(1)
    return flash(query_heads, packs, positions, docs_rows, query_docs, query_base)


def ring_order(mesh):
    line = list(mesh.devices[(0,) * (mesh.devices.ndim - 1)].reshape(-1))
    try:
        where = {(d.coords[0], d.coords[2]): number for number, d in enumerate(line)}
        xs = sorted({key[0] for key in where})
        zs = sorted({key[1] for key in where})
        order = []
        for turn, x in enumerate(xs):
            for z in zs if turn % 2 == 0 else zs[::-1]:
                order.append(where[(x, z)])
    except (AttributeError, KeyError, IndexError, TypeError):
        return list(range(len(line)))
    if sorted(order) != list(range(len(line))):
        return list(range(len(line)))
    return order


def solution(mesh):
    placed = (
        P(("grp", "ctx"), "tp", None),
        P(("grp", "ctx", "tp"), None),
        P(("grp", "ctx", "tp")),
        P(None, "tp"),
        P(None, "tp"),
    )
    return jax.shard_map(
        functools.partial(body, order=ring_order(mesh)),
        mesh=mesh,
        in_specs=placed,
        out_specs=P(("grp", "ctx"), "tp"),
        check_vma=False,
    )
```

```python
import functools
import math

import jax
import jax.numpy as jnp
import numpy as np
from jax import lax
from jax.experimental import pallas as pl
from jax.experimental.pallas import tpu as pltpu
from jax.sharding import PartitionSpec as P

KV_RANK = 512
ROPE_DIM = 64
NOPE_DIM = 128
LANES = 128
BLOCK_Q = 256
BLOCK_K = 256
FAR = 1 << 30


def flash_kernel(
    qbase_ref, qdf_ref, qdl_ref, kminp_ref, kmaxp_ref, kmind_ref, kmaxd_ref,
    q_ref, *rest, sets, tiles, factor,
):
    set_refs = [rest[5 * n : 5 * n + 5] for n in range(sets)]
    qd_ref, o_ref = rest[5 * sets], rest[5 * sets + 1]
    qt = pl.program_id(1)
    bq = q_ref.shape[0]
    bk = BLOCK_K
    first_pos = qbase_ref[0] + qt * bq
    last_pos = first_pos + (bq - 1)
    first_doc = qdf_ref[qt]
    last_doc = qdl_ref[qt]
    q = q_ref[...]
    q_nope = q[:, :NOPE_DIM]
    q_rope = q[:, NOPE_DIM:]
    q_pos = first_pos + lax.broadcasted_iota(jnp.int32, (bq, 1), 0)
    q_doc = qd_ref[...]
    nt = (((1,), (1,)), ((), ()))

    m_sc, l_sc, acc_sc = rest[5 * sets + 2 :]
    m_sc[...] = jnp.full(m_sc.shape, -1e30, jnp.float32)
    l_sc[...] = jnp.zeros(l_sc.shape, jnp.float32)
    acc_sc[...] = jnp.zeros(acc_sc.shape, jnp.float32)

    def make_step(number, k_ref, v_ref, r_ref, kp_ref, kd_ref):
        def tile(masked, t):
            start = pl.multiple_of(t * bk, bk)
            keys = k_ref[pl.ds(start, bk), :]
            ropes = r_ref[pl.ds(start, bk), :]
            scores = lax.dot_general(q_nope, keys, nt, preferred_element_type=jnp.float32)
            scores = scores + lax.dot_general(
                q_rope, ropes[:, :ROPE_DIM], nt, preferred_element_type=jnp.float32
            )
            scores = scores * factor
            if masked:
                k_pos = kp_ref[:, pl.ds(start, bk)]
                k_doc = kd_ref[:, pl.ds(start, bk)]
                visible = (k_pos <= q_pos) & (k_doc == q_doc)
                scores = jnp.where(visible, scores, jnp.float32(-1e30))
            m_prev = m_sc[...]
            m_new = jnp.maximum(m_prev, jnp.max(scores, axis=1, keepdims=True))
            alpha = jnp.exp(m_prev - m_new)
            weights = jnp.exp(scores - m_new)
            if masked:
                weights = jnp.where(visible, weights, jnp.float32(0.0))
            l_sc[...] = alpha * l_sc[...] + jnp.sum(weights, axis=1, keepdims=True)
            acc_sc[...] = alpha * acc_sc[...] + jnp.dot(
                weights.astype(jnp.bfloat16),
                v_ref[pl.ds(start, bk), :],
                preferred_element_type=jnp.float32,
            )
            m_sc[...] = m_new

        def step(t, carry):
            at = number * tiles + t
            active = (
                (kminp_ref[at] <= last_pos)
                & (kmaxd_ref[at] >= first_doc)
                & (kmind_ref[at] <= last_doc)
            )
            full = (
                (kmaxp_ref[at] <= first_pos)
                & (kmind_ref[at] == last_doc)
                & (kmaxd_ref[at] == first_doc)
            )

            @pl.when(active & full)
            def _():
                tile(False, t)

            @pl.when(active & jnp.logical_not(full))
            def _():
                tile(True, t)

            return carry

        return step

    for number, refs in enumerate(set_refs):
        lax.fori_loop(0, tiles, make_step(number, *refs), 0)
    o_ref[...] = (acc_sc[...] / l_sc[...]).astype(o_ref.dtype)


def flash(query_heads, packs, positions, docs_rows, query_docs, query_base):
    heads_here, rows, _ = query_heads.shape
    count = packs[0].shape[0]
    bq = min(BLOCK_Q, rows)
    bk = BLOCK_K
    q_tiles = rows // bq
    tiles = count // bk
    sets = len(packs)
    qdf = query_docs[::bq]
    qdl = query_docs[bq - 1 :: bq]
    pos_tiles = jnp.concatenate(positions, axis=0).reshape(sets * tiles, bk)
    doc_tiles = jnp.concatenate(docs_rows, axis=0).reshape(sets * tiles, bk)
    kminp = jnp.min(pos_tiles, axis=1)
    kmaxp = jnp.max(pos_tiles, axis=1)
    kmind = jnp.min(doc_tiles, axis=1)
    kmaxd = jnp.max(doc_tiles, axis=1)

    whole = lambda width: pl.BlockSpec((count, width), lambda h, qt, *_: (0, 0))
    in_specs = [pl.BlockSpec((None, bq, query_heads.shape[2]), lambda h, qt, *_: (h, qt, 0))]
    operands = [query_heads]
    for pack, pos, doc in zip(packs, positions, docs_rows):
        in_specs += [
            pl.BlockSpec((count, LANES), lambda h, qt, *_: (0, h)),
            pl.BlockSpec((count, LANES), lambda h, qt, *_: (0, heads_here + h)),
            pl.BlockSpec((count, LANES), lambda h, qt, *_: (0, 2 * heads_here)),
            pl.BlockSpec((1, count), lambda h, qt, *_: (0, 0)),
            pl.BlockSpec((1, count), lambda h, qt, *_: (0, 0)),
        ]
        operands += [pack, pack, pack, pos.reshape(1, count), doc.reshape(1, count)]
    in_specs.append(pl.BlockSpec((bq, 1), lambda h, qt, *_: (qt, 0)))
    operands.append(query_docs.reshape(rows, 1))
    del whole

    kernel = functools.partial(
        flash_kernel, sets=sets, tiles=tiles, factor=1.0 / math.sqrt(NOPE_DIM + ROPE_DIM)
    )
    grid_spec = pltpu.PrefetchScalarGridSpec(
        num_scalar_prefetch=7,
        grid=(heads_here, q_tiles),
        in_specs=in_specs,
        out_specs=pl.BlockSpec((bq, LANES), lambda h, qt, *_: (qt, h)),
        scratch_shapes=[
            pltpu.VMEM((bq, 1), jnp.float32),
            pltpu.VMEM((bq, 1), jnp.float32),
            pltpu.VMEM((bq, LANES), jnp.float32),
        ],
    )
    return pl.pallas_call(
        kernel,
        grid_spec=grid_spec,
        out_shape=jax.ShapeDtypeStruct((rows, heads_here * LANES), jnp.bfloat16),
        compiler_params=pltpu.CompilerParams(dimension_semantics=("arbitrary", "arbitrary")),
    )(query_base, qdf, qdl, kminp, kmaxp, kmind, kmaxd, *operands)


def ring_gather(block, order):
    count = len(order)
    place = {device: number for number, device in enumerate(order)}
    forward = [(order[i], order[(i + 1) % count]) for i in range(count)]
    backward = [(order[(i + 1) % count], order[i]) for i in range(count)]
    ahead = count // 2
    behind = count - 1 - ahead
    arrived = [block]
    sources = [list(range(count))]
    moving_f = block
    moving_b = block
    for step in range(1, ahead + 1):
        moving_f = lax.ppermute(moving_f, "tp", forward)
        arrived.append(moving_f)
        sources.append([order[(place[d] - step) % count] for d in range(count)])
        if step <= behind:
            moving_b = lax.ppermute(moving_b, "tp", backward)
            arrived.append(moving_b)
            sources.append([order[(place[d] + step) % count] for d in range(count)])
    source_of = np.zeros((count, count), np.int32)
    slot_of = np.zeros((count, count), np.int32)
    for number, row in enumerate(sources):
        for device, source in enumerate(row):
            source_of[device, number] = source
            slot_of[device, source] = number
    me = lax.axis_index("tp")
    return (
        jnp.concatenate(arrived, axis=0),
        jnp.asarray(source_of)[me],
        jnp.asarray(slot_of)[me],
    )


def body(queries, latent_rows, doc_ids, key_weight, value_weight, *, order):
    block_rows = queries.shape[0]
    chunk_rows = latent_rows.shape[0]
    chunks = block_rows // chunk_rows
    cycle_size = lax.axis_size("ctx")
    cycle_index = lax.axis_index("ctx")
    heads_here = key_weight.shape[1] // NOPE_DIM
    width = latent_rows.shape[1]
    pad = (-(width + 1)) % LANES
    doc_column = jnp.concatenate(
        [doc_ids.astype(jnp.bfloat16)[:, None], jnp.zeros((chunk_rows, pad), jnp.bfloat16)],
        axis=1,
    )
    chunk = jnp.concatenate([latent_rows, doc_column], axis=1)
    gathered, source_of, slot_of = ring_gather(chunk, order)
    latent_part = gathered[:, :KV_RANK]
    key_heads = jnp.dot(latent_part, key_weight, preferred_element_type=jnp.float32).astype(
        jnp.bfloat16
    )
    value_heads = jnp.dot(latent_part, value_weight, preferred_element_type=jnp.float32).astype(
        jnp.bfloat16
    )
    pack = jnp.concatenate([key_heads, value_heads, gathered[:, KV_RANK:]], axis=1)
    docs = gathered[:, width].astype(jnp.int32)
    offsets = (
        source_of[:, None] * chunk_rows + jnp.arange(chunk_rows, dtype=jnp.int32)[None, :]
    ).reshape(block_rows)
    query_docs = jnp.take(docs.reshape(chunks, chunk_rows), slot_of, axis=0).reshape(block_rows)

    packs, positions, docs_rows = [], [], []
    for distance in range(cycle_size - 1, 0, -1):
        route = [(i - distance, i) for i in range(cycle_size) if i - distance >= 0]
        moved = lax.ppermute(pack, "ctx", route)
        source = cycle_index - distance
        packs.append(moved)
        positions.append(jnp.where(source >= 0, source * block_rows + offsets, FAR))
        docs_rows.append(moved[:, 2 * heads_here * NOPE_DIM + ROPE_DIM].astype(jnp.int32))
    packs.append(pack)
    positions.append(cycle_index * block_rows + offsets)
    docs_rows.append(docs)

    query_heads = jnp.transpose(queries, (1, 0, 2))
    query_base = (cycle_index * block_rows).astype(jnp.int32).reshape(1)
    return flash(query_heads, packs, positions, docs_rows, query_docs, query_base)


def ring_order(mesh):
    line = list(mesh.devices[(0,) * (mesh.devices.ndim - 1)].reshape(-1))
    try:
        where = {(d.coords[0], d.coords[2]): number for number, d in enumerate(line)}
        xs = sorted({key[0] for key in where})
        zs = sorted({key[1] for key in where})
        order = []
        for turn, x in enumerate(xs):
            for z in zs if turn % 2 == 0 else zs[::-1]:
                order.append(where[(x, z)])
    except (AttributeError, KeyError, IndexError, TypeError):
        return list(range(len(line)))
    if sorted(order) != list(range(len(line))):
        return list(range(len(line)))
    return order


def solution(mesh):
    placed = (
        P(("grp", "ctx"), "tp", None),
        P(("grp", "ctx", "tp"), None),
        P(("grp", "ctx", "tp")),
        P(None, "tp"),
        P(None, "tp"),
    )
    return jax.shard_map(
        functools.partial(body, order=ring_order(mesh)),
        mesh=mesh,
        in_specs=placed,
        out_specs=P(("grp", "ctx"), "tp"),
        check_vma=False,
    )
```

```python
import functools
import math

import jax
import jax.numpy as jnp
import numpy as np
from jax import lax
from jax.experimental import pallas as pl
from jax.experimental.pallas import tpu as pltpu
from jax.sharding import PartitionSpec as P

KV_RANK = 512
ROPE_DIM = 64
NOPE_DIM = 128
LANES = 128
BLOCK_Q = 256
BLOCK_K = 256
FAR = 1 << 30


def flash_kernel(
    qbase_ref, qdf_ref, qdl_ref, kminp_ref, kmaxp_ref, kmind_ref, kmaxd_ref,
    q_ref, *rest, sets, tiles, factor,
):
    set_refs = [rest[5 * n : 5 * n + 5] for n in range(sets)]
    qd_ref, o_ref = rest[5 * sets], rest[5 * sets + 1]
    qt = pl.program_id(1)
    bq = q_ref.shape[0]
    bk = BLOCK_K
    first_pos = qbase_ref[0] + qt * bq
    last_pos = first_pos + (bq - 1)
    first_doc = qdf_ref[qt]
    last_doc = qdl_ref[qt]
    q = q_ref[...]
    q_nope = q[:, :NOPE_DIM]
    q_rope = q[:, NOPE_DIM:]
    q_pos = first_pos + lax.broadcasted_iota(jnp.int32, (bq, 1), 0)
    q_doc = qd_ref[...]
    nt = (((1,), (1,)), ((), ()))

    m_sc, l_sc, acc_sc = rest[5 * sets + 2 :]
    m_sc[...] = jnp.full(m_sc.shape, -1e30, jnp.float32)
    l_sc[...] = jnp.zeros(l_sc.shape, jnp.float32)
    acc_sc[...] = jnp.zeros(acc_sc.shape, jnp.float32)

    def make_step(number, k_ref, v_ref, r_ref, kp_ref, kd_ref):
        def tile(masked, t):
            start = pl.multiple_of(t * bk, bk)
            keys = k_ref[pl.ds(start, bk), :]
            ropes = r_ref[pl.ds(start, bk), :]
            scores = lax.dot_general(q_nope, keys, nt, preferred_element_type=jnp.float32)
            scores = scores + lax.dot_general(
                q_rope, ropes[:, :ROPE_DIM], nt, preferred_element_type=jnp.float32
            )
            scores = scores * factor
            if masked:
                k_pos = kp_ref[:, pl.ds(start, bk)]
                k_doc = kd_ref[:, pl.ds(start, bk)]
                visible = (k_pos <= q_pos) & (k_doc == q_doc)
                scores = jnp.where(visible, scores, jnp.float32(-1e30))
            m_prev = m_sc[...]
            m_new = jnp.maximum(m_prev, jnp.max(scores, axis=1, keepdims=True))
            alpha = jnp.exp(m_prev - m_new)
            weights = jnp.exp(scores - m_new)
            if masked:
                weights = jnp.where(visible, weights, jnp.float32(0.0))
            l_sc[...] = alpha * l_sc[...] + jnp.sum(weights, axis=1, keepdims=True)
            acc_sc[...] = alpha * acc_sc[...] + jnp.dot(
                weights.astype(jnp.bfloat16),
                v_ref[pl.ds(start, bk), :],
                preferred_element_type=jnp.float32,
            )
            m_sc[...] = m_new

        def step(t, carry):
            at = number * tiles + t
            active = (
                (kminp_ref[at] <= last_pos)
                & (kmaxd_ref[at] >= first_doc)
                & (kmind_ref[at] <= last_doc)
            )
            full = (
                (kmaxp_ref[at] <= first_pos)
                & (kmind_ref[at] == last_doc)
                & (kmaxd_ref[at] == first_doc)
            )

            @pl.when(active & full)
            def _():
                tile(False, t)

            @pl.when(active & jnp.logical_not(full))
            def _():
                tile(True, t)

            return carry

        return step

    for number, refs in enumerate(set_refs):
        lax.fori_loop(0, tiles, make_step(number, *refs), 0)
    o_ref[...] = (acc_sc[...] / l_sc[...]).astype(o_ref.dtype)


def flash(queries, packs, positions, pos_tables, docs_rows, query_docs, query_base):
    rows, heads_here, _ = queries.shape
    count = packs[0].shape[0]
    bq = min(BLOCK_Q, rows)
    bk = BLOCK_K
    q_tiles = rows // bq
    tiles = count // bk
    sets = len(packs)
    qdf = query_docs[::bq]
    qdl = query_docs[bq - 1 :: bq]
    kminp, kmaxp = pos_tables
    doc_tiles = jnp.concatenate(docs_rows, axis=0).reshape(sets * tiles, bk)
    kmind = jnp.min(doc_tiles, axis=1)
    kmaxd = jnp.max(doc_tiles, axis=1)

    in_specs = [pl.BlockSpec((bq, None, queries.shape[2]), lambda h, qt, *_: (qt, h, 0))]
    operands = [queries]
    for pack, pos, doc in zip(packs, positions, docs_rows):
        in_specs += [
            pl.BlockSpec((count, LANES), lambda h, qt, *_: (0, h)),
            pl.BlockSpec((count, LANES), lambda h, qt, *_: (0, heads_here + h)),
            pl.BlockSpec((count, LANES), lambda h, qt, *_: (0, 2 * heads_here)),
            pl.BlockSpec((1, count), lambda h, qt, *_: (0, 0)),
            pl.BlockSpec((1, count), lambda h, qt, *_: (0, 0)),
        ]
        operands += [pack, pack, pack, pos, doc.reshape(1, count)]
    in_specs.append(pl.BlockSpec((bq, 1), lambda h, qt, *_: (qt, 0)))
    operands.append(query_docs.reshape(rows, 1))

    kernel = functools.partial(
        flash_kernel, sets=sets, tiles=tiles, factor=1.0 / math.sqrt(NOPE_DIM + ROPE_DIM)
    )
    grid_spec = pltpu.PrefetchScalarGridSpec(
        num_scalar_prefetch=7,
        grid=(heads_here, q_tiles),
        in_specs=in_specs,
        out_specs=pl.BlockSpec((bq, LANES), lambda h, qt, *_: (qt, h)),
        scratch_shapes=[
            pltpu.VMEM((bq, 1), jnp.float32),
            pltpu.VMEM((bq, 1), jnp.float32),
            pltpu.VMEM((bq, LANES), jnp.float32),
        ],
    )
    return pl.pallas_call(
        kernel,
        grid_spec=grid_spec,
        out_shape=jax.ShapeDtypeStruct((rows, heads_here * LANES), jnp.bfloat16),
        compiler_params=pltpu.CompilerParams(dimension_semantics=("arbitrary", "arbitrary")),
    )(query_base, qdf, qdl, kminp, kmaxp, kmind, kmaxd, *operands)


def ring_tables(order):
    count = len(order)
    place = {device: number for number, device in enumerate(order)}
    ahead = count // 2
    behind = count - 1 - ahead
    sources = [list(range(count))]
    for step in range(1, ahead + 1):
        sources.append([order[(place[d] - step) % count] for d in range(count)])
        if step <= behind:
            sources.append([order[(place[d] + step) % count] for d in range(count)])
    source_of = np.zeros((count, count), np.int32)
    slot_of = np.zeros((count, count), np.int32)
    for number, row in enumerate(sources):
        for device, source in enumerate(row):
            source_of[device, number] = source
            slot_of[device, source] = number
    me = lax.axis_index("tp")
    return jnp.asarray(source_of)[me], jnp.asarray(slot_of)[me]


def ring_gather(block, order, early):
    count = len(order)
    place = {device: number for number, device in enumerate(order)}
    forward = [(order[i], order[(i + 1) % count]) for i in range(count)]
    backward = [(order[(i + 1) % count], order[i]) for i in range(count)]
    ahead = count // 2
    behind = count - 1 - ahead
    arrived = [block]
    moving_f = block
    moving_b = block
    for step in range(1, ahead + 1):
        moving_f = lax.ppermute(moving_f, "tp", forward)
        if step <= behind:
            moving_b = lax.ppermute(moving_b, "tp", backward)
        if step == 1:
            moving_f, moving_b, early = lax.optimization_barrier((moving_f, moving_b, early))
        arrived.append(moving_f)
        if step <= behind:
            arrived.append(moving_b)
    return jnp.concatenate(arrived, axis=0), early


def body(queries, latent_rows, doc_ids, key_weight, value_weight, *, order):
    block_rows = queries.shape[0]
    chunk_rows = latent_rows.shape[0]
    chunks = block_rows // chunk_rows
    cycle_size = lax.axis_size("ctx")
    cycle_index = lax.axis_index("ctx")
    heads_here = key_weight.shape[1] // NOPE_DIM
    width = latent_rows.shape[1]
    pad = (-(width + 1)) % LANES
    doc_column = jnp.concatenate(
        [doc_ids.astype(jnp.bfloat16)[:, None], jnp.zeros((chunk_rows, pad), jnp.bfloat16)],
        axis=1,
    )
    chunk = jnp.concatenate([latent_rows, doc_column], axis=1)
    source_of, slot_of = ring_tables(order)
    offsets = (
        source_of[:, None] * chunk_rows + jnp.arange(chunk_rows, dtype=jnp.int32)[None, :]
    ).reshape(block_rows)
    positions = []
    for distance in range(cycle_size - 1, 0, -1):
        source = cycle_index - distance
        positions.append(jnp.where(source >= 0, source * block_rows + offsets, FAR))
    positions.append(cycle_index * block_rows + offsets)
    pos_tiles = jnp.concatenate(positions, axis=0).reshape(-1, BLOCK_K)
    pos_tables = (jnp.min(pos_tiles, axis=1), jnp.max(pos_tiles, axis=1))
    query_base = (cycle_index * block_rows).astype(jnp.int32).reshape(1)
    early = (tuple(pos.reshape(1, -1) for pos in positions), pos_tables, query_base, queries)
    gathered, early = ring_gather(chunk, order, early)
    positions, pos_tables, query_base, queries = early
    latent_part = gathered[:, :KV_RANK]
    key_heads = jnp.dot(latent_part, key_weight, preferred_element_type=jnp.float32).astype(
        jnp.bfloat16
    )
    value_heads = jnp.dot(latent_part, value_weight, preferred_element_type=jnp.float32).astype(
        jnp.bfloat16
    )
    pack = jnp.concatenate([key_heads, value_heads, gathered[:, KV_RANK:]], axis=1)
    docs = gathered[:, width].astype(jnp.int32)
    query_docs = jnp.take(docs.reshape(chunks, chunk_rows), slot_of, axis=0).reshape(block_rows)

    packs, docs_rows = [], []
    for distance in range(cycle_size - 1, 0, -1):
        route = [(i - distance, i) for i in range(cycle_size) if i - distance >= 0]
        moved = lax.ppermute(pack, "ctx", route)
        packs.append(moved)
        docs_rows.append(moved[:, 2 * heads_here * NOPE_DIM + ROPE_DIM].astype(jnp.int32))
    packs.append(pack)
    docs_rows.append(docs)
    return flash(queries, packs, positions, pos_tables, docs_rows, query_docs, query_base)


def ring_order(mesh):
    line = list(mesh.devices[(0,) * (mesh.devices.ndim - 1)].reshape(-1))
    try:
        where = {(d.coords[0], d.coords[2]): number for number, d in enumerate(line)}
        xs = sorted({key[0] for key in where})
        zs = sorted({key[1] for key in where})
        order = []
        for turn, x in enumerate(xs):
            for z in zs if turn % 2 == 0 else zs[::-1]:
                order.append(where[(x, z)])
    except (AttributeError, KeyError, IndexError, TypeError):
        return list(range(len(line)))
    if sorted(order) != list(range(len(line))):
        return list(range(len(line)))
    return order


def solution(mesh):
    placed = (
        P(("grp", "ctx"), "tp", None),
        P(("grp", "ctx", "tp"), None),
        P(("grp", "ctx", "tp")),
        P(None, "tp"),
        P(None, "tp"),
    )
    return jax.shard_map(
        functools.partial(body, order=ring_order(mesh)),
        mesh=mesh,
        in_specs=placed,
        out_specs=P(("grp", "ctx"), "tp"),
        check_vma=False,
    )
```

```python
import functools
import math

import jax
import jax.numpy as jnp
import numpy as np
from jax import lax
from jax.experimental import pallas as pl
from jax.experimental.pallas import tpu as pltpu
from jax.sharding import PartitionSpec as P

KV_RANK = 512
ROPE_DIM = 64
NOPE_DIM = 128
LANES = 128
BLOCK_Q = 512
BLOCK_K = 512
FAR = 1 << 30


def flash_kernel(
    qbase_ref, qdf_ref, qdl_ref, kminp_ref, kmaxp_ref, kmind_ref, kmaxd_ref,
    q_ref, *rest, sets, tiles, factor,
):
    set_refs = [rest[5 * n : 5 * n + 5] for n in range(sets)]
    qd_ref, o_ref = rest[5 * sets], rest[5 * sets + 1]
    qt = pl.program_id(1)
    bq = q_ref.shape[0]
    bk = BLOCK_K
    first_pos = qbase_ref[0] + qt * bq
    last_pos = first_pos + (bq - 1)
    first_doc = qdf_ref[qt]
    last_doc = qdl_ref[qt]
    q = q_ref[...]
    q_nope = q[:, :NOPE_DIM]
    q_rope = q[:, NOPE_DIM:]
    q_pos = first_pos + lax.broadcasted_iota(jnp.int32, (bq, 1), 0)
    q_doc = qd_ref[...]
    nt = (((1,), (1,)), ((), ()))

    m_sc, l_sc, acc_sc = rest[5 * sets + 2 :]
    m_sc[...] = jnp.full(m_sc.shape, -1e30, jnp.float32)
    l_sc[...] = jnp.zeros(l_sc.shape, jnp.float32)
    acc_sc[...] = jnp.zeros(acc_sc.shape, jnp.float32)

    def make_step(number, k_ref, v_ref, r_ref, kp_ref, kd_ref):
        def tile(masked, t):
            start = pl.multiple_of(t * bk, bk)
            keys = k_ref[pl.ds(start, bk), :]
            ropes = r_ref[pl.ds(start, bk), :]
            scores = lax.dot_general(q_nope, keys, nt, preferred_element_type=jnp.float32)
            scores = scores + lax.dot_general(
                q_rope, ropes[:, :ROPE_DIM], nt, preferred_element_type=jnp.float32
            )
            scores = scores * factor
            if masked:
                k_pos = kp_ref[:, pl.ds(start, bk)]
                k_doc = kd_ref[:, pl.ds(start, bk)]
                visible = (k_pos <= q_pos) & (k_doc == q_doc)
                scores = jnp.where(visible, scores, jnp.float32(-1e30))
            m_prev = m_sc[...]
            m_new = jnp.maximum(m_prev, jnp.max(scores, axis=1, keepdims=True))
            alpha = jnp.exp(m_prev - m_new)
            weights = jnp.exp(scores - m_new)
            if masked:
                weights = jnp.where(visible, weights, jnp.float32(0.0))
            l_sc[...] = alpha * l_sc[...] + jnp.sum(weights, axis=1, keepdims=True)
            acc_sc[...] = alpha * acc_sc[...] + jnp.dot(
                weights.astype(jnp.bfloat16),
                v_ref[pl.ds(start, bk), :],
                preferred_element_type=jnp.float32,
            )
            m_sc[...] = m_new

        def step(t, carry):
            at = number * tiles + t
            active = (
                (kminp_ref[at] <= last_pos)
                & (kmaxd_ref[at] >= first_doc)
                & (kmind_ref[at] <= last_doc)
            )
            full = (
                (kmaxp_ref[at] <= first_pos)
                & (kmind_ref[at] == last_doc)
                & (kmaxd_ref[at] == first_doc)
            )

            @pl.when(active & full)
            def _():
                tile(False, t)

            @pl.when(active & jnp.logical_not(full))
            def _():
                tile(True, t)

            return carry

        return step

    for number, refs in enumerate(set_refs):
        lax.fori_loop(0, tiles, make_step(number, *refs), 0)
    o_ref[...] = (acc_sc[...] / l_sc[...]).astype(o_ref.dtype)


def flash(query_heads, packs, positions, pos_tables, docs_rows, query_docs, query_base):
    heads_here, rows, _ = query_heads.shape
    count = packs[0].shape[0]
    bq = min(BLOCK_Q, rows)
    bk = BLOCK_K
    q_tiles = rows // bq
    tiles = count // bk
    sets = len(packs)
    qdf = query_docs[::bq]
    qdl = query_docs[bq - 1 :: bq]
    kminp, kmaxp = pos_tables
    doc_tiles = jnp.concatenate(docs_rows, axis=0).reshape(sets * tiles, bk)
    kmind = jnp.min(doc_tiles, axis=1)
    kmaxd = jnp.max(doc_tiles, axis=1)

    in_specs = [pl.BlockSpec((None, bq, query_heads.shape[2]), lambda h, qt, *_: (h, qt, 0))]
    operands = [query_heads]
    for pack, pos, doc in zip(packs, positions, docs_rows):
        in_specs += [
            pl.BlockSpec((count, LANES), lambda h, qt, *_: (0, h)),
            pl.BlockSpec((count, LANES), lambda h, qt, *_: (0, heads_here + h)),
            pl.BlockSpec((count, LANES), lambda h, qt, *_: (0, 2 * heads_here)),
            pl.BlockSpec((1, count), lambda h, qt, *_: (0, 0)),
            pl.BlockSpec((1, count), lambda h, qt, *_: (0, 0)),
        ]
        operands += [pack, pack, pack, pos, doc.reshape(1, count)]
    in_specs.append(pl.BlockSpec((bq, 1), lambda h, qt, *_: (qt, 0)))
    operands.append(query_docs.reshape(rows, 1))

    kernel = functools.partial(
        flash_kernel, sets=sets, tiles=tiles, factor=1.0 / math.sqrt(NOPE_DIM + ROPE_DIM)
    )
    grid_spec = pltpu.PrefetchScalarGridSpec(
        num_scalar_prefetch=7,
        grid=(heads_here, q_tiles),
        in_specs=in_specs,
        out_specs=pl.BlockSpec((bq, LANES), lambda h, qt, *_: (qt, h)),
        scratch_shapes=[
            pltpu.VMEM((bq, 1), jnp.float32),
            pltpu.VMEM((bq, 1), jnp.float32),
            pltpu.VMEM((bq, LANES), jnp.float32),
        ],
    )
    return pl.pallas_call(
        kernel,
        grid_spec=grid_spec,
        out_shape=jax.ShapeDtypeStruct((rows, heads_here * LANES), jnp.bfloat16),
        compiler_params=pltpu.CompilerParams(dimension_semantics=("arbitrary", "arbitrary")),
    )(query_base, qdf, qdl, kminp, kmaxp, kmind, kmaxd, *operands)


def ring_tables(order):
    count = len(order)
    place = {device: number for number, device in enumerate(order)}
    ahead = count // 2
    behind = count - 1 - ahead
    sources = [list(range(count))]
    for step in range(1, ahead + 1):
        sources.append([order[(place[d] - step) % count] for d in range(count)])
        if step <= behind:
            sources.append([order[(place[d] + step) % count] for d in range(count)])
    source_of = np.zeros((count, count), np.int32)
    slot_of = np.zeros((count, count), np.int32)
    for number, row in enumerate(sources):
        for device, source in enumerate(row):
            source_of[device, number] = source
            slot_of[device, source] = number
    me = lax.axis_index("tp")
    return jnp.asarray(source_of)[me], jnp.asarray(slot_of)[me]


def ring_gather(block, order, early):
    count = len(order)
    place = {device: number for number, device in enumerate(order)}
    forward = [(order[i], order[(i + 1) % count]) for i in range(count)]
    backward = [(order[(i + 1) % count], order[i]) for i in range(count)]
    ahead = count // 2
    behind = count - 1 - ahead
    arrived = [block]
    moving_f = block
    moving_b = block
    for step in range(1, ahead + 1):
        moving_f = lax.ppermute(moving_f, "tp", forward)
        if step <= behind:
            moving_b = lax.ppermute(moving_b, "tp", backward)
        if step == 1:
            moving_f, moving_b, early = lax.optimization_barrier((moving_f, moving_b, early))
        arrived.append(moving_f)
        if step <= behind:
            arrived.append(moving_b)
    return jnp.concatenate(arrived, axis=0), early


def body(queries, latent_rows, doc_ids, key_weight, value_weight, *, order):
    block_rows = queries.shape[0]
    chunk_rows = latent_rows.shape[0]
    chunks = block_rows // chunk_rows
    cycle_size = lax.axis_size("ctx")
    cycle_index = lax.axis_index("ctx")
    heads_here = key_weight.shape[1] // NOPE_DIM
    width = latent_rows.shape[1]
    pad = (-(width + 1)) % LANES
    doc_column = jnp.concatenate(
        [doc_ids.astype(jnp.bfloat16)[:, None], jnp.zeros((chunk_rows, pad), jnp.bfloat16)],
        axis=1,
    )
    chunk = jnp.concatenate([latent_rows, doc_column], axis=1)
    source_of, slot_of = ring_tables(order)
    offsets = (
        source_of[:, None] * chunk_rows + jnp.arange(chunk_rows, dtype=jnp.int32)[None, :]
    ).reshape(block_rows)
    positions = []
    for distance in range(cycle_size - 1, 0, -1):
        source = cycle_index - distance
        positions.append(jnp.where(source >= 0, source * block_rows + offsets, FAR))
    positions.append(cycle_index * block_rows + offsets)
    pos_tiles = jnp.concatenate(positions, axis=0).reshape(-1, BLOCK_K)
    pos_tables = (jnp.min(pos_tiles, axis=1), jnp.max(pos_tiles, axis=1))
    query_base = (cycle_index * block_rows).astype(jnp.int32).reshape(1)
    query_heads = jnp.transpose(queries, (1, 0, 2))
    early = (tuple(pos.reshape(1, -1) for pos in positions), pos_tables, query_base, query_heads)
    gathered, early = ring_gather(chunk, order, early)
    positions, pos_tables, query_base, query_heads = early
    latent_part = gathered[:, :KV_RANK]
    key_heads = jnp.dot(latent_part, key_weight, preferred_element_type=jnp.float32).astype(
        jnp.bfloat16
    )
    value_heads = jnp.dot(latent_part, value_weight, preferred_element_type=jnp.float32).astype(
        jnp.bfloat16
    )
    pack = jnp.concatenate([key_heads, value_heads, gathered[:, KV_RANK:]], axis=1)
    docs = gathered[:, width].astype(jnp.int32)
    query_docs = jnp.take(docs.reshape(chunks, chunk_rows), slot_of, axis=0).reshape(block_rows)

    packs, docs_rows = [], []
    for distance in range(cycle_size - 1, 0, -1):
        route = [(i - distance, i) for i in range(cycle_size) if i - distance >= 0]
        moved = lax.ppermute(pack, "ctx", route)
        packs.append(moved)
        docs_rows.append(moved[:, 2 * heads_here * NOPE_DIM + ROPE_DIM].astype(jnp.int32))
    packs.append(pack)
    docs_rows.append(docs)
    return flash(query_heads, packs, positions, pos_tables, docs_rows, query_docs, query_base)


def ring_order(mesh):
    line = list(mesh.devices[(0,) * (mesh.devices.ndim - 1)].reshape(-1))
    try:
        where = {(d.coords[0], d.coords[2]): number for number, d in enumerate(line)}
        xs = sorted({key[0] for key in where})
        zs = sorted({key[1] for key in where})
        order = []
        for turn, x in enumerate(xs):
            for z in zs if turn % 2 == 0 else zs[::-1]:
                order.append(where[(x, z)])
    except (AttributeError, KeyError, IndexError, TypeError):
        return list(range(len(line)))
    if sorted(order) != list(range(len(line))):
        return list(range(len(line)))
    return order


def solution(mesh):
    placed = (
        P(("grp", "ctx"), "tp", None),
        P(("grp", "ctx", "tp"), None),
        P(("grp", "ctx", "tp")),
        P(None, "tp"),
        P(None, "tp"),
    )
    return jax.shard_map(
        functools.partial(body, order=ring_order(mesh)),
        mesh=mesh,
        in_specs=placed,
        out_specs=P(("grp", "ctx"), "tp"),
        check_vma=False,
    )
```

```python
import functools
import math

import jax
import jax.numpy as jnp
import numpy as np
from jax import lax
from jax.experimental import pallas as pl
from jax.experimental.pallas import tpu as pltpu
from jax.sharding import PartitionSpec as P

KV_RANK = 512
ROPE_DIM = 64
NOPE_DIM = 128
LANES = 128
BLOCK_Q = 512
BLOCK_K = 512
FAR = 1 << 30


def flash_kernel(
    qbase_ref, qdf_ref, qdl_ref, kminp_ref, kmaxp_ref, kmind_ref, kmaxd_ref,
    q_ref, *rest, sets, tiles, factor,
):
    set_refs = [rest[5 * n : 5 * n + 5] for n in range(sets)]
    qd_ref, o_ref = rest[5 * sets], rest[5 * sets + 1]
    qt = pl.program_id(1)
    bq = q_ref.shape[0]
    bk = BLOCK_K
    first_pos = qbase_ref[0] + qt * bq
    last_pos = first_pos + (bq - 1)
    first_doc = qdf_ref[qt]
    last_doc = qdl_ref[qt]
    q = q_ref[...]
    q_nope = q[:, :NOPE_DIM]
    q_rope = q[:, NOPE_DIM:]
    q_pos = first_pos + lax.broadcasted_iota(jnp.int32, (bq, 1), 0)
    q_doc = qd_ref[...]
    nt = (((1,), (1,)), ((), ()))

    m_sc, l_sc, acc_sc = rest[5 * sets + 2 :]
    m_sc[...] = jnp.full(m_sc.shape, -1e30, jnp.float32)
    l_sc[...] = jnp.zeros(l_sc.shape, jnp.float32)
    acc_sc[...] = jnp.zeros(acc_sc.shape, jnp.float32)

    def make_step(number, k_ref, v_ref, r_ref, kp_ref, kd_ref):
        def tile(masked, t):
            start = pl.multiple_of(t * bk, bk)
            keys = k_ref[pl.ds(start, bk), :]
            ropes = r_ref[pl.ds(start, bk), :]
            scores = lax.dot_general(q_nope, keys, nt, preferred_element_type=jnp.float32)
            scores = scores + lax.dot_general(
                q_rope, ropes[:, :ROPE_DIM], nt, preferred_element_type=jnp.float32
            )
            scores = scores * factor
            if masked:
                k_pos = kp_ref[:, pl.ds(start, bk)]
                k_doc = kd_ref[:, pl.ds(start, bk)]
                visible = (k_pos <= q_pos) & (k_doc == q_doc)
                scores = jnp.where(visible, scores, jnp.float32(-1e30))
            m_prev = m_sc[...]
            m_new = jnp.maximum(m_prev, jnp.max(scores, axis=1, keepdims=True))
            alpha = jnp.exp(m_prev - m_new)
            weights = jnp.exp(scores - m_new)
            l_sc[...] = alpha * l_sc[...] + jnp.sum(weights, axis=1, keepdims=True)
            acc_sc[...] = alpha * acc_sc[...] + jnp.dot(
                weights.astype(jnp.bfloat16),
                v_ref[pl.ds(start, bk), :],
                preferred_element_type=jnp.float32,
            )
            m_sc[...] = m_new

        def step(t, carry):
            at = number * tiles + t
            active = (
                (kminp_ref[at] <= last_pos)
                & (kmaxd_ref[at] >= first_doc)
                & (kmind_ref[at] <= last_doc)
            )
            full = (
                (kmaxp_ref[at] <= first_pos)
                & (kmind_ref[at] == last_doc)
                & (kmaxd_ref[at] == first_doc)
            )

            @pl.when(active & full)
            def _():
                tile(False, t)

            @pl.when(active & jnp.logical_not(full))
            def _():
                tile(True, t)

            return carry

        return step

    for number, refs in enumerate(set_refs):
        lax.fori_loop(0, tiles, make_step(number, *refs), 0)
    o_ref[...] = (acc_sc[...] / l_sc[...]).astype(o_ref.dtype)


def flash(query_heads, packs, positions, pos_tables, docs_rows, query_docs, query_base):
    heads_here, rows, _ = query_heads.shape
    count = packs[0].shape[0]
    bq = min(BLOCK_Q, rows)
    bk = BLOCK_K
    q_tiles = rows // bq
    tiles = count // bk
    sets = len(packs)
    qdf = query_docs[::bq]
    qdl = query_docs[bq - 1 :: bq]
    kminp, kmaxp = pos_tables
    doc_tiles = jnp.concatenate(docs_rows, axis=0).reshape(sets * tiles, bk)
    kmind = jnp.min(doc_tiles, axis=1)
    kmaxd = jnp.max(doc_tiles, axis=1)

    in_specs = [pl.BlockSpec((None, bq, query_heads.shape[2]), lambda h, qt, *_: (h, qt, 0))]
    operands = [query_heads]
    for pack, pos, doc in zip(packs, positions, docs_rows):
        in_specs += [
            pl.BlockSpec((count, LANES), lambda h, qt, *_: (0, h)),
            pl.BlockSpec((count, LANES), lambda h, qt, *_: (0, heads_here + h)),
            pl.BlockSpec((count, LANES), lambda h, qt, *_: (0, 2 * heads_here)),
            pl.BlockSpec((1, count), lambda h, qt, *_: (0, 0)),
            pl.BlockSpec((1, count), lambda h, qt, *_: (0, 0)),
        ]
        operands += [pack, pack, pack, pos, doc.reshape(1, count)]
    in_specs.append(pl.BlockSpec((bq, 1), lambda h, qt, *_: (qt, 0)))
    operands.append(query_docs.reshape(rows, 1))

    kernel = functools.partial(
        flash_kernel, sets=sets, tiles=tiles, factor=1.0 / math.sqrt(NOPE_DIM + ROPE_DIM)
    )
    grid_spec = pltpu.PrefetchScalarGridSpec(
        num_scalar_prefetch=7,
        grid=(heads_here, q_tiles),
        in_specs=in_specs,
        out_specs=pl.BlockSpec((bq, LANES), lambda h, qt, *_: (qt, h)),
        scratch_shapes=[
            pltpu.VMEM((bq, 1), jnp.float32),
            pltpu.VMEM((bq, 1), jnp.float32),
            pltpu.VMEM((bq, LANES), jnp.float32),
        ],
    )
    return pl.pallas_call(
        kernel,
        grid_spec=grid_spec,
        out_shape=jax.ShapeDtypeStruct((rows, heads_here * LANES), jnp.bfloat16),
        compiler_params=pltpu.CompilerParams(dimension_semantics=("arbitrary", "arbitrary")),
    )(query_base, qdf, qdl, kminp, kmaxp, kmind, kmaxd, *operands)


def ring_tables(order):
    count = len(order)
    place = {device: number for number, device in enumerate(order)}
    ahead = count // 2
    behind = count - 1 - ahead
    sources = [list(range(count))]
    for step in range(1, ahead + 1):
        sources.append([order[(place[d] - step) % count] for d in range(count)])
        if step <= behind:
            sources.append([order[(place[d] + step) % count] for d in range(count)])
    source_of = np.zeros((count, count), np.int32)
    slot_of = np.zeros((count, count), np.int32)
    for number, row in enumerate(sources):
        for device, source in enumerate(row):
            source_of[device, number] = source
            slot_of[device, source] = number
    me = lax.axis_index("tp")
    return jnp.asarray(source_of)[me], jnp.asarray(slot_of)[me]


def ring_gather(block, order, early, source_of):
    count = len(order)
    place = {device: number for number, device in enumerate(order)}
    forward = [(order[i], order[(i + 1) % count]) for i in range(count)]
    backward = [(order[(i + 1) % count], order[i]) for i in range(count)]
    ahead = count // 2
    behind = count - 1 - ahead
    arrived = [block]
    moving_f = block
    moving_b = block
    for step in range(1, ahead + 1):
        moving_f = lax.ppermute(moving_f, "tp", forward)
        if step <= behind:
            moving_b = lax.ppermute(moving_b, "tp", backward)
        if step == 1:
            moving_f, moving_b, early = lax.optimization_barrier((moving_f, moving_b, early))
        arrived.append(moving_f)
        if step <= behind:
            arrived.append(moving_b)
    rows = block.shape[0]
    placed = jnp.zeros((count * rows, block.shape[1]), block.dtype)
    for number, piece in enumerate(arrived):
        placed = lax.dynamic_update_slice(placed, piece, (source_of[number] * rows, 0))
    return placed, early


def body(queries, latent_rows, doc_ids, key_weight, value_weight, *, order):
    block_rows = queries.shape[0]
    chunk_rows = latent_rows.shape[0]
    chunks = block_rows // chunk_rows
    cycle_size = lax.axis_size("ctx")
    cycle_index = lax.axis_index("ctx")
    heads_here = key_weight.shape[1] // NOPE_DIM
    width = latent_rows.shape[1]
    pad = (-(width + 1)) % LANES
    doc_column = jnp.concatenate(
        [doc_ids.astype(jnp.bfloat16)[:, None], jnp.zeros((chunk_rows, pad), jnp.bfloat16)],
        axis=1,
    )
    chunk = jnp.concatenate([latent_rows, doc_column], axis=1)
    source_of, slot_of = ring_tables(order)
    offsets = jnp.arange(block_rows, dtype=jnp.int32)
    positions = []
    for distance in range(cycle_size - 1, 0, -1):
        source = cycle_index - distance
        positions.append(jnp.where(source >= 0, source * block_rows + offsets, FAR))
    positions.append(cycle_index * block_rows + offsets)
    pos_tiles = jnp.concatenate(positions, axis=0).reshape(-1, BLOCK_K)
    pos_tables = (jnp.min(pos_tiles, axis=1), jnp.max(pos_tiles, axis=1))
    query_base = (cycle_index * block_rows).astype(jnp.int32).reshape(1)
    query_heads = jnp.transpose(queries, (1, 0, 2))
    early = (tuple(pos.reshape(1, -1) for pos in positions), pos_tables, query_base, query_heads)
    gathered, early = ring_gather(chunk, order, early, source_of)
    positions, pos_tables, query_base, query_heads = early
    latent_part = gathered[:, :KV_RANK]
    key_heads = jnp.dot(latent_part, key_weight, preferred_element_type=jnp.float32).astype(
        jnp.bfloat16
    )
    value_heads = jnp.dot(latent_part, value_weight, preferred_element_type=jnp.float32).astype(
        jnp.bfloat16
    )
    pack = jnp.concatenate([key_heads, value_heads, gathered[:, KV_RANK:]], axis=1)
    docs = gathered[:, width].astype(jnp.int32)
    query_docs = docs

    packs, docs_rows = [], []
    for distance in range(cycle_size - 1, 0, -1):
        route = [(i - distance, i) for i in range(cycle_size) if i - distance >= 0]
        moved = lax.ppermute(pack, "ctx", route)
        packs.append(moved)
        docs_rows.append(moved[:, 2 * heads_here * NOPE_DIM + ROPE_DIM].astype(jnp.int32))
    packs.append(pack)
    docs_rows.append(docs)
    return flash(query_heads, packs, positions, pos_tables, docs_rows, query_docs, query_base)


def ring_order(mesh):
    line = list(mesh.devices[(0,) * (mesh.devices.ndim - 1)].reshape(-1))
    try:
        where = {(d.coords[0], d.coords[2]): number for number, d in enumerate(line)}
        xs = sorted({key[0] for key in where})
        zs = sorted({key[1] for key in where})
        order = []
        for turn, x in enumerate(xs):
            for z in zs if turn % 2 == 0 else zs[::-1]:
                order.append(where[(x, z)])
    except (AttributeError, KeyError, IndexError, TypeError):
        return list(range(len(line)))
    if sorted(order) != list(range(len(line))):
        return list(range(len(line)))
    return order


def solution(mesh):
    placed = (
        P(("grp", "ctx"), "tp", None),
        P(("grp", "ctx", "tp"), None),
        P(("grp", "ctx", "tp")),
        P(None, "tp"),
        P(None, "tp"),
    )
    return jax.shard_map(
        functools.partial(body, order=ring_order(mesh)),
        mesh=mesh,
        in_specs=placed,
        out_specs=P(("grp", "ctx"), "tp"),
        check_vma=False,
    )
```

```python
import functools
import math

import jax
import jax.numpy as jnp
import numpy as np
from jax import lax
from jax.experimental import pallas as pl
from jax.experimental.pallas import tpu as pltpu
from jax.sharding import PartitionSpec as P

KV_RANK = 512
ROPE_DIM = 64
NOPE_DIM = 128
LANES = 128
BLOCK_Q = 512
BLOCK_K = 512
FAR = 1 << 30


def flash_kernel(
    qbase_ref, kminp_ref, kmaxp_ref, kmind_ref, kmaxd_ref,
    q_ref, *rest, sets, tiles, factor,
):
    set_refs = [rest[5 * n : 5 * n + 5] for n in range(sets)]
    qd_ref, o_ref = rest[5 * sets], rest[5 * sets + 1]
    qt = pl.program_id(1)
    bq = q_ref.shape[0]
    bk = BLOCK_K
    first_pos = qbase_ref[0] + qt * bq
    last_pos = first_pos + (bq - 1)
    own = (sets - 1) * tiles + qt
    first_doc = kmind_ref[own]
    last_doc = kmaxd_ref[own]
    q = q_ref[...]
    q_nope = q[:, :NOPE_DIM]
    q_rope = q[:, NOPE_DIM:]
    q_pos = first_pos + lax.broadcasted_iota(jnp.int32, (bq, 1), 0)
    q_doc = qd_ref[...]
    nt = (((1,), (1,)), ((), ()))

    m_sc, l_sc, acc_sc = rest[5 * sets + 2 :]
    m_sc[...] = jnp.full(m_sc.shape, -1e30, jnp.float32)
    l_sc[...] = jnp.zeros(l_sc.shape, jnp.float32)
    acc_sc[...] = jnp.zeros(acc_sc.shape, jnp.float32)

    def make_step(number, k_ref, v_ref, r_ref, kp_ref, kd_ref):
        def tile(masked, t):
            start = pl.multiple_of(t * bk, bk)
            keys = k_ref[pl.ds(start, bk), :]
            ropes = r_ref[pl.ds(start, bk), :]
            scores = lax.dot_general(q_nope, keys, nt, preferred_element_type=jnp.float32)
            scores = scores + lax.dot_general(
                q_rope, ropes[:, :ROPE_DIM], nt, preferred_element_type=jnp.float32
            )
            scores = scores * factor
            if masked:
                k_pos = kp_ref[:, pl.ds(start, bk)]
                k_doc = kd_ref[:, pl.ds(start, bk)]
                visible = (k_pos <= q_pos) & (k_doc == q_doc)
                scores = jnp.where(visible, scores, jnp.float32(-1e30))
            m_prev = m_sc[...]
            m_new = jnp.maximum(m_prev, jnp.max(scores, axis=1, keepdims=True))
            alpha = jnp.exp(m_prev - m_new)
            weights = jnp.exp(scores - m_new)
            l_sc[...] = alpha * l_sc[...] + jnp.sum(weights, axis=1, keepdims=True)
            acc_sc[...] = alpha * acc_sc[...] + jnp.dot(
                weights.astype(jnp.bfloat16),
                v_ref[pl.ds(start, bk), :],
                preferred_element_type=jnp.float32,
            )
            m_sc[...] = m_new

        def step(t, carry):
            at = number * tiles + t
            active = (
                (kminp_ref[at] <= last_pos)
                & (kmaxd_ref[at] >= first_doc)
                & (kmind_ref[at] <= last_doc)
            )
            full = (
                (kmaxp_ref[at] <= first_pos)
                & (kmind_ref[at] == last_doc)
                & (kmaxd_ref[at] == first_doc)
            )

            @pl.when(active & full)
            def _():
                tile(False, t)

            @pl.when(active & jnp.logical_not(full))
            def _():
                tile(True, t)

            return carry

        return step

    for number, refs in enumerate(set_refs):
        lax.fori_loop(0, tiles, make_step(number, *refs), 0)
    o_ref[...] = (acc_sc[...] / l_sc[...]).astype(o_ref.dtype)


def flash(query_heads, packs, positions, pos_tables, docs_rows, query_docs, query_base):
    heads_here, rows, _ = query_heads.shape
    count = packs[0].shape[0]
    bq = min(BLOCK_Q, rows)
    bk = BLOCK_K
    q_tiles = rows // bq
    tiles = count // bk
    sets = len(packs)
    assert bq == bk and rows == count
    kminp, kmaxp = pos_tables
    doc_tiles = jnp.concatenate(docs_rows, axis=0).reshape(sets * tiles, bk)
    kmind = jnp.min(doc_tiles, axis=1)
    kmaxd = jnp.max(doc_tiles, axis=1)

    in_specs = [pl.BlockSpec((None, bq, query_heads.shape[2]), lambda h, qt, *_: (h, qt, 0))]
    operands = [query_heads]
    for pack, pos, doc in zip(packs, positions, docs_rows):
        in_specs += [
            pl.BlockSpec((count, LANES), lambda h, qt, *_: (0, h)),
            pl.BlockSpec((count, LANES), lambda h, qt, *_: (0, heads_here + h)),
            pl.BlockSpec((count, LANES), lambda h, qt, *_: (0, 2 * heads_here)),
            pl.BlockSpec((1, count), lambda h, qt, *_: (0, 0)),
            pl.BlockSpec((1, count), lambda h, qt, *_: (0, 0)),
        ]
        operands += [pack, pack, pack, pos, doc.reshape(1, count)]
    in_specs.append(pl.BlockSpec((bq, 1), lambda h, qt, *_: (qt, 0)))
    operands.append(query_docs.reshape(rows, 1))

    kernel = functools.partial(
        flash_kernel, sets=sets, tiles=tiles, factor=1.0 / math.sqrt(NOPE_DIM + ROPE_DIM)
    )
    grid_spec = pltpu.PrefetchScalarGridSpec(
        num_scalar_prefetch=5,
        grid=(heads_here, q_tiles),
        in_specs=in_specs,
        out_specs=pl.BlockSpec((bq, LANES), lambda h, qt, *_: (qt, h)),
        scratch_shapes=[
            pltpu.VMEM((bq, 1), jnp.float32),
            pltpu.VMEM((bq, 1), jnp.float32),
            pltpu.VMEM((bq, LANES), jnp.float32),
        ],
    )
    return pl.pallas_call(
        kernel,
        grid_spec=grid_spec,
        out_shape=jax.ShapeDtypeStruct((rows, heads_here * LANES), jnp.bfloat16),
        compiler_params=pltpu.CompilerParams(dimension_semantics=("arbitrary", "arbitrary")),
    )(query_base, kminp, kmaxp, kmind, kmaxd, *operands)


def ring_tables(order):
    count = len(order)
    place = {device: number for number, device in enumerate(order)}
    ahead = count // 2
    behind = count - 1 - ahead
    sources = [list(range(count))]
    for step in range(1, ahead + 1):
        sources.append([order[(place[d] - step) % count] for d in range(count)])
        if step <= behind:
            sources.append([order[(place[d] + step) % count] for d in range(count)])
    source_of = np.zeros((count, count), np.int32)
    slot_of = np.zeros((count, count), np.int32)
    for number, row in enumerate(sources):
        for device, source in enumerate(row):
            source_of[device, number] = source
            slot_of[device, source] = number
    me = lax.axis_index("tp")
    return jnp.asarray(source_of)[me], jnp.asarray(slot_of)[me]


def ring_gather(block, order, early, source_of):
    count = len(order)
    place = {device: number for number, device in enumerate(order)}
    forward = [(order[i], order[(i + 1) % count]) for i in range(count)]
    backward = [(order[(i + 1) % count], order[i]) for i in range(count)]
    ahead = count // 2
    behind = count - 1 - ahead
    arrived = [block]
    moving_f = block
    moving_b = block
    for step in range(1, ahead + 1):
        moving_f = lax.ppermute(moving_f, "tp", forward)
        if step <= behind:
            moving_b = lax.ppermute(moving_b, "tp", backward)
        if step == 1:
            moving_f, moving_b, early = lax.optimization_barrier((moving_f, moving_b, early))
        arrived.append(moving_f)
        if step <= behind:
            arrived.append(moving_b)
    rows = block.shape[0]
    placed = jnp.zeros((count * rows, block.shape[1]), block.dtype)
    for number, piece in enumerate(arrived):
        placed = lax.dynamic_update_slice(placed, piece, (source_of[number] * rows, 0))
    return placed, early


def body(queries, latent_rows, doc_ids, key_weight, value_weight, *, order):
    block_rows = queries.shape[0]
    chunk_rows = latent_rows.shape[0]
    chunks = block_rows // chunk_rows
    cycle_size = lax.axis_size("ctx")
    cycle_index = lax.axis_index("ctx")
    heads_here = key_weight.shape[1] // NOPE_DIM
    width = latent_rows.shape[1]
    pad = (-(width + 1)) % LANES
    doc_column = jnp.concatenate(
        [doc_ids.astype(jnp.bfloat16)[:, None], jnp.zeros((chunk_rows, pad), jnp.bfloat16)],
        axis=1,
    )
    chunk = jnp.concatenate([latent_rows, doc_column], axis=1)
    source_of, slot_of = ring_tables(order)
    offsets = jnp.arange(block_rows, dtype=jnp.int32)
    positions = []
    for distance in range(cycle_size - 1, 0, -1):
        source = cycle_index - distance
        positions.append(jnp.where(source >= 0, source * block_rows + offsets, FAR))
    positions.append(cycle_index * block_rows + offsets)
    pos_tiles = jnp.concatenate(positions, axis=0).reshape(-1, BLOCK_K)
    pos_tables = (jnp.min(pos_tiles, axis=1), jnp.max(pos_tiles, axis=1))
    query_base = (cycle_index * block_rows).astype(jnp.int32).reshape(1)
    query_heads = jnp.transpose(queries, (1, 0, 2))
    early = (tuple(pos.reshape(1, -1) for pos in positions), pos_tables, query_base, query_heads)
    gathered, early = ring_gather(chunk, order, early, source_of)
    positions, pos_tables, query_base, query_heads = early
    latent_part = gathered[:, :KV_RANK]
    key_heads = jnp.dot(latent_part, key_weight, preferred_element_type=jnp.float32).astype(
        jnp.bfloat16
    )
    value_heads = jnp.dot(latent_part, value_weight, preferred_element_type=jnp.float32).astype(
        jnp.bfloat16
    )
    pack = jnp.concatenate([key_heads, value_heads, gathered[:, KV_RANK:]], axis=1)
    docs = gathered[:, width].astype(jnp.int32)
    query_docs = docs

    packs, docs_rows = [], []
    for distance in range(cycle_size - 1, 0, -1):
        route = [(i - distance, i) for i in range(cycle_size) if i - distance >= 0]
        moved = lax.ppermute(pack, "ctx", route)
        packs.append(moved)
        docs_rows.append(moved[:, 2 * heads_here * NOPE_DIM + ROPE_DIM].astype(jnp.int32))
    packs.append(pack)
    docs_rows.append(docs)
    return flash(query_heads, packs, positions, pos_tables, docs_rows, query_docs, query_base)


def ring_order(mesh):
    line = list(mesh.devices[(0,) * (mesh.devices.ndim - 1)].reshape(-1))
    try:
        where = {(d.coords[0], d.coords[2]): number for number, d in enumerate(line)}
        xs = sorted({key[0] for key in where})
        zs = sorted({key[1] for key in where})
        order = []
        for turn, x in enumerate(xs):
            for z in zs if turn % 2 == 0 else zs[::-1]:
                order.append(where[(x, z)])
    except (AttributeError, KeyError, IndexError, TypeError):
        return list(range(len(line)))
    if sorted(order) != list(range(len(line))):
        return list(range(len(line)))
    return order


def solution(mesh):
    placed = (
        P(("grp", "ctx"), "tp", None),
        P(("grp", "ctx", "tp"), None),
        P(("grp", "ctx", "tp")),
        P(None, "tp"),
        P(None, "tp"),
    )
    return jax.shard_map(
        functools.partial(body, order=ring_order(mesh)),
        mesh=mesh,
        in_specs=placed,
        out_specs=P(("grp", "ctx"), "tp"),
        check_vma=False,
    )
```

```python
import functools
import math

import jax
import jax.numpy as jnp
import numpy as np
from jax import lax
from jax.experimental import pallas as pl
from jax.experimental.pallas import tpu as pltpu
from jax.sharding import PartitionSpec as P

KV_RANK = 512
ROPE_DIM = 64
NOPE_DIM = 128
LANES = 128
BLOCK_Q = 512
BLOCK_K = 512
FAR = 1 << 30


def flash_kernel(
    qbase_ref, kminp_ref, kmaxp_ref, kmind_ref, kmaxd_ref,
    q_ref, *rest, sets, tiles, factor,
):
    set_refs = [rest[5 * n : 5 * n + 5] for n in range(sets)]
    qd_ref, o_ref = rest[5 * sets], rest[5 * sets + 1]
    qt = pl.program_id(1)
    bq = q_ref.shape[0]
    bk = BLOCK_K
    first_pos = qbase_ref[0] + qt * bq
    last_pos = first_pos + (bq - 1)
    own = (sets - 1) * tiles + qt
    first_doc = kmind_ref[own]
    last_doc = kmaxd_ref[own]
    q = q_ref[...]
    q_nope = q[:, :NOPE_DIM]
    q_rope = q[:, NOPE_DIM:]
    q_pos = first_pos + lax.broadcasted_iota(jnp.int32, (bq, 1), 0)
    q_doc = qd_ref[...]
    nt = (((1,), (1,)), ((), ()))

    m_sc, l_sc, acc_sc = rest[5 * sets + 2 :]
    m_sc[...] = jnp.full(m_sc.shape, -1e30, jnp.float32)
    l_sc[...] = jnp.zeros(l_sc.shape, jnp.float32)
    acc_sc[...] = jnp.zeros(acc_sc.shape, jnp.float32)

    def make_step(number, k_ref, v_ref, r_ref, kp_ref, kd_ref):
        def tile(masked, t):
            start = pl.multiple_of(t * bk, bk)
            keys = k_ref[pl.ds(start, bk), :]
            ropes = r_ref[pl.ds(start, bk), :]
            scores = lax.dot_general(q_nope, keys, nt, preferred_element_type=jnp.float32)
            scores = scores + lax.dot_general(
                q_rope, ropes[:, :ROPE_DIM], nt, preferred_element_type=jnp.float32
            )
            scores = scores * factor
            if masked:
                k_pos = kp_ref[:, pl.ds(start, bk)]
                k_doc = kd_ref[:, pl.ds(start, bk)]
                visible = (k_pos <= q_pos) & (k_doc == q_doc)
                scores = jnp.where(visible, scores, jnp.float32(-1e30))
            m_prev = m_sc[...]
            m_new = jnp.maximum(m_prev, jnp.max(scores, axis=1, keepdims=True))
            alpha = jnp.exp(m_prev - m_new)
            weights = jnp.exp(scores - m_new)
            l_sc[...] = alpha * l_sc[...] + jnp.sum(weights, axis=1, keepdims=True)
            acc_sc[...] = alpha * acc_sc[...] + jnp.dot(
                weights.astype(jnp.bfloat16),
                v_ref[pl.ds(start, bk), :],
                preferred_element_type=jnp.float32,
            )
            m_sc[...] = m_new

        def step(t, carry):
            at = number * tiles + t
            active = (
                (kminp_ref[at] <= last_pos)
                & (kmaxd_ref[at] >= first_doc)
                & (kmind_ref[at] <= last_doc)
            )
            full = (
                (kmaxp_ref[at] <= first_pos)
                & (kmind_ref[at] == last_doc)
                & (kmaxd_ref[at] == first_doc)
            )

            @pl.when(active & full)
            def _():
                tile(False, t)

            @pl.when(active & jnp.logical_not(full))
            def _():
                tile(True, t)

            return carry

        return step

    for number, refs in enumerate(set_refs):
        lax.fori_loop(0, tiles, make_step(number, *refs), 0)
    o_ref[...] = (acc_sc[...] / l_sc[...]).astype(o_ref.dtype)


def flash(query_heads, packs, positions, pos_tables, docs_rows, query_docs, query_base):
    heads_here, rows, _ = query_heads.shape
    count = packs[0].shape[0]
    bq = min(BLOCK_Q, rows)
    bk = BLOCK_K
    q_tiles = rows // bq
    tiles = count // bk
    sets = len(packs)
    assert bq == bk and rows == count
    kminp, kmaxp = pos_tables
    doc_tiles = jnp.concatenate(docs_rows, axis=0).reshape(sets * tiles, bk)
    kmind = jnp.min(doc_tiles, axis=1)
    kmaxd = jnp.max(doc_tiles, axis=1)

    in_specs = [pl.BlockSpec((None, bq, query_heads.shape[2]), lambda h, qt, *_: (h, qt, 0))]
    operands = [query_heads]
    for pack, pos, doc in zip(packs, positions, docs_rows):
        in_specs += [
            pl.BlockSpec((count, LANES), lambda h, qt, *_: (0, h)),
            pl.BlockSpec((count, LANES), lambda h, qt, *_: (0, heads_here + h)),
            pl.BlockSpec((count, LANES), lambda h, qt, *_: (0, 2 * heads_here)),
            pl.BlockSpec((1, count), lambda h, qt, *_: (0, 0)),
            pl.BlockSpec((1, count), lambda h, qt, *_: (0, 0)),
        ]
        operands += [pack, pack, pack, pos, doc.reshape(1, count)]
    in_specs.append(pl.BlockSpec((bq, 1), lambda h, qt, *_: (qt, 0)))
    operands.append(query_docs.reshape(rows, 1))

    kernel = functools.partial(
        flash_kernel, sets=sets, tiles=tiles, factor=1.0 / math.sqrt(NOPE_DIM + ROPE_DIM)
    )
    grid_spec = pltpu.PrefetchScalarGridSpec(
        num_scalar_prefetch=5,
        grid=(heads_here, q_tiles),
        in_specs=in_specs,
        out_specs=pl.BlockSpec((bq, LANES), lambda h, qt, *_: (qt, h)),
        scratch_shapes=[
            pltpu.VMEM((bq, 1), jnp.float32),
            pltpu.VMEM((bq, 1), jnp.float32),
            pltpu.VMEM((bq, LANES), jnp.float32),
        ],
    )
    return pl.pallas_call(
        kernel,
        grid_spec=grid_spec,
        out_shape=jax.ShapeDtypeStruct((rows, heads_here * LANES), jnp.bfloat16),
        compiler_params=pltpu.CompilerParams(dimension_semantics=("arbitrary", "arbitrary")),
    )(query_base, kminp, kmaxp, kmind, kmaxd, *operands)


def ring_tables(order):
    count = len(order)
    place = {device: number for number, device in enumerate(order)}
    ahead = count // 2
    behind = count - 1 - ahead
    sources = [list(range(count))]
    for step in range(1, ahead + 1):
        sources.append([order[(place[d] - step) % count] for d in range(count)])
        if step <= behind:
            sources.append([order[(place[d] + step) % count] for d in range(count)])
    source_of = np.zeros((count, count), np.int32)
    slot_of = np.zeros((count, count), np.int32)
    for number, row in enumerate(sources):
        for device, source in enumerate(row):
            source_of[device, number] = source
            slot_of[device, source] = number
    me = lax.axis_index("tp")
    return jnp.asarray(source_of)[me], jnp.asarray(slot_of)[me]


def ring_gather(block, order, early, source_of):
    count = len(order)
    place = {device: number for number, device in enumerate(order)}
    forward = [(order[i], order[(i + 1) % count]) for i in range(count)]
    backward = [(order[(i + 1) % count], order[i]) for i in range(count)]
    ahead = count // 2
    behind = count - 1 - ahead
    arrived = [block]
    moving_f = block
    moving_b = block
    for step in range(1, ahead + 1):
        moving_f = lax.ppermute(moving_f, "tp", forward)
        if step <= behind:
            moving_b = lax.ppermute(moving_b, "tp", backward)
        if step == 1:
            moving_f, moving_b, early = lax.optimization_barrier((moving_f, moving_b, early))
        arrived.append(moving_f)
        if step <= behind:
            arrived.append(moving_b)
    placed = []
    for part, _ in enumerate(block):
        rows = block[part].shape[0]
        buffer = jnp.zeros((count * rows,) + block[part].shape[1:], block[part].dtype)
        for number, piece in enumerate(arrived):
            at = (source_of[number] * rows,) + (0,) * (block[part].ndim - 1)
            buffer = lax.dynamic_update_slice(buffer, piece[part], at)
        placed.append(buffer)
    return tuple(placed), early


def body(queries, latent_rows, doc_ids, key_weight, value_weight, *, order):
    block_rows = queries.shape[0]
    chunk_rows = latent_rows.shape[0]
    chunks = block_rows // chunk_rows
    cycle_size = lax.axis_size("ctx")
    cycle_index = lax.axis_index("ctx")
    heads_here = key_weight.shape[1] // NOPE_DIM
    width = latent_rows.shape[1]
    pad = (-(width - KV_RANK)) % LANES
    source_of, slot_of = ring_tables(order)
    offsets = jnp.arange(block_rows, dtype=jnp.int32)
    positions = []
    for distance in range(cycle_size - 1, 0, -1):
        source = cycle_index - distance
        positions.append(jnp.where(source >= 0, source * block_rows + offsets, FAR))
    positions.append(cycle_index * block_rows + offsets)
    pos_tiles = jnp.concatenate(positions, axis=0).reshape(-1, BLOCK_K)
    pos_tables = (jnp.min(pos_tiles, axis=1), jnp.max(pos_tiles, axis=1))
    query_base = (cycle_index * block_rows).astype(jnp.int32).reshape(1)
    query_heads = jnp.transpose(queries, (1, 0, 2))
    early = (tuple(pos.reshape(1, -1) for pos in positions), pos_tables, query_base, query_heads)
    (gathered, docs), early = ring_gather((latent_rows, doc_ids), order, early, source_of)
    positions, pos_tables, query_base, query_heads = early
    latent_part = gathered[:, :KV_RANK]
    key_heads = jnp.dot(latent_part, key_weight, preferred_element_type=jnp.float32).astype(
        jnp.bfloat16
    )
    value_heads = jnp.dot(latent_part, value_weight, preferred_element_type=jnp.float32).astype(
        jnp.bfloat16
    )
    pack = jnp.concatenate(
        [key_heads, value_heads, gathered[:, KV_RANK:], jnp.zeros((block_rows, pad), jnp.bfloat16)],
        axis=1,
    )
    query_docs = docs

    packs, docs_rows = [], []
    for distance in range(cycle_size - 1, 0, -1):
        route = [(i - distance, i) for i in range(cycle_size) if i - distance >= 0]
        moved, moved_docs = lax.ppermute((pack, docs), "ctx", route)
        packs.append(moved)
        docs_rows.append(moved_docs)
    packs.append(pack)
    docs_rows.append(docs)
    return flash(query_heads, packs, positions, pos_tables, docs_rows, query_docs, query_base)


def ring_order(mesh):
    line = list(mesh.devices[(0,) * (mesh.devices.ndim - 1)].reshape(-1))
    try:
        where = {(d.coords[0], d.coords[2]): number for number, d in enumerate(line)}
        xs = sorted({key[0] for key in where})
        zs = sorted({key[1] for key in where})
        order = []
        for turn, x in enumerate(xs):
            for z in zs if turn % 2 == 0 else zs[::-1]:
                order.append(where[(x, z)])
    except (AttributeError, KeyError, IndexError, TypeError):
        return list(range(len(line)))
    if sorted(order) != list(range(len(line))):
        return list(range(len(line)))
    return order


def solution(mesh):
    placed = (
        P(("grp", "ctx"), "tp", None),
        P(("grp", "ctx", "tp"), None),
        P(("grp", "ctx", "tp")),
        P(None, "tp"),
        P(None, "tp"),
    )
    return jax.shard_map(
        functools.partial(body, order=ring_order(mesh)),
        mesh=mesh,
        in_specs=placed,
        out_specs=P(("grp", "ctx"), "tp"),
        check_vma=False,
    )
```

```python
import functools
import math

import jax
import jax.numpy as jnp
import numpy as np
from jax import lax
from jax.experimental import pallas as pl
from jax.experimental.pallas import tpu as pltpu
from jax.sharding import PartitionSpec as P

KV_RANK = 512
ROPE_DIM = 64
NOPE_DIM = 128
LANES = 128
BLOCK_Q = 512
BLOCK_K = 512
FAR = 1 << 30


def flash_kernel(
    qbase_ref, kminp_ref, kmaxp_ref, kmind_ref, kmaxd_ref,
    q_ref, *rest, sets, tiles, factor,
):
    set_refs = [rest[4 * n : 4 * n + 4] for n in range(sets)]
    qd_ref, o_ref = rest[4 * sets], rest[4 * sets + 1]
    qt = pl.program_id(1)
    bq = q_ref.shape[0]
    bk = BLOCK_K
    first_pos = qbase_ref[0] + qt * bq
    last_pos = first_pos + (bq - 1)
    own = (sets - 1) * tiles + qt
    first_doc = kmind_ref[own]
    last_doc = kmaxd_ref[own]
    q = q_ref[...]
    q_nope = q[:, :NOPE_DIM]
    q_rope = q[:, NOPE_DIM:]
    q_pos = first_pos + lax.broadcasted_iota(jnp.int32, (bq, 1), 0)
    q_doc = qd_ref[:, :1]
    nt = (((1,), (1,)), ((), ()))

    m_sc, l_sc, acc_sc = rest[4 * sets + 2 :]
    m_sc[...] = jnp.full(m_sc.shape, -1e30, jnp.float32)
    l_sc[...] = jnp.zeros(l_sc.shape, jnp.float32)
    acc_sc[...] = jnp.zeros(acc_sc.shape, jnp.float32)

    def make_step(number, k_ref, v_ref, r_ref, kd_ref):
        def tile(masked, t):
            at = number * tiles + t
            start = pl.multiple_of(t * bk, bk)
            keys = k_ref[pl.ds(start, bk), :]
            ropes = r_ref[pl.ds(start, bk), :]
            scores = lax.dot_general(q_nope, keys, nt, preferred_element_type=jnp.float32)
            scores = scores + lax.dot_general(
                q_rope, ropes[:, :ROPE_DIM], nt, preferred_element_type=jnp.float32
            )
            scores = scores * factor
            if masked:
                k_pos = kminp_ref[at] + lax.broadcasted_iota(jnp.int32, (1, bk), 1)
                k_doc = kd_ref[:, pl.ds(start, bk)]
                visible = (k_pos <= q_pos) & (k_doc == q_doc)
                scores = jnp.where(visible, scores, jnp.float32(-1e30))
            m_prev = m_sc[...]
            m_new = jnp.maximum(m_prev, jnp.max(scores, axis=1, keepdims=True))
            alpha = jnp.exp(m_prev - m_new)
            weights = jnp.exp(scores - m_new)
            l_sc[...] = alpha * l_sc[...] + jnp.sum(weights, axis=1, keepdims=True)
            acc_sc[...] = alpha * acc_sc[...] + jnp.dot(
                weights.astype(jnp.bfloat16),
                v_ref[pl.ds(start, bk), :],
                preferred_element_type=jnp.float32,
            )
            m_sc[...] = m_new

        def step(t, carry):
            at = number * tiles + t
            active = (
                (kminp_ref[at] <= last_pos)
                & (kmaxd_ref[at] >= first_doc)
                & (kmind_ref[at] <= last_doc)
            )
            full = (
                (kmaxp_ref[at] <= first_pos)
                & (kmind_ref[at] == last_doc)
                & (kmaxd_ref[at] == first_doc)
            )

            @pl.when(active & full)
            def _():
                tile(False, t)

            @pl.when(active & jnp.logical_not(full))
            def _():
                tile(True, t)

            return carry

        return step

    for number, refs in enumerate(set_refs):
        lax.fori_loop(0, tiles, make_step(number, *refs), 0)
    o_ref[...] = (acc_sc[...] / l_sc[...]).astype(o_ref.dtype)


def flash(query_heads, packs, pos_tables, docs_rows, query_docs, query_base):
    heads_here, rows, _ = query_heads.shape
    count = packs[0].shape[0]
    bq = min(BLOCK_Q, rows)
    bk = BLOCK_K
    q_tiles = rows // bq
    tiles = count // bk
    sets = len(packs)
    assert bq == bk and rows == count
    kminp, kmaxp = pos_tables
    doc_tiles = jnp.concatenate(docs_rows, axis=0).reshape(sets * tiles, bk)
    kmind = jnp.min(doc_tiles, axis=1)
    kmaxd = jnp.max(doc_tiles, axis=1)

    in_specs = [pl.BlockSpec((None, bq, query_heads.shape[2]), lambda h, qt, *_: (h, qt, 0))]
    operands = [query_heads]
    for pack, doc in zip(packs, docs_rows):
        in_specs += [
            pl.BlockSpec((count, LANES), lambda h, qt, *_: (0, h)),
            pl.BlockSpec((count, LANES), lambda h, qt, *_: (0, heads_here + h)),
            pl.BlockSpec((count, LANES), lambda h, qt, *_: (0, 2 * heads_here)),
            pl.BlockSpec((1, count), lambda h, qt, *_: (0, 0)),
        ]
        operands += [pack, pack, pack, doc.reshape(1, count)]
    in_specs.append(pl.BlockSpec((bq, LANES), lambda h, qt, *_: (qt, 0)))
    operands.append(jnp.broadcast_to(query_docs[:, None], (rows, LANES)))

    kernel = functools.partial(
        flash_kernel, sets=sets, tiles=tiles, factor=1.0 / math.sqrt(NOPE_DIM + ROPE_DIM)
    )
    grid_spec = pltpu.PrefetchScalarGridSpec(
        num_scalar_prefetch=5,
        grid=(heads_here, q_tiles),
        in_specs=in_specs,
        out_specs=pl.BlockSpec((bq, LANES), lambda h, qt, *_: (qt, h)),
        scratch_shapes=[
            pltpu.VMEM((bq, 1), jnp.float32),
            pltpu.VMEM((bq, 1), jnp.float32),
            pltpu.VMEM((bq, LANES), jnp.float32),
        ],
    )
    return pl.pallas_call(
        kernel,
        grid_spec=grid_spec,
        out_shape=jax.ShapeDtypeStruct((rows, heads_here * LANES), jnp.bfloat16),
        compiler_params=pltpu.CompilerParams(dimension_semantics=("arbitrary", "arbitrary")),
    )(query_base, kminp, kmaxp, kmind, kmaxd, *operands)


def ring_tables(order):
    count = len(order)
    place = {device: number for number, device in enumerate(order)}
    ahead = count // 2
    behind = count - 1 - ahead
    sources = [list(range(count))]
    for step in range(1, ahead + 1):
        sources.append([order[(place[d] - step) % count] for d in range(count)])
        if step <= behind:
            sources.append([order[(place[d] + step) % count] for d in range(count)])
    source_of = np.zeros((count, count), np.int32)
    slot_of = np.zeros((count, count), np.int32)
    for number, row in enumerate(sources):
        for device, source in enumerate(row):
            source_of[device, number] = source
            slot_of[device, source] = number
    me = lax.axis_index("tp")
    return jnp.asarray(source_of)[me], jnp.asarray(slot_of)[me]


def ring_gather(block, order, early, source_of):
    count = len(order)
    place = {device: number for number, device in enumerate(order)}
    forward = [(order[i], order[(i + 1) % count]) for i in range(count)]
    backward = [(order[(i + 1) % count], order[i]) for i in range(count)]
    ahead = count // 2
    behind = count - 1 - ahead
    arrived = [block]
    moving_f = block
    moving_b = block
    for step in range(1, ahead + 1):
        moving_f = lax.ppermute(moving_f, "tp", forward)
        if step <= behind:
            moving_b = lax.ppermute(moving_b, "tp", backward)
        if step == 1:
            moving_f, moving_b, early = lax.optimization_barrier((moving_f, moving_b, early))
        arrived.append(moving_f)
        if step <= behind:
            arrived.append(moving_b)
    rows = block.shape[0]
    placed = jnp.zeros((count * rows, block.shape[1]), block.dtype)
    for number, piece in enumerate(arrived):
        placed = lax.dynamic_update_slice(placed, piece, (source_of[number] * rows, 0))
    return placed, early


def body(queries, latent_rows, doc_ids, key_weight, value_weight, *, order):
    block_rows = queries.shape[0]
    chunk_rows = latent_rows.shape[0]
    chunks = block_rows // chunk_rows
    cycle_size = lax.axis_size("ctx")
    cycle_index = lax.axis_index("ctx")
    heads_here = key_weight.shape[1] // NOPE_DIM
    width = latent_rows.shape[1]
    pad = (-(width + 1)) % LANES
    doc_column = jnp.concatenate(
        [doc_ids.astype(jnp.bfloat16)[:, None], jnp.zeros((chunk_rows, pad), jnp.bfloat16)],
        axis=1,
    )
    chunk = jnp.concatenate([latent_rows, doc_column], axis=1)
    source_of, slot_of = ring_tables(order)
    offsets = jnp.arange(block_rows, dtype=jnp.int32)
    positions = []
    for distance in range(cycle_size - 1, 0, -1):
        source = cycle_index - distance
        positions.append(jnp.where(source >= 0, source * block_rows + offsets, FAR))
    positions.append(cycle_index * block_rows + offsets)
    pos_tiles = jnp.concatenate(positions, axis=0).reshape(-1, BLOCK_K)
    pos_tables = (jnp.min(pos_tiles, axis=1), jnp.max(pos_tiles, axis=1))
    query_base = (cycle_index * block_rows).astype(jnp.int32).reshape(1)
    query_heads = jnp.transpose(queries, (1, 0, 2))
    early = (pos_tables, query_base, query_heads)
    gathered, early = ring_gather(chunk, order, early, source_of)
    pos_tables, query_base, query_heads = early
    latent_part = gathered[:, :KV_RANK]
    key_heads = jnp.dot(latent_part, key_weight, preferred_element_type=jnp.float32).astype(
        jnp.bfloat16
    )
    value_heads = jnp.dot(latent_part, value_weight, preferred_element_type=jnp.float32).astype(
        jnp.bfloat16
    )
    pack = jnp.concatenate([key_heads, value_heads, gathered[:, KV_RANK:]], axis=1)
    docs = gathered[:, width].astype(jnp.int32)
    query_docs = docs

    packs, docs_rows = [], []
    for distance in range(cycle_size - 1, 0, -1):
        route = [(i - distance, i) for i in range(cycle_size) if i - distance >= 0]
        moved = lax.ppermute(pack, "ctx", route)
        packs.append(moved)
        docs_rows.append(moved[:, 2 * heads_here * NOPE_DIM + ROPE_DIM].astype(jnp.int32))
    packs.append(pack)
    docs_rows.append(docs)
    return flash(query_heads, packs, pos_tables, docs_rows, query_docs, query_base)


def ring_order(mesh):
    line = list(mesh.devices[(0,) * (mesh.devices.ndim - 1)].reshape(-1))
    try:
        where = {(d.coords[0], d.coords[2]): number for number, d in enumerate(line)}
        xs = sorted({key[0] for key in where})
        zs = sorted({key[1] for key in where})
        order = []
        for turn, x in enumerate(xs):
            for z in zs if turn % 2 == 0 else zs[::-1]:
                order.append(where[(x, z)])
    except (AttributeError, KeyError, IndexError, TypeError):
        return list(range(len(line)))
    if sorted(order) != list(range(len(line))):
        return list(range(len(line)))
    return order


def solution(mesh):
    placed = (
        P(("grp", "ctx"), "tp", None),
        P(("grp", "ctx", "tp"), None),
        P(("grp", "ctx", "tp")),
        P(None, "tp"),
        P(None, "tp"),
    )
    return jax.shard_map(
        functools.partial(body, order=ring_order(mesh)),
        mesh=mesh,
        in_specs=placed,
        out_specs=P(("grp", "ctx"), "tp"),
        check_vma=False,
    )
```

```python
import functools
import math

import jax
import jax.numpy as jnp
import numpy as np
from jax import lax
from jax.experimental import pallas as pl
from jax.experimental.pallas import tpu as pltpu
from jax.sharding import PartitionSpec as P

KV_RANK = 512
ROPE_DIM = 64
NOPE_DIM = 128
LANES = 128
BLOCK_Q = 512
BLOCK_K = 512
FAR = 1 << 30


def flash_kernel(
    qbase_ref, qdf_ref, qdl_ref, kminp_ref, kmaxp_ref, kmind_ref, kmaxd_ref,
    q_ref, *rest, sets, tiles, factor, carry_in, final,
):
    set_refs = [rest[4 * n : 4 * n + 4] for n in range(sets)]
    rest = rest[4 * sets :]
    qd_ref, rest = rest[0], rest[1:]
    if carry_in:
        m_in, l_in, acc_in, rest = rest[0], rest[1], rest[2], rest[3:]
    if final:
        o_ref, rest = rest[0], rest[1:]
    else:
        m_out, l_out, acc_out, rest = rest[0], rest[1], rest[2], rest[3:]
    qt = pl.program_id(1)
    bq = q_ref.shape[0]
    bk = BLOCK_K
    first_pos = qbase_ref[0] + qt * bq
    last_pos = first_pos + (bq - 1)
    first_doc = qdf_ref[qt]
    last_doc = qdl_ref[qt]
    q = q_ref[...]
    q_nope = q[:, :NOPE_DIM]
    q_rope = q[:, NOPE_DIM:]
    q_pos = first_pos + lax.broadcasted_iota(jnp.int32, (bq, 1), 0)
    q_doc = qd_ref[:, :1]
    nt = (((1,), (1,)), ((), ()))

    m_sc, l_sc, acc_sc = rest
    if carry_in:
        m_sc[...] = m_in[:, :1]
        l_sc[...] = l_in[:, :1]
        acc_sc[...] = acc_in[...]
    else:
        m_sc[...] = jnp.full(m_sc.shape, -1e30, jnp.float32)
        l_sc[...] = jnp.zeros(l_sc.shape, jnp.float32)
        acc_sc[...] = jnp.zeros(acc_sc.shape, jnp.float32)

    def make_step(number, k_ref, v_ref, r_ref, kd_ref):
        def tile(masked, t):
            at = number * tiles + t
            start = pl.multiple_of(t * bk, bk)
            keys = k_ref[pl.ds(start, bk), :]
            ropes = r_ref[pl.ds(start, bk), :]
            scores = lax.dot_general(q_nope, keys, nt, preferred_element_type=jnp.float32)
            scores = scores + lax.dot_general(
                q_rope, ropes[:, :ROPE_DIM], nt, preferred_element_type=jnp.float32
            )
            scores = scores * factor
            if masked:
                k_pos = kminp_ref[at] + lax.broadcasted_iota(jnp.int32, (1, bk), 1)
                k_doc = kd_ref[:, pl.ds(start, bk)]
                visible = (k_pos <= q_pos) & (k_doc == q_doc)
                scores = jnp.where(visible, scores, jnp.float32(-1e30))
            m_prev = m_sc[...]
            m_new = jnp.maximum(m_prev, jnp.max(scores, axis=1, keepdims=True))
            alpha = jnp.exp(m_prev - m_new)
            weights = jnp.exp(scores - m_new)
            l_sc[...] = alpha * l_sc[...] + jnp.sum(weights, axis=1, keepdims=True)
            acc_sc[...] = alpha * acc_sc[...] + jnp.dot(
                weights.astype(jnp.bfloat16),
                v_ref[pl.ds(start, bk), :],
                preferred_element_type=jnp.float32,
            )
            m_sc[...] = m_new

        def step(t, carry):
            at = number * tiles + t
            active = (
                (kminp_ref[at] <= last_pos)
                & (kmaxd_ref[at] >= first_doc)
                & (kmind_ref[at] <= last_doc)
            )
            full = (
                (kmaxp_ref[at] <= first_pos)
                & (kmind_ref[at] == last_doc)
                & (kmaxd_ref[at] == first_doc)
            )

            @pl.when(active & full)
            def _():
                tile(False, t)

            @pl.when(active & jnp.logical_not(full))
            def _():
                tile(True, t)

            return carry

        return step

    for number, refs in enumerate(set_refs):
        lax.fori_loop(0, tiles, make_step(number, *refs), 0)
    if final:
        o_ref[...] = (acc_sc[...] / l_sc[...]).astype(o_ref.dtype)
    else:
        m_out[...] = jnp.broadcast_to(m_sc[...], m_out.shape)
        l_out[...] = jnp.broadcast_to(l_sc[...], l_out.shape)
        acc_out[...] = acc_sc[...]


def flash(query_heads, packs, pos_tables, docs_rows, query_docs, query_base, qdocs, state):
    heads_here, rows, _ = query_heads.shape
    count = packs[0].shape[0]
    bq = min(BLOCK_Q, rows)
    bk = BLOCK_K
    q_tiles = rows // bq
    tiles = count // bk
    sets = len(packs)
    assert bq == bk and rows == count
    kminp, kmaxp = pos_tables
    doc_tiles = jnp.concatenate(docs_rows, axis=0).reshape(sets * tiles, bk)
    kmind = jnp.min(doc_tiles, axis=1)
    kmaxd = jnp.max(doc_tiles, axis=1)
    if qdocs is None:
        qdocs = (kmind[-q_tiles:], kmaxd[-q_tiles:], query_docs)
    qdf, qdl, query_docs = qdocs

    in_specs = [pl.BlockSpec((None, bq, query_heads.shape[2]), lambda h, qt, *_: (h, qt, 0))]
    operands = [query_heads]
    for pack, doc in zip(packs, docs_rows):
        in_specs += [
            pl.BlockSpec((count, LANES), lambda h, qt, *_: (0, h)),
            pl.BlockSpec((count, LANES), lambda h, qt, *_: (0, heads_here + h)),
            pl.BlockSpec((count, LANES), lambda h, qt, *_: (0, 2 * heads_here)),
            pl.BlockSpec((1, count), lambda h, qt, *_: (0, 0)),
        ]
        operands += [pack, pack, pack, doc.reshape(1, count)]
    if query_docs.ndim == 1:
        query_docs = jnp.broadcast_to(query_docs[:, None], (rows, LANES))
    in_specs.append(pl.BlockSpec((bq, LANES), lambda h, qt, *_: (qt, 0)))
    operands.append(query_docs)
    tile_spec = pl.BlockSpec((bq, LANES), lambda h, qt, *_: (qt, h))
    if state is not None:
        in_specs += [tile_spec] * 3
        operands += list(state)
    final = state is not None
    wide = jax.ShapeDtypeStruct((rows, heads_here * LANES), jnp.float32)
    if final:
        out_shape = jax.ShapeDtypeStruct((rows, heads_here * LANES), jnp.bfloat16)
        out_specs = tile_spec
    else:
        out_shape = (wide, wide, wide)
        out_specs = (tile_spec, tile_spec, tile_spec)

    kernel = functools.partial(
        flash_kernel, sets=sets, tiles=tiles, factor=1.0 / math.sqrt(NOPE_DIM + ROPE_DIM),
        carry_in=state is not None, final=final,
    )
    grid_spec = pltpu.PrefetchScalarGridSpec(
        num_scalar_prefetch=7,
        grid=(heads_here, q_tiles),
        in_specs=in_specs,
        out_specs=out_specs,
        scratch_shapes=[
            pltpu.VMEM((bq, 1), jnp.float32),
            pltpu.VMEM((bq, 1), jnp.float32),
            pltpu.VMEM((bq, LANES), jnp.float32),
        ],
    )
    result = pl.pallas_call(
        kernel,
        grid_spec=grid_spec,
        out_shape=out_shape,
        compiler_params=pltpu.CompilerParams(dimension_semantics=("arbitrary", "arbitrary")),
    )(query_base, qdf, qdl, kminp, kmaxp, kmind, kmaxd, *operands)
    return result if final else (result, (qdf, qdl, query_docs))


def ring_tables(order):
    count = len(order)
    place = {device: number for number, device in enumerate(order)}
    ahead = count // 2
    behind = count - 1 - ahead
    sources = [list(range(count))]
    for step in range(1, ahead + 1):
        sources.append([order[(place[d] - step) % count] for d in range(count)])
        if step <= behind:
            sources.append([order[(place[d] + step) % count] for d in range(count)])
    source_of = np.zeros((count, count), np.int32)
    slot_of = np.zeros((count, count), np.int32)
    for number, row in enumerate(sources):
        for device, source in enumerate(row):
            source_of[device, number] = source
            slot_of[device, source] = number
    me = lax.axis_index("tp")
    return jnp.asarray(source_of)[me], jnp.asarray(slot_of)[me]


def ring_gather(block, order, early, source_of):
    count = len(order)
    place = {device: number for number, device in enumerate(order)}
    forward = [(order[i], order[(i + 1) % count]) for i in range(count)]
    backward = [(order[(i + 1) % count], order[i]) for i in range(count)]
    ahead = count // 2
    behind = count - 1 - ahead
    arrived = [block]
    moving_f = block
    moving_b = block
    for step in range(1, ahead + 1):
        moving_f = lax.ppermute(moving_f, "tp", forward)
        if step <= behind:
            moving_b = lax.ppermute(moving_b, "tp", backward)
        if step == 1:
            moving_f, moving_b, early = lax.optimization_barrier((moving_f, moving_b, early))
        arrived.append(moving_f)
        if step <= behind:
            arrived.append(moving_b)
    rows = block.shape[0]
    placed = jnp.zeros((count * rows, block.shape[1]), block.dtype)
    for number, piece in enumerate(arrived):
        placed = lax.dynamic_update_slice(placed, piece, (source_of[number] * rows, 0))
    return placed, early


def body(queries, latent_rows, doc_ids, key_weight, value_weight, *, order):
    block_rows = queries.shape[0]
    chunk_rows = latent_rows.shape[0]
    chunks = block_rows // chunk_rows
    cycle_size = lax.axis_size("ctx")
    cycle_index = lax.axis_index("ctx")
    heads_here = key_weight.shape[1] // NOPE_DIM
    width = latent_rows.shape[1]
    pad = (-(width + 1)) % LANES
    doc_column = jnp.concatenate(
        [doc_ids.astype(jnp.bfloat16)[:, None], jnp.zeros((chunk_rows, pad), jnp.bfloat16)],
        axis=1,
    )
    chunk = jnp.concatenate([latent_rows, doc_column], axis=1)
    source_of, slot_of = ring_tables(order)
    offsets = jnp.arange(block_rows, dtype=jnp.int32)
    positions = []
    for distance in range(cycle_size - 1, 0, -1):
        source = cycle_index - distance
        positions.append(jnp.where(source >= 0, source * block_rows + offsets, FAR))
    positions.append(cycle_index * block_rows + offsets)
    def tables_of(group):
        tiles_of = jnp.concatenate(group, axis=0).reshape(-1, BLOCK_K)
        return (jnp.min(tiles_of, axis=1), jnp.max(tiles_of, axis=1))

    pos_tables = (tables_of(positions[:-1]), tables_of(positions[-1:]))
    query_base = (cycle_index * block_rows).astype(jnp.int32).reshape(1)
    query_heads = jnp.transpose(queries, (1, 0, 2))
    early = (pos_tables, query_base, query_heads)
    gathered, early = ring_gather(chunk, order, early, source_of)
    pos_tables, query_base, query_heads = early
    latent_part = gathered[:, :KV_RANK]
    key_heads = jnp.dot(latent_part, key_weight, preferred_element_type=jnp.float32).astype(
        jnp.bfloat16
    )
    value_heads = jnp.dot(latent_part, value_weight, preferred_element_type=jnp.float32).astype(
        jnp.bfloat16
    )
    pack = jnp.concatenate([key_heads, value_heads, gathered[:, KV_RANK:]], axis=1)
    docs = gathered[:, width].astype(jnp.int32)
    query_docs = docs

    packs, docs_rows = [], []
    for distance in range(cycle_size - 1, 0, -1):
        route = [(i - distance, i) for i in range(cycle_size) if i - distance >= 0]
        moved = lax.ppermute(pack, "ctx", route)
        packs.append(moved)
        docs_rows.append(moved[:, 2 * heads_here * NOPE_DIM + ROPE_DIM].astype(jnp.int32))
    packs.append(pack)
    docs_rows.append(docs)
    state, qdocs = flash(
        query_heads, packs[-1:], pos_tables[1], docs_rows[-1:], query_docs, query_base, None, None
    )
    return flash(
        query_heads, packs[:-1], pos_tables[0], docs_rows[:-1], None, query_base, qdocs, state
    )


def ring_order(mesh):
    line = list(mesh.devices[(0,) * (mesh.devices.ndim - 1)].reshape(-1))
    try:
        where = {(d.coords[0], d.coords[2]): number for number, d in enumerate(line)}
        xs = sorted({key[0] for key in where})
        zs = sorted({key[1] for key in where})
        order = []
        for turn, x in enumerate(xs):
            for z in zs if turn % 2 == 0 else zs[::-1]:
                order.append(where[(x, z)])
    except (AttributeError, KeyError, IndexError, TypeError):
        return list(range(len(line)))
    if sorted(order) != list(range(len(line))):
        return list(range(len(line)))
    return order


def solution(mesh):
    placed = (
        P(("grp", "ctx"), "tp", None),
        P(("grp", "ctx", "tp"), None),
        P(("grp", "ctx", "tp")),
        P(None, "tp"),
        P(None, "tp"),
    )
    return jax.shard_map(
        functools.partial(body, order=ring_order(mesh)),
        mesh=mesh,
        in_specs=placed,
        out_specs=P(("grp", "ctx"), "tp"),
        check_vma=False,
    )
```

```python
import functools
import math

import jax
import jax.numpy as jnp
import numpy as np
from jax import lax
from jax.experimental import pallas as pl
from jax.experimental.pallas import tpu as pltpu
from jax.sharding import PartitionSpec as P

KV_RANK = 512
ROPE_DIM = 64
NOPE_DIM = 128
LANES = 128
BLOCK_Q = 512
BLOCK_K = 512
FAR = 1 << 30


def flash_kernel(
    qbase_ref, kminp_ref, kmaxp_ref, kmind_ref, kmaxd_ref,
    q_ref, *rest, sets, tiles, factor,
):
    set_refs = [rest[4 * n : 4 * n + 4] for n in range(sets)]
    o_ref = rest[4 * sets]
    qt = pl.program_id(1)
    bq = q_ref.shape[0]
    bk = BLOCK_K
    first_pos = qbase_ref[0] + qt * bq
    last_pos = first_pos + (bq - 1)
    own = (sets - 1) * tiles + qt
    first_doc = kmind_ref[own]
    last_doc = kmaxd_ref[own]
    q = q_ref[...]
    q_nope = q[:, :NOPE_DIM]
    q_rope = q[:, NOPE_DIM:]
    q_pos = first_pos + lax.broadcasted_iota(jnp.int32, (bq, 1), 0)
    own_docs = set_refs[-1][3][:, pl.ds(pl.multiple_of(qt * bq, bq), bq)]
    q_doc = jnp.transpose(jnp.broadcast_to(own_docs, (8, bq)))[:, :1]
    nt = (((1,), (1,)), ((), ()))

    m_sc, l_sc, acc_sc = rest[4 * sets + 1 :]
    m_sc[...] = jnp.full(m_sc.shape, -1e30, jnp.float32)
    l_sc[...] = jnp.zeros(l_sc.shape, jnp.float32)
    acc_sc[...] = jnp.zeros(acc_sc.shape, jnp.float32)

    def make_step(number, k_ref, v_ref, r_ref, kd_ref):
        def tile(masked, t):
            at = number * tiles + t
            start = pl.multiple_of(t * bk, bk)
            keys = k_ref[pl.ds(start, bk), :]
            ropes = r_ref[pl.ds(start, bk), :]
            scores = lax.dot_general(q_nope, keys, nt, preferred_element_type=jnp.float32)
            scores = scores + lax.dot_general(
                q_rope, ropes[:, :ROPE_DIM], nt, preferred_element_type=jnp.float32
            )
            scores = scores * factor
            if masked:
                k_pos = kminp_ref[at] + lax.broadcasted_iota(jnp.int32, (1, bk), 1)
                k_doc = kd_ref[:, pl.ds(start, bk)]
                visible = (k_pos <= q_pos) & (k_doc == q_doc)
                scores = jnp.where(visible, scores, jnp.float32(-1e30))
            m_prev = m_sc[...]
            m_new = jnp.maximum(m_prev, jnp.max(scores, axis=1, keepdims=True))
            alpha = jnp.exp(m_prev - m_new)
            weights = jnp.exp(scores - m_new)
            l_sc[...] = alpha * l_sc[...] + jnp.sum(weights, axis=1, keepdims=True)
            acc_sc[...] = alpha * acc_sc[...] + jnp.dot(
                weights.astype(jnp.bfloat16),
                v_ref[pl.ds(start, bk), :],
                preferred_element_type=jnp.float32,
            )
            m_sc[...] = m_new

        def step(t, carry):
            at = number * tiles + t
            active = (
                (kminp_ref[at] <= last_pos)
                & (kmaxd_ref[at] >= first_doc)
                & (kmind_ref[at] <= last_doc)
            )
            full = (
                (kmaxp_ref[at] <= first_pos)
                & (kmind_ref[at] == last_doc)
                & (kmaxd_ref[at] == first_doc)
            )

            @pl.when(active & full)
            def _():
                tile(False, t)

            @pl.when(active & jnp.logical_not(full))
            def _():
                tile(True, t)

            return carry

        return step

    for number, refs in enumerate(set_refs):
        lax.fori_loop(0, tiles, make_step(number, *refs), 0)
    o_ref[...] = (acc_sc[...] / l_sc[...]).astype(o_ref.dtype)


def flash(query_heads, packs, pos_tables, docs_rows, query_docs, query_base):
    heads_here, rows, _ = query_heads.shape
    count = packs[0].shape[0]
    bq = min(BLOCK_Q, rows)
    bk = BLOCK_K
    q_tiles = rows // bq
    tiles = count // bk
    sets = len(packs)
    assert bq == bk and rows == count
    kminp, kmaxp = pos_tables
    doc_tiles = jnp.concatenate(docs_rows, axis=0).reshape(sets * tiles, bk)
    kmind = jnp.min(doc_tiles, axis=1)
    kmaxd = jnp.max(doc_tiles, axis=1)

    in_specs = [pl.BlockSpec((None, bq, query_heads.shape[2]), lambda h, qt, *_: (h, qt, 0))]
    operands = [query_heads]
    for pack, doc in zip(packs, docs_rows):
        in_specs += [
            pl.BlockSpec((count, LANES), lambda h, qt, *_: (0, h)),
            pl.BlockSpec((count, LANES), lambda h, qt, *_: (0, heads_here + h)),
            pl.BlockSpec((count, LANES), lambda h, qt, *_: (0, 2 * heads_here)),
            pl.BlockSpec((1, count), lambda h, qt, *_: (0, 0)),
        ]
        operands += [pack, pack, pack, doc.reshape(1, count)]

    kernel = functools.partial(
        flash_kernel, sets=sets, tiles=tiles, factor=1.0 / math.sqrt(NOPE_DIM + ROPE_DIM)
    )
    grid_spec = pltpu.PrefetchScalarGridSpec(
        num_scalar_prefetch=5,
        grid=(heads_here, q_tiles),
        in_specs=in_specs,
        out_specs=pl.BlockSpec((bq, LANES), lambda h, qt, *_: (qt, h)),
        scratch_shapes=[
            pltpu.VMEM((bq, 1), jnp.float32),
            pltpu.VMEM((bq, 1), jnp.float32),
            pltpu.VMEM((bq, LANES), jnp.float32),
        ],
    )
    return pl.pallas_call(
        kernel,
        grid_spec=grid_spec,
        out_shape=jax.ShapeDtypeStruct((rows, heads_here * LANES), jnp.bfloat16),
        compiler_params=pltpu.CompilerParams(dimension_semantics=("arbitrary", "arbitrary")),
    )(query_base, kminp, kmaxp, kmind, kmaxd, *operands)


def ring_tables(order):
    count = len(order)
    place = {device: number for number, device in enumerate(order)}
    ahead = count // 2
    behind = count - 1 - ahead
    sources = [list(range(count))]
    for step in range(1, ahead + 1):
        sources.append([order[(place[d] - step) % count] for d in range(count)])
        if step <= behind:
            sources.append([order[(place[d] + step) % count] for d in range(count)])
    source_of = np.zeros((count, count), np.int32)
    slot_of = np.zeros((count, count), np.int32)
    for number, row in enumerate(sources):
        for device, source in enumerate(row):
            source_of[device, number] = source
            slot_of[device, source] = number
    me = lax.axis_index("tp")
    return jnp.asarray(source_of)[me], jnp.asarray(slot_of)[me]


def ring_gather(block, order, early, source_of):
    count = len(order)
    place = {device: number for number, device in enumerate(order)}
    forward = [(order[i], order[(i + 1) % count]) for i in range(count)]
    backward = [(order[(i + 1) % count], order[i]) for i in range(count)]
    ahead = count // 2
    behind = count - 1 - ahead
    arrived = [block]
    moving_f = block
    moving_b = block
    for step in range(1, ahead + 1):
        moving_f = lax.ppermute(moving_f, "tp", forward)
        if step <= behind:
            moving_b = lax.ppermute(moving_b, "tp", backward)
        if step == 1:
            moving_f, moving_b, early = lax.optimization_barrier((moving_f, moving_b, early))
        arrived.append(moving_f)
        if step <= behind:
            arrived.append(moving_b)
    rows = block.shape[0]
    placed = jnp.zeros((count * rows, block.shape[1]), block.dtype)
    for number, piece in enumerate(arrived):
        placed = lax.dynamic_update_slice(placed, piece, (source_of[number] * rows, 0))
    return placed, early


def body(queries, latent_rows, doc_ids, key_weight, value_weight, *, order):
    block_rows = queries.shape[0]
    chunk_rows = latent_rows.shape[0]
    chunks = block_rows // chunk_rows
    cycle_size = lax.axis_size("ctx")
    cycle_index = lax.axis_index("ctx")
    heads_here = key_weight.shape[1] // NOPE_DIM
    width = latent_rows.shape[1]
    pad = (-(width + 1)) % LANES
    doc_column = jnp.concatenate(
        [doc_ids.astype(jnp.bfloat16)[:, None], jnp.zeros((chunk_rows, pad), jnp.bfloat16)],
        axis=1,
    )
    chunk = jnp.concatenate([latent_rows, doc_column], axis=1)
    source_of, slot_of = ring_tables(order)
    offsets = jnp.arange(block_rows, dtype=jnp.int32)
    positions = []
    for distance in range(cycle_size - 1, 0, -1):
        source = cycle_index - distance
        positions.append(jnp.where(source >= 0, source * block_rows + offsets, FAR))
    positions.append(cycle_index * block_rows + offsets)
    pos_tiles = jnp.concatenate(positions, axis=0).reshape(-1, BLOCK_K)
    pos_tables = (jnp.min(pos_tiles, axis=1), jnp.max(pos_tiles, axis=1))
    query_base = (cycle_index * block_rows).astype(jnp.int32).reshape(1)
    query_heads = jnp.transpose(queries, (1, 0, 2))
    early = (pos_tables, query_base, query_heads)
    gathered, early = ring_gather(chunk, order, early, source_of)
    pos_tables, query_base, query_heads = early
    latent_part = gathered[:, :KV_RANK]
    key_heads = jnp.dot(latent_part, key_weight, preferred_element_type=jnp.float32).astype(
        jnp.bfloat16
    )
    value_heads = jnp.dot(latent_part, value_weight, preferred_element_type=jnp.float32).astype(
        jnp.bfloat16
    )
    pack = jnp.concatenate([key_heads, value_heads, gathered[:, KV_RANK:]], axis=1)
    docs = gathered[:, width].astype(jnp.int32)
    query_docs = docs

    packs, docs_rows = [], []
    for distance in range(cycle_size - 1, 0, -1):
        route = [(i - distance, i) for i in range(cycle_size) if i - distance >= 0]
        moved = lax.ppermute(pack, "ctx", route)
        packs.append(moved)
        docs_rows.append(moved[:, 2 * heads_here * NOPE_DIM + ROPE_DIM].astype(jnp.int32))
    packs.append(pack)
    docs_rows.append(docs)
    return flash(query_heads, packs, pos_tables, docs_rows, query_docs, query_base)


def ring_order(mesh):
    line = list(mesh.devices[(0,) * (mesh.devices.ndim - 1)].reshape(-1))
    try:
        where = {(d.coords[0], d.coords[2]): number for number, d in enumerate(line)}
        xs = sorted({key[0] for key in where})
        zs = sorted({key[1] for key in where})
        order = []
        for turn, x in enumerate(xs):
            for z in zs if turn % 2 == 0 else zs[::-1]:
                order.append(where[(x, z)])
    except (AttributeError, KeyError, IndexError, TypeError):
        return list(range(len(line)))
    if sorted(order) != list(range(len(line))):
        return list(range(len(line)))
    return order


def solution(mesh):
    placed = (
        P(("grp", "ctx"), "tp", None),
        P(("grp", "ctx", "tp"), None),
        P(("grp", "ctx", "tp")),
        P(None, "tp"),
        P(None, "tp"),
    )
    return jax.shard_map(
        functools.partial(body, order=ring_order(mesh)),
        mesh=mesh,
        in_specs=placed,
        out_specs=P(("grp", "ctx"), "tp"),
        check_vma=False,
    )
```

```python
import functools
import math

import jax
import jax.numpy as jnp
import numpy as np
from jax import lax
from jax.experimental import pallas as pl
from jax.experimental.pallas import tpu as pltpu
from jax.sharding import PartitionSpec as P

KV_RANK = 512
ROPE_DIM = 64
NOPE_DIM = 128
LANES = 128
BLOCK_Q = 512
BLOCK_K = 512
FAR = 1 << 30


def flash_kernel(
    qbase_ref, kminp_ref, kmaxp_ref, kmind_ref, kmaxd_ref,
    q_ref, *rest, sets, tiles, factor,
):
    set_refs = [rest[3 * n : 3 * n + 3] for n in range(sets)]
    o_ref = rest[3 * sets]
    qt = pl.program_id(1)
    bq = q_ref.shape[0]
    bk = BLOCK_K
    first_pos = qbase_ref[0] + qt * bq
    last_pos = first_pos + (bq - 1)
    own = (sets - 1) * tiles + qt
    first_doc = kmind_ref[own]
    last_doc = kmaxd_ref[own]
    q = q_ref[...]
    q_pos = first_pos + lax.broadcasted_iota(jnp.int32, (bq, 1), 0)
    own_docs = set_refs[-1][2][:, pl.ds(pl.multiple_of(qt * bq, bq), bq)]
    q_doc = jnp.transpose(jnp.broadcast_to(own_docs, (8, bq)))[:, :1]
    nt = (((1,), (1,)), ((), ()))

    m_sc, l_sc, acc_sc = rest[3 * sets + 1 :]
    m_sc[...] = jnp.full(m_sc.shape, -1e30, jnp.float32)
    l_sc[...] = jnp.zeros(l_sc.shape, jnp.float32)
    acc_sc[...] = jnp.zeros(acc_sc.shape, jnp.float32)

    def make_step(number, kr_ref, v_ref, kd_ref):
        def tile(masked, by_pos, t):
            at = number * tiles + t
            start = pl.multiple_of(t * bk, bk)
            keys = kr_ref[pl.ds(start, bk), :][:, : NOPE_DIM + ROPE_DIM]
            scores = lax.dot_general(q, keys, nt, preferred_element_type=jnp.float32)
            scores = scores * factor
            if masked:
                visible = kd_ref[:, pl.ds(start, bk)] == q_doc
                if by_pos:
                    k_pos = kminp_ref[at] + lax.broadcasted_iota(jnp.int32, (1, bk), 1)
                    visible = visible & (k_pos <= q_pos)
                scores = jnp.where(visible, scores, jnp.float32(-1e30))
            m_prev = m_sc[...]
            m_new = jnp.maximum(m_prev, jnp.max(scores, axis=1, keepdims=True))
            alpha = jnp.exp(m_prev - m_new)
            weights = jnp.exp(scores - m_new)
            l_sc[...] = alpha * l_sc[...] + jnp.sum(weights, axis=1, keepdims=True)
            acc_sc[...] = alpha * acc_sc[...] + jnp.dot(
                weights.astype(jnp.bfloat16),
                v_ref[pl.ds(start, bk), :],
                preferred_element_type=jnp.float32,
            )
            m_sc[...] = m_new

        def step(t, carry):
            at = number * tiles + t
            active = (
                (kminp_ref[at] <= last_pos)
                & (kmaxd_ref[at] >= first_doc)
                & (kmind_ref[at] <= last_doc)
            )
            before = kmaxp_ref[at] <= first_pos
            same = (kmind_ref[at] == last_doc) & (kmaxd_ref[at] == first_doc)

            @pl.when(active & before & same)
            def _():
                tile(False, False, t)

            @pl.when(active & before & jnp.logical_not(same))
            def _():
                tile(True, False, t)

            @pl.when(active & jnp.logical_not(before))
            def _():
                tile(True, True, t)

            return carry

        return step

    for number, refs in enumerate(set_refs):
        lax.fori_loop(0, tiles, make_step(number, *refs), 0)
    o_ref[...] = (acc_sc[...] / l_sc[...]).astype(o_ref.dtype)


def flash(query_heads, packs, pos_tables, docs_rows, query_docs, query_base):
    heads_here, rows, _ = query_heads.shape
    count = packs[0].shape[0]
    bq = min(BLOCK_Q, rows)
    bk = BLOCK_K
    q_tiles = rows // bq
    tiles = count // bk
    sets = len(packs)
    assert bq == bk and rows == count
    kminp, kmaxp = pos_tables
    doc_tiles = jnp.concatenate(docs_rows, axis=0).reshape(sets * tiles, bk)
    kmind = jnp.min(doc_tiles, axis=1)
    kmaxd = jnp.max(doc_tiles, axis=1)

    in_specs = [pl.BlockSpec((None, bq, query_heads.shape[2]), lambda h, qt, *_: (h, qt, 0))]
    operands = [query_heads]
    for pack, doc in zip(packs, docs_rows):
        in_specs += [
            pl.BlockSpec((count, 2 * LANES), lambda h, qt, *_: (0, 0)),
            pl.BlockSpec((count, LANES), lambda h, qt, *_: (0, 2)),
            pl.BlockSpec((1, count), lambda h, qt, *_: (0, 0)),
        ]
        operands += [pack, pack, doc.reshape(1, count)]

    kernel = functools.partial(
        flash_kernel, sets=sets, tiles=tiles, factor=1.0 / math.sqrt(NOPE_DIM + ROPE_DIM)
    )
    grid_spec = pltpu.PrefetchScalarGridSpec(
        num_scalar_prefetch=5,
        grid=(heads_here, q_tiles),
        in_specs=in_specs,
        out_specs=pl.BlockSpec((bq, LANES), lambda h, qt, *_: (qt, h)),
        scratch_shapes=[
            pltpu.VMEM((bq, 1), jnp.float32),
            pltpu.VMEM((bq, 1), jnp.float32),
            pltpu.VMEM((bq, LANES), jnp.float32),
        ],
    )
    return pl.pallas_call(
        kernel,
        grid_spec=grid_spec,
        out_shape=jax.ShapeDtypeStruct((rows, heads_here * LANES), jnp.bfloat16),
        compiler_params=pltpu.CompilerParams(dimension_semantics=("arbitrary", "arbitrary")),
    )(query_base, kminp, kmaxp, kmind, kmaxd, *operands)


def ring_tables(order):
    count = len(order)
    place = {device: number for number, device in enumerate(order)}
    ahead = count // 2
    behind = count - 1 - ahead
    sources = [list(range(count))]
    for step in range(1, ahead + 1):
        sources.append([order[(place[d] - step) % count] for d in range(count)])
        if step <= behind:
            sources.append([order[(place[d] + step) % count] for d in range(count)])
    source_of = np.zeros((count, count), np.int32)
    slot_of = np.zeros((count, count), np.int32)
    for number, row in enumerate(sources):
        for device, source in enumerate(row):
            source_of[device, number] = source
            slot_of[device, source] = number
    me = lax.axis_index("tp")
    return jnp.asarray(source_of)[me], jnp.asarray(slot_of)[me]


def ring_gather(block, order, early, source_of):
    count = len(order)
    place = {device: number for number, device in enumerate(order)}
    forward = [(order[i], order[(i + 1) % count]) for i in range(count)]
    backward = [(order[(i + 1) % count], order[i]) for i in range(count)]
    ahead = count // 2
    behind = count - 1 - ahead
    arrived = [block]
    moving_f = block
    moving_b = block
    for step in range(1, ahead + 1):
        moving_f = lax.ppermute(moving_f, "tp", forward)
        if step <= behind:
            moving_b = lax.ppermute(moving_b, "tp", backward)
        if step == 1:
            moving_f, moving_b, early = lax.optimization_barrier((moving_f, moving_b, early))
        arrived.append(moving_f)
        if step <= behind:
            arrived.append(moving_b)
    rows = block.shape[0]
    placed = jnp.zeros((count * rows, block.shape[1]), block.dtype)
    for number, piece in enumerate(arrived):
        placed = lax.dynamic_update_slice(placed, piece, (source_of[number] * rows, 0))
    return placed, early


def body(queries, latent_rows, doc_ids, key_weight, value_weight, *, order):
    block_rows = queries.shape[0]
    chunk_rows = latent_rows.shape[0]
    chunks = block_rows // chunk_rows
    cycle_size = lax.axis_size("ctx")
    cycle_index = lax.axis_index("ctx")
    heads_here = key_weight.shape[1] // NOPE_DIM
    width = latent_rows.shape[1]
    pad = (-(width + 1)) % LANES
    doc_column = jnp.concatenate(
        [doc_ids.astype(jnp.bfloat16)[:, None], jnp.zeros((chunk_rows, pad), jnp.bfloat16)],
        axis=1,
    )
    chunk = jnp.concatenate([latent_rows, doc_column], axis=1)
    source_of, slot_of = ring_tables(order)
    offsets = jnp.arange(block_rows, dtype=jnp.int32)
    positions = []
    for distance in range(cycle_size - 1, 0, -1):
        source = cycle_index - distance
        positions.append(jnp.where(source >= 0, source * block_rows + offsets, FAR))
    positions.append(cycle_index * block_rows + offsets)
    pos_tiles = jnp.concatenate(positions, axis=0).reshape(-1, BLOCK_K)
    pos_tables = (jnp.min(pos_tiles, axis=1), jnp.max(pos_tiles, axis=1))
    query_base = (cycle_index * block_rows).astype(jnp.int32).reshape(1)
    query_heads = jnp.transpose(queries, (1, 0, 2))
    early = (pos_tables, query_base, query_heads)
    gathered, early = ring_gather(chunk, order, early, source_of)
    pos_tables, query_base, query_heads = early
    latent_part = gathered[:, :KV_RANK]
    key_heads = jnp.dot(latent_part, key_weight, preferred_element_type=jnp.float32).astype(
        jnp.bfloat16
    )
    value_heads = jnp.dot(latent_part, value_weight, preferred_element_type=jnp.float32).astype(
        jnp.bfloat16
    )
    if heads_here != 1:
        raise ValueError(heads_here)
    pack = jnp.concatenate([key_heads, gathered[:, KV_RANK:], value_heads], axis=1)
    docs = gathered[:, width].astype(jnp.int32)
    query_docs = docs

    packs, docs_rows = [], []
    for distance in range(cycle_size - 1, 0, -1):
        route = [(i - distance, i) for i in range(cycle_size) if i - distance >= 0]
        moved = lax.ppermute(pack, "ctx", route)
        packs.append(moved)
        docs_rows.append(moved[:, NOPE_DIM + ROPE_DIM].astype(jnp.int32))
    packs.append(pack)
    docs_rows.append(docs)
    return flash(query_heads, packs, pos_tables, docs_rows, query_docs, query_base)


def ring_order(mesh):
    line = list(mesh.devices[(0,) * (mesh.devices.ndim - 1)].reshape(-1))
    try:
        where = {(d.coords[0], d.coords[2]): number for number, d in enumerate(line)}
        xs = sorted({key[0] for key in where})
        zs = sorted({key[1] for key in where})
        order = []
        for turn, x in enumerate(xs):
            for z in zs if turn % 2 == 0 else zs[::-1]:
                order.append(where[(x, z)])
    except (AttributeError, KeyError, IndexError, TypeError):
        return list(range(len(line)))
    if sorted(order) != list(range(len(line))):
        return list(range(len(line)))
    return order


def solution(mesh):
    placed = (
        P(("grp", "ctx"), "tp", None),
        P(("grp", "ctx", "tp"), None),
        P(("grp", "ctx", "tp")),
        P(None, "tp"),
        P(None, "tp"),
    )
    return jax.shard_map(
        functools.partial(body, order=ring_order(mesh)),
        mesh=mesh,
        in_specs=placed,
        out_specs=P(("grp", "ctx"), "tp"),
        check_vma=False,
    )
```

```python
import functools
import math

import jax
import jax.numpy as jnp
import numpy as np
from jax import lax
from jax.experimental import pallas as pl
from jax.experimental.pallas import tpu as pltpu
from jax.sharding import PartitionSpec as P

KV_RANK = 512
ROPE_DIM = 64
NOPE_DIM = 128
LANES = 128
BLOCK_Q = 512
BLOCK_K = 512
FAR = 1 << 30


def flash_kernel(
    qbase_ref, kminp_ref, kmaxp_ref, kmind_ref, kmaxd_ref,
    q_ref, *rest, sets, tiles, factor,
):
    set_refs = [rest[4 * n : 4 * n + 4] for n in range(sets)]
    o_ref = rest[4 * sets]
    qt = pl.program_id(1)
    bq = q_ref.shape[0]
    bk = BLOCK_K
    first_pos = qbase_ref[0] + qt * bq
    last_pos = first_pos + (bq - 1)
    own = (sets - 1) * tiles + qt
    first_doc = kmind_ref[own]
    last_doc = kmaxd_ref[own]
    q = q_ref[...]
    q_nope = q[:, :NOPE_DIM]
    q_rope = q[:, NOPE_DIM:]
    q_pos = first_pos + lax.broadcasted_iota(jnp.int32, (bq, 1), 0)
    q_doc = set_refs[-1][2][pl.ds(pl.multiple_of(qt * bq, bq), bq), :][:, ROPE_DIM : ROPE_DIM + 1].astype(jnp.float32)
    nt = (((1,), (1,)), ((), ()))

    m_sc, l_sc, acc_sc = rest[4 * sets + 1 :]
    m_sc[...] = jnp.full(m_sc.shape, -1e30, jnp.float32)
    l_sc[...] = jnp.zeros(l_sc.shape, jnp.float32)
    acc_sc[...] = jnp.zeros(acc_sc.shape, jnp.float32)

    def make_step(number, k_ref, v_ref, r_ref, kp_ref):
        def tile(masked, t):
            start = pl.multiple_of(t * bk, bk)
            keys = k_ref[pl.ds(start, bk), :]
            ropes = r_ref[pl.ds(start, bk), :]
            scores = lax.dot_general(q_nope, keys, nt, preferred_element_type=jnp.float32)
            scores = scores + lax.dot_general(
                q_rope, ropes[:, :ROPE_DIM], nt, preferred_element_type=jnp.float32
            )
            scores = scores * factor
            if masked:
                k_pos = kp_ref[:, pl.ds(start, bk)]
                k_doc = jnp.transpose(ropes.astype(jnp.float32))[ROPE_DIM : ROPE_DIM + 1, :]
                visible = (k_pos <= q_pos) & (k_doc == q_doc)
                scores = jnp.where(visible, scores, jnp.float32(-1e30))
            m_prev = m_sc[...]
            m_new = jnp.maximum(m_prev, jnp.max(scores, axis=1, keepdims=True))
            alpha = jnp.exp(m_prev - m_new)
            weights = jnp.exp(scores - m_new)
            l_sc[...] = alpha * l_sc[...] + jnp.sum(weights, axis=1, keepdims=True)
            acc_sc[...] = alpha * acc_sc[...] + jnp.dot(
                weights.astype(jnp.bfloat16),
                v_ref[pl.ds(start, bk), :],
                preferred_element_type=jnp.float32,
            )
            m_sc[...] = m_new

        def step(t, carry):
            at = number * tiles + t
            active = (
                (kminp_ref[at] <= last_pos)
                & (kmaxd_ref[at] >= first_doc)
                & (kmind_ref[at] <= last_doc)
            )
            full = (
                (kmaxp_ref[at] <= first_pos)
                & (kmind_ref[at] == last_doc)
                & (kmaxd_ref[at] == first_doc)
            )

            @pl.when(active & full)
            def _():
                tile(False, t)

            @pl.when(active & jnp.logical_not(full))
            def _():
                tile(True, t)

            return carry

        return step

    for number, refs in enumerate(set_refs):
        lax.fori_loop(0, tiles, make_step(number, *refs), 0)
    o_ref[...] = (acc_sc[...] / l_sc[...]).astype(o_ref.dtype)


def flash(query_heads, packs, positions, pos_tables, doc_ends, query_base):
    heads_here, rows, _ = query_heads.shape
    count = packs[0].shape[0]
    bq = min(BLOCK_Q, rows)
    bk = BLOCK_K
    q_tiles = rows // bq
    tiles = count // bk
    sets = len(packs)
    assert bq == bk and rows == count
    kminp, kmaxp = pos_tables
    kmind = jnp.concatenate([ends[0] for ends in doc_ends], axis=0)
    kmaxd = jnp.concatenate([ends[1] for ends in doc_ends], axis=0)

    in_specs = [pl.BlockSpec((None, bq, query_heads.shape[2]), lambda h, qt, *_: (h, qt, 0))]
    operands = [query_heads]
    for pack, pos in zip(packs, positions):
        in_specs += [
            pl.BlockSpec((count, LANES), lambda h, qt, *_: (0, h)),
            pl.BlockSpec((count, LANES), lambda h, qt, *_: (0, heads_here + h)),
            pl.BlockSpec((count, LANES), lambda h, qt, *_: (0, 2 * heads_here)),
            pl.BlockSpec((1, count), lambda h, qt, *_: (0, 0)),
        ]
        operands += [pack, pack, pack, pos]

    kernel = functools.partial(
        flash_kernel, sets=sets, tiles=tiles, factor=1.0 / math.sqrt(NOPE_DIM + ROPE_DIM)
    )
    grid_spec = pltpu.PrefetchScalarGridSpec(
        num_scalar_prefetch=5,
        grid=(heads_here, q_tiles),
        in_specs=in_specs,
        out_specs=pl.BlockSpec((bq, LANES), lambda h, qt, *_: (qt, h)),
        scratch_shapes=[
            pltpu.VMEM((bq, 1), jnp.float32),
            pltpu.VMEM((bq, 1), jnp.float32),
            pltpu.VMEM((bq, LANES), jnp.float32),
        ],
    )
    return pl.pallas_call(
        kernel,
        grid_spec=grid_spec,
        out_shape=jax.ShapeDtypeStruct((rows, heads_here * LANES), jnp.bfloat16),
        compiler_params=pltpu.CompilerParams(dimension_semantics=("arbitrary", "arbitrary")),
    )(query_base, kminp, kmaxp, kmind, kmaxd, *operands)


def ring_tables(order):
    count = len(order)
    place = {device: number for number, device in enumerate(order)}
    ahead = count // 2
    behind = count - 1 - ahead
    sources = [list(range(count))]
    for step in range(1, ahead + 1):
        sources.append([order[(place[d] - step) % count] for d in range(count)])
        if step <= behind:
            sources.append([order[(place[d] + step) % count] for d in range(count)])
    source_of = np.zeros((count, count), np.int32)
    slot_of = np.zeros((count, count), np.int32)
    for number, row in enumerate(sources):
        for device, source in enumerate(row):
            source_of[device, number] = source
            slot_of[device, source] = number
    me = lax.axis_index("tp")
    return jnp.asarray(source_of)[me], jnp.asarray(slot_of)[me]


def ring_gather(block, order, early, source_of):
    count = len(order)
    place = {device: number for number, device in enumerate(order)}
    forward = [(order[i], order[(i + 1) % count]) for i in range(count)]
    backward = [(order[(i + 1) % count], order[i]) for i in range(count)]
    ahead = count // 2
    behind = count - 1 - ahead
    arrived = [block]
    moving_f = block
    moving_b = block
    for step in range(1, ahead + 1):
        moving_f = lax.ppermute(moving_f, "tp", forward)
        if step <= behind:
            moving_b = lax.ppermute(moving_b, "tp", backward)
        if step == 1:
            moving_f, moving_b, early = lax.optimization_barrier((moving_f, moving_b, early))
        arrived.append(moving_f)
        if step <= behind:
            arrived.append(moving_b)
    rows = block.shape[0]
    placed = jnp.zeros((count * rows, block.shape[1]), block.dtype)
    for number, piece in enumerate(arrived):
        placed = lax.dynamic_update_slice(placed, piece, (source_of[number] * rows, 0))
    return placed, early


def body(queries, latent_rows, doc_ids, key_weight, value_weight, *, order):
    block_rows = queries.shape[0]
    chunk_rows = latent_rows.shape[0]
    chunks = block_rows // chunk_rows
    cycle_size = lax.axis_size("ctx")
    cycle_index = lax.axis_index("ctx")
    heads_here = key_weight.shape[1] // NOPE_DIM
    width = latent_rows.shape[1]
    pad = (-(width + 1)) % LANES
    doc_column = jnp.concatenate(
        [doc_ids.astype(jnp.bfloat16)[:, None], jnp.zeros((chunk_rows, pad), jnp.bfloat16)],
        axis=1,
    )
    chunk = jnp.concatenate([latent_rows, doc_column], axis=1)
    source_of, slot_of = ring_tables(order)
    offsets = jnp.arange(block_rows, dtype=jnp.int32)
    positions = []
    for distance in range(cycle_size - 1, 0, -1):
        source = cycle_index - distance
        positions.append(jnp.where(source >= 0, source * block_rows + offsets, FAR))
    positions.append(cycle_index * block_rows + offsets)
    pos_tiles = jnp.concatenate(positions, axis=0).reshape(-1, BLOCK_K)
    pos_tables = (jnp.min(pos_tiles, axis=1), jnp.max(pos_tiles, axis=1))
    query_base = (cycle_index * block_rows).astype(jnp.int32).reshape(1)
    query_heads = jnp.transpose(queries, (1, 0, 2))
    early = (tuple(pos.reshape(1, -1) for pos in positions), pos_tables, query_base, query_heads)
    gathered, early = ring_gather(chunk, order, early, source_of)
    positions, pos_tables, query_base, query_heads = early
    latent_part = gathered[:, :KV_RANK]
    key_heads = jnp.dot(latent_part, key_weight, preferred_element_type=jnp.float32).astype(
        jnp.bfloat16
    )
    value_heads = jnp.dot(latent_part, value_weight, preferred_element_type=jnp.float32).astype(
        jnp.bfloat16
    )
    pack = jnp.concatenate([key_heads, value_heads, gathered[:, KV_RANK:]], axis=1)
    doc_at = 2 * heads_here * NOPE_DIM + ROPE_DIM

    def ends_of(source):
        return (
            source[::BLOCK_K, doc_at].astype(jnp.int32),
            source[BLOCK_K - 1 :: BLOCK_K, doc_at].astype(jnp.int32),
        )

    packs, doc_ends = [], []
    for distance in range(cycle_size - 1, 0, -1):
        route = [(i - distance, i) for i in range(cycle_size) if i - distance >= 0]
        moved = lax.ppermute(pack, "ctx", route)
        packs.append(moved)
        doc_ends.append(ends_of(moved))
    packs.append(pack)
    doc_ends.append(ends_of(pack))
    return flash(query_heads, packs, positions, pos_tables, doc_ends, query_base)


def ring_order(mesh):
    line = list(mesh.devices[(0,) * (mesh.devices.ndim - 1)].reshape(-1))
    try:
        where = {(d.coords[0], d.coords[2]): number for number, d in enumerate(line)}
        xs = sorted({key[0] for key in where})
        zs = sorted({key[1] for key in where})
        order = []
        for turn, x in enumerate(xs):
            for z in zs if turn % 2 == 0 else zs[::-1]:
                order.append(where[(x, z)])
    except (AttributeError, KeyError, IndexError, TypeError):
        return list(range(len(line)))
    if sorted(order) != list(range(len(line))):
        return list(range(len(line)))
    return order


def solution(mesh):
    placed = (
        P(("grp", "ctx"), "tp", None),
        P(("grp", "ctx", "tp"), None),
        P(("grp", "ctx", "tp")),
        P(None, "tp"),
        P(None, "tp"),
    )
    return jax.shard_map(
        functools.partial(body, order=ring_order(mesh)),
        mesh=mesh,
        in_specs=placed,
        out_specs=P(("grp", "ctx"), "tp"),
        check_vma=False,
    )
```

```python
import functools
import math

import jax
import jax.numpy as jnp
import numpy as np
from jax import lax
from jax.experimental import pallas as pl
from jax.experimental.pallas import tpu as pltpu
from jax.sharding import PartitionSpec as P

KV_RANK = 512
ROPE_DIM = 64
NOPE_DIM = 128
LANES = 128
BLOCK_Q = 512
BLOCK_K = 512
FAR = 1 << 30


def flash_kernel(
    qbase_ref, kminp_ref, kmaxp_ref, kmind_ref, kmaxd_ref,
    q_ref, *rest, sets, tiles, factor,
):
    set_refs = [rest[3 * n : 3 * n + 3] for n in range(sets)]
    o_ref = rest[3 * sets]
    qt = pl.program_id(1)
    bq = q_ref.shape[0]
    bk = BLOCK_K
    first_pos = qbase_ref[0] + qt * bq
    last_pos = first_pos + (bq - 1)
    own = (sets - 1) * tiles + qt
    first_doc = kmind_ref[own]
    last_doc = kmaxd_ref[own]
    q = q_ref[...]
    q_nope = q[:, :NOPE_DIM]
    q_rope = q[:, NOPE_DIM:]
    q_pos = first_pos + lax.broadcasted_iota(jnp.int32, (bq, 1), 0)
    q_doc = set_refs[-1][2][pl.ds(pl.multiple_of(qt * bq, bq), bq), :][:, ROPE_DIM : ROPE_DIM + 1].astype(jnp.float32)
    nt = (((1,), (1,)), ((), ()))

    m_sc, l_sc, acc_sc = rest[3 * sets + 1 :]
    m_sc[...] = jnp.full(m_sc.shape, -1e30, jnp.float32)
    l_sc[...] = jnp.zeros(l_sc.shape, jnp.float32)
    acc_sc[...] = jnp.zeros(acc_sc.shape, jnp.float32)

    def make_step(number, k_ref, v_ref, r_ref):
        def tile(masked, t):
            start = pl.multiple_of(t * bk, bk)
            keys = k_ref[pl.ds(start, bk), :]
            ropes = r_ref[pl.ds(start, bk), :]
            scores = lax.dot_general(q_nope, keys, nt, preferred_element_type=jnp.float32)
            scores = scores + lax.dot_general(
                q_rope, ropes[:, :ROPE_DIM], nt, preferred_element_type=jnp.float32
            )
            scores = scores * factor
            if masked:
                k_pos = kminp_ref[number * tiles + t] + lax.broadcasted_iota(jnp.int32, (1, bk), 1)
                k_doc = jnp.transpose(ropes.astype(jnp.float32))[ROPE_DIM : ROPE_DIM + 1, :]
                visible = (k_pos <= q_pos) & (k_doc == q_doc)
                scores = jnp.where(visible, scores, jnp.float32(-1e30))
            m_prev = m_sc[...]
            m_new = jnp.maximum(m_prev, jnp.max(scores, axis=1, keepdims=True))
            alpha = jnp.exp(m_prev - m_new)
            weights = jnp.exp(scores - m_new)
            l_sc[...] = alpha * l_sc[...] + jnp.sum(weights, axis=1, keepdims=True)
            acc_sc[...] = alpha * acc_sc[...] + jnp.dot(
                weights.astype(jnp.bfloat16),
                v_ref[pl.ds(start, bk), :],
                preferred_element_type=jnp.float32,
            )
            m_sc[...] = m_new

        def step(t, carry):
            at = number * tiles + t
            active = (
                (kminp_ref[at] <= last_pos)
                & (kmaxd_ref[at] >= first_doc)
                & (kmind_ref[at] <= last_doc)
            )
            full = (
                (kmaxp_ref[at] <= first_pos)
                & (kmind_ref[at] == last_doc)
                & (kmaxd_ref[at] == first_doc)
            )

            @pl.when(active & full)
            def _():
                tile(False, t)

            @pl.when(active & jnp.logical_not(full))
            def _():
                tile(True, t)

            return carry

        return step

    for number, refs in enumerate(set_refs):
        lax.fori_loop(0, tiles, make_step(number, *refs), 0)
    o_ref[...] = (acc_sc[...] / l_sc[...]).astype(o_ref.dtype)


def flash(query_heads, packs, positions, pos_tables, doc_ends, query_base):
    heads_here, rows, _ = query_heads.shape
    count = packs[0].shape[0]
    bq = min(BLOCK_Q, rows)
    bk = BLOCK_K
    q_tiles = rows // bq
    tiles = count // bk
    sets = len(packs)
    assert bq == bk and rows == count
    kminp, kmaxp = pos_tables
    kmind = jnp.concatenate([ends[0] for ends in doc_ends], axis=0)
    kmaxd = jnp.concatenate([ends[1] for ends in doc_ends], axis=0)

    in_specs = [pl.BlockSpec((None, bq, query_heads.shape[2]), lambda h, qt, *_: (h, qt, 0))]
    operands = [query_heads]
    for pack in packs:
        in_specs += [
            pl.BlockSpec((count, LANES), lambda h, qt, *_: (0, h)),
            pl.BlockSpec((count, LANES), lambda h, qt, *_: (0, heads_here + h)),
            pl.BlockSpec((count, LANES), lambda h, qt, *_: (0, 2 * heads_here)),
        ]
        operands += [pack, pack, pack]

    kernel = functools.partial(
        flash_kernel, sets=sets, tiles=tiles, factor=1.0 / math.sqrt(NOPE_DIM + ROPE_DIM)
    )
    grid_spec = pltpu.PrefetchScalarGridSpec(
        num_scalar_prefetch=5,
        grid=(heads_here, q_tiles),
        in_specs=in_specs,
        out_specs=pl.BlockSpec((bq, LANES), lambda h, qt, *_: (qt, h)),
        scratch_shapes=[
            pltpu.VMEM((bq, 1), jnp.float32),
            pltpu.VMEM((bq, 1), jnp.float32),
            pltpu.VMEM((bq, LANES), jnp.float32),
        ],
    )
    return pl.pallas_call(
        kernel,
        grid_spec=grid_spec,
        out_shape=jax.ShapeDtypeStruct((rows, heads_here * LANES), jnp.bfloat16),
        compiler_params=pltpu.CompilerParams(dimension_semantics=("arbitrary", "arbitrary")),
    )(query_base, kminp, kmaxp, kmind, kmaxd, *operands)


def ring_tables(order):
    count = len(order)
    place = {device: number for number, device in enumerate(order)}
    ahead = count // 2
    behind = count - 1 - ahead
    sources = [list(range(count))]
    for step in range(1, ahead + 1):
        sources.append([order[(place[d] - step) % count] for d in range(count)])
        if step <= behind:
            sources.append([order[(place[d] + step) % count] for d in range(count)])
    source_of = np.zeros((count, count), np.int32)
    slot_of = np.zeros((count, count), np.int32)
    for number, row in enumerate(sources):
        for device, source in enumerate(row):
            source_of[device, number] = source
            slot_of[device, source] = number
    me = lax.axis_index("tp")
    return jnp.asarray(source_of)[me], jnp.asarray(slot_of)[me]


def ring_gather(block, order, early, source_of):
    count = len(order)
    place = {device: number for number, device in enumerate(order)}
    forward = [(order[i], order[(i + 1) % count]) for i in range(count)]
    backward = [(order[(i + 1) % count], order[i]) for i in range(count)]
    ahead = count // 2
    behind = count - 1 - ahead
    arrived = [block]
    moving_f = block
    moving_b = block
    for step in range(1, ahead + 1):
        moving_f = lax.ppermute(moving_f, "tp", forward)
        if step <= behind:
            moving_b = lax.ppermute(moving_b, "tp", backward)
        if step == 1:
            moving_f, moving_b, early = lax.optimization_barrier((moving_f, moving_b, early))
        arrived.append(moving_f)
        if step <= behind:
            arrived.append(moving_b)
    rows = block.shape[0]
    placed = jnp.zeros((count * rows, block.shape[1]), block.dtype)
    for number, piece in enumerate(arrived):
        placed = lax.dynamic_update_slice(placed, piece, (source_of[number] * rows, 0))
    return placed, early


def body(queries, latent_rows, doc_ids, key_weight, value_weight, *, order):
    block_rows = queries.shape[0]
    chunk_rows = latent_rows.shape[0]
    chunks = block_rows // chunk_rows
    cycle_size = lax.axis_size("ctx")
    cycle_index = lax.axis_index("ctx")
    heads_here = key_weight.shape[1] // NOPE_DIM
    width = latent_rows.shape[1]
    pad = (-(width + 1)) % LANES
    doc_column = jnp.concatenate(
        [doc_ids.astype(jnp.bfloat16)[:, None], jnp.zeros((chunk_rows, pad), jnp.bfloat16)],
        axis=1,
    )
    chunk = jnp.concatenate([latent_rows, doc_column], axis=1)
    source_of, slot_of = ring_tables(order)
    offsets = jnp.arange(block_rows, dtype=jnp.int32)
    positions = []
    for distance in range(cycle_size - 1, 0, -1):
        source = cycle_index - distance
        positions.append(jnp.where(source >= 0, source * block_rows + offsets, FAR))
    positions.append(cycle_index * block_rows + offsets)
    pos_tiles = jnp.concatenate(positions, axis=0).reshape(-1, BLOCK_K)
    pos_tables = (jnp.min(pos_tiles, axis=1), jnp.max(pos_tiles, axis=1))
    query_base = (cycle_index * block_rows).astype(jnp.int32).reshape(1)
    query_heads = jnp.transpose(queries, (1, 0, 2))
    early = (pos_tables, query_base, query_heads)
    gathered, early = ring_gather(chunk, order, early, source_of)
    pos_tables, query_base, query_heads = early
    latent_part = gathered[:, :KV_RANK]
    key_heads = jnp.dot(latent_part, key_weight, preferred_element_type=jnp.float32).astype(
        jnp.bfloat16
    )
    value_heads = jnp.dot(latent_part, value_weight, preferred_element_type=jnp.float32).astype(
        jnp.bfloat16
    )
    pack = jnp.concatenate([key_heads, value_heads, gathered[:, KV_RANK:]], axis=1)
    doc_at = 2 * heads_here * NOPE_DIM + ROPE_DIM

    def ends_of(source):
        return (
            source[::BLOCK_K, doc_at].astype(jnp.int32),
            source[BLOCK_K - 1 :: BLOCK_K, doc_at].astype(jnp.int32),
        )

    packs, doc_ends = [], []
    for distance in range(cycle_size - 1, 0, -1):
        route = [(i - distance, i) for i in range(cycle_size) if i - distance >= 0]
        moved = lax.ppermute(pack, "ctx", route)
        packs.append(moved)
        doc_ends.append(ends_of(moved))
    packs.append(pack)
    doc_ends.append(ends_of(pack))
    return flash(query_heads, packs, positions, pos_tables, doc_ends, query_base)


def ring_order(mesh):
    line = list(mesh.devices[(0,) * (mesh.devices.ndim - 1)].reshape(-1))
    try:
        where = {(d.coords[0], d.coords[2]): number for number, d in enumerate(line)}
        xs = sorted({key[0] for key in where})
        zs = sorted({key[1] for key in where})
        order = []
        for turn, x in enumerate(xs):
            for z in zs if turn % 2 == 0 else zs[::-1]:
                order.append(where[(x, z)])
    except (AttributeError, KeyError, IndexError, TypeError):
        return list(range(len(line)))
    if sorted(order) != list(range(len(line))):
        return list(range(len(line)))
    return order


def solution(mesh):
    placed = (
        P(("grp", "ctx"), "tp", None),
        P(("grp", "ctx", "tp"), None),
        P(("grp", "ctx", "tp")),
        P(None, "tp"),
        P(None, "tp"),
    )
    return jax.shard_map(
        functools.partial(body, order=ring_order(mesh)),
        mesh=mesh,
        in_specs=placed,
        out_specs=P(("grp", "ctx"), "tp"),
        check_vma=False,
    )
```

```python
import functools
import math

import jax
import jax.numpy as jnp
import numpy as np
from jax import lax
from jax.experimental import pallas as pl
from jax.experimental.pallas import tpu as pltpu
from jax.sharding import PartitionSpec as P

KV_RANK = 512
ROPE_DIM = 64
NOPE_DIM = 128
LANES = 128
BLOCK_Q = 512
BLOCK_K = 512
FAR = 1 << 30


def flash_kernel(
    qbase_ref, kminp_ref, kmaxp_ref, kmind_ref, kmaxd_ref,
    q_ref, *rest, sets, tiles, factor,
):
    set_refs = [rest[4 * n : 4 * n + 4] for n in range(sets)]
    o_ref = rest[4 * sets]
    qt = pl.program_id(1)
    bq = q_ref.shape[0]
    bk = BLOCK_K
    first_pos = qbase_ref[0] + qt * bq
    last_pos = first_pos + (bq - 1)
    own = (sets - 1) * tiles + qt
    first_doc = kmind_ref[own]
    last_doc = kmaxd_ref[own]
    q = q_ref[...]
    q_nope = q[:, :NOPE_DIM]
    q_rope = q[:, NOPE_DIM:]
    q_pos = first_pos + lax.broadcasted_iota(jnp.int32, (bq, 1), 0)
    q_doc = set_refs[-1][2][pl.ds(pl.multiple_of(qt * bq, bq), bq), :][:, ROPE_DIM : ROPE_DIM + 1].astype(jnp.float32)
    nt = (((1,), (1,)), ((), ()))

    m_sc, l_sc, acc_sc, kdoc_sc = rest[4 * sets + 1 :]

    @pl.when(qt == 0)
    def _():
        for number, refs in enumerate(set_refs):
            for t in range(tiles):
                block = refs[2][t * bk : (t + 1) * bk, :].astype(jnp.float32)
                kdoc_sc[number * 8 : number * 8 + 1, t * bk : (t + 1) * bk] = jnp.transpose(
                    block
                )[ROPE_DIM : ROPE_DIM + 1, :]

    m_sc[...] = jnp.full(m_sc.shape, -1e30, jnp.float32)
    l_sc[...] = jnp.zeros(l_sc.shape, jnp.float32)
    acc_sc[...] = jnp.zeros(acc_sc.shape, jnp.float32)

    def make_step(number, k_ref, v_ref, r_ref, kp_ref):
        def tile(masked, t):
            start = pl.multiple_of(t * bk, bk)
            keys = k_ref[pl.ds(start, bk), :]
            ropes = r_ref[pl.ds(start, bk), :]
            scores = lax.dot_general(q_nope, keys, nt, preferred_element_type=jnp.float32)
            scores = scores + lax.dot_general(
                q_rope, ropes[:, :ROPE_DIM], nt, preferred_element_type=jnp.float32
            )
            scores = scores * factor
            if masked:
                k_pos = kp_ref[:, pl.ds(start, bk)]
                k_doc = kdoc_sc[pl.ds(number * 8, 1), pl.ds(start, bk)]
                visible = (k_pos <= q_pos) & (k_doc == q_doc)
                scores = jnp.where(visible, scores, jnp.float32(-1e30))
            m_prev = m_sc[...]
            m_new = jnp.maximum(m_prev, jnp.max(scores, axis=1, keepdims=True))
            alpha = jnp.exp(m_prev - m_new)
            weights = jnp.exp(scores - m_new)
            l_sc[...] = alpha * l_sc[...] + jnp.sum(weights, axis=1, keepdims=True)
            acc_sc[...] = alpha * acc_sc[...] + jnp.dot(
                weights.astype(jnp.bfloat16),
                v_ref[pl.ds(start, bk), :],
                preferred_element_type=jnp.float32,
            )
            m_sc[...] = m_new

        def step(t, carry):
            at = number * tiles + t
            active = (
                (kminp_ref[at] <= last_pos)
                & (kmaxd_ref[at] >= first_doc)
                & (kmind_ref[at] <= last_doc)
            )
            full = (
                (kmaxp_ref[at] <= first_pos)
                & (kmind_ref[at] == last_doc)
                & (kmaxd_ref[at] == first_doc)
            )

            @pl.when(active & full)
            def _():
                tile(False, t)

            @pl.when(active & jnp.logical_not(full))
            def _():
                tile(True, t)

            return carry

        return step

    for number, refs in enumerate(set_refs):
        lax.fori_loop(0, tiles, make_step(number, *refs), 0)
    o_ref[...] = (acc_sc[...] / l_sc[...]).astype(o_ref.dtype)


def flash(query_heads, packs, positions, pos_tables, doc_ends, query_base):
    heads_here, rows, _ = query_heads.shape
    count = packs[0].shape[0]
    bq = min(BLOCK_Q, rows)
    bk = BLOCK_K
    q_tiles = rows // bq
    tiles = count // bk
    sets = len(packs)
    assert bq == bk and rows == count
    kminp, kmaxp = pos_tables
    kmind = jnp.concatenate([ends[0] for ends in doc_ends], axis=0)
    kmaxd = jnp.concatenate([ends[1] for ends in doc_ends], axis=0)

    in_specs = [pl.BlockSpec((None, bq, query_heads.shape[2]), lambda h, qt, *_: (h, qt, 0))]
    operands = [query_heads]
    for pack, pos in zip(packs, positions):
        in_specs += [
            pl.BlockSpec((count, LANES), lambda h, qt, *_: (0, h)),
            pl.BlockSpec((count, LANES), lambda h, qt, *_: (0, heads_here + h)),
            pl.BlockSpec((count, LANES), lambda h, qt, *_: (0, 2 * heads_here)),
            pl.BlockSpec((1, count), lambda h, qt, *_: (0, 0)),
        ]
        operands += [pack, pack, pack, pos]

    kernel = functools.partial(
        flash_kernel, sets=sets, tiles=tiles, factor=1.0 / math.sqrt(NOPE_DIM + ROPE_DIM)
    )
    grid_spec = pltpu.PrefetchScalarGridSpec(
        num_scalar_prefetch=5,
        grid=(heads_here, q_tiles),
        in_specs=in_specs,
        out_specs=pl.BlockSpec((bq, LANES), lambda h, qt, *_: (qt, h)),
        scratch_shapes=[
            pltpu.VMEM((bq, 1), jnp.float32),
            pltpu.VMEM((bq, 1), jnp.float32),
            pltpu.VMEM((bq, LANES), jnp.float32),
            pltpu.VMEM((8 * sets, count), jnp.float32),
        ],
    )
    return pl.pallas_call(
        kernel,
        grid_spec=grid_spec,
        out_shape=jax.ShapeDtypeStruct((rows, heads_here * LANES), jnp.bfloat16),
        compiler_params=pltpu.CompilerParams(dimension_semantics=("arbitrary", "arbitrary")),
    )(query_base, kminp, kmaxp, kmind, kmaxd, *operands)


def ring_tables(order):
    count = len(order)
    place = {device: number for number, device in enumerate(order)}
    ahead = count // 2
    behind = count - 1 - ahead
    sources = [list(range(count))]
    for step in range(1, ahead + 1):
        sources.append([order[(place[d] - step) % count] for d in range(count)])
        if step <= behind:
            sources.append([order[(place[d] + step) % count] for d in range(count)])
    source_of = np.zeros((count, count), np.int32)
    slot_of = np.zeros((count, count), np.int32)
    for number, row in enumerate(sources):
        for device, source in enumerate(row):
            source_of[device, number] = source
            slot_of[device, source] = number
    me = lax.axis_index("tp")
    return jnp.asarray(source_of)[me], jnp.asarray(slot_of)[me]


def ring_gather(block, order, early, source_of):
    count = len(order)
    place = {device: number for number, device in enumerate(order)}
    forward = [(order[i], order[(i + 1) % count]) for i in range(count)]
    backward = [(order[(i + 1) % count], order[i]) for i in range(count)]
    ahead = count // 2
    behind = count - 1 - ahead
    arrived = [block]
    moving_f = block
    moving_b = block
    for step in range(1, ahead + 1):
        moving_f = lax.ppermute(moving_f, "tp", forward)
        if step <= behind:
            moving_b = lax.ppermute(moving_b, "tp", backward)
        if step == 1:
            moving_f, moving_b, early = lax.optimization_barrier((moving_f, moving_b, early))
        arrived.append(moving_f)
        if step <= behind:
            arrived.append(moving_b)
    rows = block.shape[0]
    placed = jnp.zeros((count * rows, block.shape[1]), block.dtype)
    for number, piece in enumerate(arrived):
        placed = lax.dynamic_update_slice(placed, piece, (source_of[number] * rows, 0))
    return placed, early


def body(queries, latent_rows, doc_ids, key_weight, value_weight, *, order):
    block_rows = queries.shape[0]
    chunk_rows = latent_rows.shape[0]
    chunks = block_rows // chunk_rows
    cycle_size = lax.axis_size("ctx")
    cycle_index = lax.axis_index("ctx")
    heads_here = key_weight.shape[1] // NOPE_DIM
    width = latent_rows.shape[1]
    pad = (-(width + 1)) % LANES
    doc_column = jnp.concatenate(
        [doc_ids.astype(jnp.bfloat16)[:, None], jnp.zeros((chunk_rows, pad), jnp.bfloat16)],
        axis=1,
    )
    chunk = jnp.concatenate([latent_rows, doc_column], axis=1)
    source_of, slot_of = ring_tables(order)
    offsets = jnp.arange(block_rows, dtype=jnp.int32)
    positions = []
    for distance in range(cycle_size - 1, 0, -1):
        source = cycle_index - distance
        positions.append(jnp.where(source >= 0, source * block_rows + offsets, FAR))
    positions.append(cycle_index * block_rows + offsets)
    pos_tiles = jnp.concatenate(positions, axis=0).reshape(-1, BLOCK_K)
    pos_tables = (jnp.min(pos_tiles, axis=1), jnp.max(pos_tiles, axis=1))
    query_base = (cycle_index * block_rows).astype(jnp.int32).reshape(1)
    query_heads = jnp.transpose(queries, (1, 0, 2))
    early = (tuple(pos.reshape(1, -1) for pos in positions), pos_tables, query_base, query_heads)
    gathered, early = ring_gather(chunk, order, early, source_of)
    positions, pos_tables, query_base, query_heads = early
    latent_part = gathered[:, :KV_RANK]
    key_heads = jnp.dot(latent_part, key_weight, preferred_element_type=jnp.float32).astype(
        jnp.bfloat16
    )
    value_heads = jnp.dot(latent_part, value_weight, preferred_element_type=jnp.float32).astype(
        jnp.bfloat16
    )
    pack = jnp.concatenate([key_heads, value_heads, gathered[:, KV_RANK:]], axis=1)
    doc_at = 2 * heads_here * NOPE_DIM + ROPE_DIM

    def ends_of(source):
        return (
            source[::BLOCK_K, doc_at].astype(jnp.int32),
            source[BLOCK_K - 1 :: BLOCK_K, doc_at].astype(jnp.int32),
        )

    packs, doc_ends = [], []
    for distance in range(cycle_size - 1, 0, -1):
        route = [(i - distance, i) for i in range(cycle_size) if i - distance >= 0]
        moved = lax.ppermute(pack, "ctx", route)
        packs.append(moved)
        doc_ends.append(ends_of(moved))
    packs.append(pack)
    doc_ends.append(ends_of(pack))
    return flash(query_heads, packs, positions, pos_tables, doc_ends, query_base)


def ring_order(mesh):
    line = list(mesh.devices[(0,) * (mesh.devices.ndim - 1)].reshape(-1))
    try:
        where = {(d.coords[0], d.coords[2]): number for number, d in enumerate(line)}
        xs = sorted({key[0] for key in where})
        zs = sorted({key[1] for key in where})
        order = []
        for turn, x in enumerate(xs):
            for z in zs if turn % 2 == 0 else zs[::-1]:
                order.append(where[(x, z)])
    except (AttributeError, KeyError, IndexError, TypeError):
        return list(range(len(line)))
    if sorted(order) != list(range(len(line))):
        return list(range(len(line)))
    return order


def solution(mesh):
    placed = (
        P(("grp", "ctx"), "tp", None),
        P(("grp", "ctx", "tp"), None),
        P(("grp", "ctx", "tp")),
        P(None, "tp"),
        P(None, "tp"),
    )
    return jax.shard_map(
        functools.partial(body, order=ring_order(mesh)),
        mesh=mesh,
        in_specs=placed,
        out_specs=P(("grp", "ctx"), "tp"),
        check_vma=False,
    )
```

```python
import functools
import math

import jax
import jax.numpy as jnp
import numpy as np
from jax import lax
from jax.experimental import pallas as pl
from jax.experimental.pallas import tpu as pltpu
from jax.sharding import PartitionSpec as P

KV_RANK = 512
ROPE_DIM = 64
NOPE_DIM = 128
LANES = 128
BLOCK_Q = 512
BLOCK_K = 512
FAR = 1 << 30


def flash_kernel(
    qbase_ref, kminp_ref, kmaxp_ref, kmind_ref, kmaxd_ref,
    q_ref, *rest, sets, tiles, factor,
):
    set_refs = [rest[4 * n : 4 * n + 4] for n in range(sets)]
    o_ref = rest[4 * sets]
    qt = pl.program_id(1)
    bq = q_ref.shape[0]
    bk = BLOCK_K
    first_pos = qbase_ref[0] + qt * bq
    last_pos = first_pos + (bq - 1)
    own = (sets - 1) * tiles + qt
    first_doc = kmind_ref[own]
    last_doc = kmaxd_ref[own]
    q = q_ref[...]
    q_nope = q[:, :NOPE_DIM]
    q_rope = q[:, NOPE_DIM:]
    q_pos = first_pos + lax.broadcasted_iota(jnp.int32, (bq, 1), 0)
    q_doc = set_refs[-1][2][pl.ds(pl.multiple_of(qt * bq, bq), bq), :][:, ROPE_DIM : ROPE_DIM + 1].astype(jnp.float32)
    nt = (((1,), (1,)), ((), ()))

    m_sc, l_sc, acc_sc = rest[4 * sets + 1 :]
    m_sc[...] = jnp.full(m_sc.shape, -1e30, jnp.float32)
    l_sc[...] = jnp.zeros(l_sc.shape, jnp.float32)
    acc_sc[...] = jnp.zeros(acc_sc.shape, jnp.float32)

    def make_step(number, k_ref, v_ref, r_ref, kp_ref):
        def tile(masked, t):
            start = pl.multiple_of(t * bk, bk)
            keys = k_ref[pl.ds(start, bk), :]
            ropes = r_ref[pl.ds(start, bk), :]
            scores = lax.dot_general(q_nope, keys, nt, preferred_element_type=jnp.float32)
            scores = scores + lax.dot_general(
                q_rope, ropes[:, :ROPE_DIM], nt, preferred_element_type=jnp.float32
            )
            scores = scores * factor
            if masked:
                k_pos = kp_ref[:, pl.ds(start, bk)]
                k_doc = jnp.transpose(ropes)[ROPE_DIM : ROPE_DIM + 1, :].astype(jnp.float32)
                visible = (k_pos <= q_pos) & (k_doc == q_doc)
                scores = jnp.where(visible, scores, jnp.float32(-1e30))
            m_prev = m_sc[...]
            m_new = jnp.maximum(m_prev, jnp.max(scores, axis=1, keepdims=True))
            alpha = jnp.exp(m_prev - m_new)
            weights = jnp.exp(scores - m_new)
            l_sc[...] = alpha * l_sc[...] + jnp.sum(weights, axis=1, keepdims=True)
            acc_sc[...] = alpha * acc_sc[...] + jnp.dot(
                weights.astype(jnp.bfloat16),
                v_ref[pl.ds(start, bk), :],
                preferred_element_type=jnp.float32,
            )
            m_sc[...] = m_new

        def step(t, carry):
            at = number * tiles + t
            active = (
                (kminp_ref[at] <= last_pos)
                & (kmaxd_ref[at] >= first_doc)
                & (kmind_ref[at] <= last_doc)
            )
            full = (
                (kmaxp_ref[at] <= first_pos)
                & (kmind_ref[at] == last_doc)
                & (kmaxd_ref[at] == first_doc)
            )

            @pl.when(active & full)
            def _():
                tile(False, t)

            @pl.when(active & jnp.logical_not(full))
            def _():
                tile(True, t)

            return carry

        return step

    for number, refs in enumerate(set_refs):
        lax.fori_loop(0, tiles, make_step(number, *refs), 0)
    o_ref[...] = (acc_sc[...] / l_sc[...]).astype(o_ref.dtype)


def flash(query_heads, packs, positions, pos_tables, doc_ends, query_base):
    heads_here, rows, _ = query_heads.shape
    count = packs[0].shape[0]
    bq = min(BLOCK_Q, rows)
    bk = BLOCK_K
    q_tiles = rows // bq
    tiles = count // bk
    sets = len(packs)
    assert bq == bk and rows == count
    kminp, kmaxp = pos_tables
    kmind = jnp.concatenate([ends[0] for ends in doc_ends], axis=0)
    kmaxd = jnp.concatenate([ends[1] for ends in doc_ends], axis=0)

    in_specs = [pl.BlockSpec((None, bq, query_heads.shape[2]), lambda h, qt, *_: (h, qt, 0))]
    operands = [query_heads]
    for pack, pos in zip(packs, positions):
        in_specs += [
            pl.BlockSpec((count, LANES), lambda h, qt, *_: (0, h)),
            pl.BlockSpec((count, LANES), lambda h, qt, *_: (0, heads_here + h)),
            pl.BlockSpec((count, LANES), lambda h, qt, *_: (0, 2 * heads_here)),
            pl.BlockSpec((1, count), lambda h, qt, *_: (0, 0)),
        ]
        operands += [pack, pack, pack, pos]

    kernel = functools.partial(
        flash_kernel, sets=sets, tiles=tiles, factor=1.0 / math.sqrt(NOPE_DIM + ROPE_DIM)
    )
    grid_spec = pltpu.PrefetchScalarGridSpec(
        num_scalar_prefetch=5,
        grid=(heads_here, q_tiles),
        in_specs=in_specs,
        out_specs=pl.BlockSpec((bq, LANES), lambda h, qt, *_: (qt, h)),
        scratch_shapes=[
            pltpu.VMEM((bq, 1), jnp.float32),
            pltpu.VMEM((bq, 1), jnp.float32),
            pltpu.VMEM((bq, LANES), jnp.float32),
        ],
    )
    return pl.pallas_call(
        kernel,
        grid_spec=grid_spec,
        out_shape=jax.ShapeDtypeStruct((rows, heads_here * LANES), jnp.bfloat16),
        compiler_params=pltpu.CompilerParams(dimension_semantics=("arbitrary", "arbitrary")),
    )(query_base, kminp, kmaxp, kmind, kmaxd, *operands)


def ring_tables(order):
    count = len(order)
    place = {device: number for number, device in enumerate(order)}
    ahead = count // 2
    behind = count - 1 - ahead
    sources = [list(range(count))]
    for step in range(1, ahead + 1):
        sources.append([order[(place[d] - step) % count] for d in range(count)])
        if step <= behind:
            sources.append([order[(place[d] + step) % count] for d in range(count)])
    source_of = np.zeros((count, count), np.int32)
    slot_of = np.zeros((count, count), np.int32)
    for number, row in enumerate(sources):
        for device, source in enumerate(row):
            source_of[device, number] = source
            slot_of[device, source] = number
    me = lax.axis_index("tp")
    return jnp.asarray(source_of)[me], jnp.asarray(slot_of)[me]


def ring_gather(block, order, early, source_of):
    count = len(order)
    place = {device: number for number, device in enumerate(order)}
    forward = [(order[i], order[(i + 1) % count]) for i in range(count)]
    backward = [(order[(i + 1) % count], order[i]) for i in range(count)]
    ahead = count // 2
    behind = count - 1 - ahead
    arrived = [block]
    moving_f = block
    moving_b = block
    for step in range(1, ahead + 1):
        moving_f = lax.ppermute(moving_f, "tp", forward)
        if step <= behind:
            moving_b = lax.ppermute(moving_b, "tp", backward)
        if step == 1:
            moving_f, moving_b, early = lax.optimization_barrier((moving_f, moving_b, early))
        arrived.append(moving_f)
        if step <= behind:
            arrived.append(moving_b)
    rows = block.shape[0]
    placed = jnp.zeros((count * rows, block.shape[1]), block.dtype)
    for number, piece in enumerate(arrived):
        placed = lax.dynamic_update_slice(placed, piece, (source_of[number] * rows, 0))
    return placed, early


def body(queries, latent_rows, doc_ids, key_weight, value_weight, *, order):
    block_rows = queries.shape[0]
    chunk_rows = latent_rows.shape[0]
    chunks = block_rows // chunk_rows
    cycle_size = lax.axis_size("ctx")
    cycle_index = lax.axis_index("ctx")
    heads_here = key_weight.shape[1] // NOPE_DIM
    width = latent_rows.shape[1]
    pad = (-(width + 1)) % LANES
    doc_column = jnp.concatenate(
        [doc_ids.astype(jnp.bfloat16)[:, None], jnp.zeros((chunk_rows, pad), jnp.bfloat16)],
        axis=1,
    )
    chunk = jnp.concatenate([latent_rows, doc_column], axis=1)
    source_of, slot_of = ring_tables(order)
    offsets = jnp.arange(block_rows, dtype=jnp.int32)
    positions = []
    for distance in range(cycle_size - 1, 0, -1):
        source = cycle_index - distance
        positions.append(jnp.where(source >= 0, source * block_rows + offsets, FAR))
    positions.append(cycle_index * block_rows + offsets)
    pos_tiles = jnp.concatenate(positions, axis=0).reshape(-1, BLOCK_K)
    pos_tables = (jnp.min(pos_tiles, axis=1), jnp.max(pos_tiles, axis=1))
    query_base = (cycle_index * block_rows).astype(jnp.int32).reshape(1)
    query_heads = jnp.transpose(queries, (1, 0, 2))
    early = (tuple(pos.reshape(1, -1) for pos in positions), pos_tables, query_base, query_heads)
    gathered, early = ring_gather(chunk, order, early, source_of)
    positions, pos_tables, query_base, query_heads = early
    latent_part = gathered[:, :KV_RANK]
    key_heads = jnp.dot(latent_part, key_weight, preferred_element_type=jnp.float32).astype(
        jnp.bfloat16
    )
    value_heads = jnp.dot(latent_part, value_weight, preferred_element_type=jnp.float32).astype(
        jnp.bfloat16
    )
    pack = jnp.concatenate([key_heads, value_heads, gathered[:, KV_RANK:]], axis=1)
    doc_at = 2 * heads_here * NOPE_DIM + ROPE_DIM

    def ends_of(source):
        return (
            source[::BLOCK_K, doc_at].astype(jnp.int32),
            source[BLOCK_K - 1 :: BLOCK_K, doc_at].astype(jnp.int32),
        )

    packs, doc_ends = [], []
    for distance in range(cycle_size - 1, 0, -1):
        route = [(i - distance, i) for i in range(cycle_size) if i - distance >= 0]
        moved = lax.ppermute(pack, "ctx", route)
        packs.append(moved)
        doc_ends.append(ends_of(moved))
    packs.append(pack)
    doc_ends.append(ends_of(pack))
    return flash(query_heads, packs, positions, pos_tables, doc_ends, query_base)


def ring_order(mesh):
    line = list(mesh.devices[(0,) * (mesh.devices.ndim - 1)].reshape(-1))
    try:
        where = {(d.coords[0], d.coords[2]): number for number, d in enumerate(line)}
        xs = sorted({key[0] for key in where})
        zs = sorted({key[1] for key in where})
        order = []
        for turn, x in enumerate(xs):
            for z in zs if turn % 2 == 0 else zs[::-1]:
                order.append(where[(x, z)])
    except (AttributeError, KeyError, IndexError, TypeError):
        return list(range(len(line)))
    if sorted(order) != list(range(len(line))):
        return list(range(len(line)))
    return order


def solution(mesh):
    placed = (
        P(("grp", "ctx"), "tp", None),
        P(("grp", "ctx", "tp"), None),
        P(("grp", "ctx", "tp")),
        P(None, "tp"),
        P(None, "tp"),
    )
    return jax.shard_map(
        functools.partial(body, order=ring_order(mesh)),
        mesh=mesh,
        in_specs=placed,
        out_specs=P(("grp", "ctx"), "tp"),
        check_vma=False,
    )
```

```python
import functools
import math

import jax
import jax.numpy as jnp
import numpy as np
from jax import lax
from jax.experimental import pallas as pl
from jax.experimental.pallas import tpu as pltpu
from jax.sharding import PartitionSpec as P

KV_RANK = 512
ROPE_DIM = 64
NOPE_DIM = 128
LANES = 128
BLOCK_Q = 512
BLOCK_K = 512
FAR = 1 << 30


def flash_kernel(
    qbase_ref, kminp_ref, kmaxp_ref, kmind_ref, kmaxd_ref,
    q_ref, *rest, sets, tiles, factor,
):
    set_refs = [rest[4 * n : 4 * n + 4] for n in range(sets)]
    o_ref = rest[4 * sets]
    qt = pl.program_id(1)
    bq = q_ref.shape[0]
    bk = BLOCK_K
    first_pos = qbase_ref[0] + qt * bq
    last_pos = first_pos + (bq - 1)
    own = (sets - 1) * tiles + qt
    first_doc = kmind_ref[own]
    last_doc = kmaxd_ref[own]
    q = q_ref[...]
    q_nope = q[:, :NOPE_DIM]
    q_rope = q[:, NOPE_DIM:]
    q_pos = first_pos + lax.broadcasted_iota(jnp.int32, (bq, 1), 0)
    q_doc = set_refs[-1][2][pl.ds(pl.multiple_of(qt * bq, bq), bq), :][:, ROPE_DIM : ROPE_DIM + 1].astype(jnp.float32)
    nt = (((1,), (1,)), ((), ()))

    m_sc, l_sc, acc_sc = rest[4 * sets + 1 :]
    m_sc[...] = jnp.full(m_sc.shape, -1e30, jnp.float32)
    l_sc[...] = jnp.zeros(l_sc.shape, jnp.float32)
    acc_sc[...] = jnp.zeros(acc_sc.shape, jnp.float32)

    def make_step(number, k_ref, v_ref, r_ref, kp_ref):
        def tile(masked, t):
            start = pl.multiple_of(t * bk, bk)
            keys = k_ref[pl.ds(start, bk), :]
            ropes = r_ref[pl.ds(start, bk), :]
            scores = lax.dot_general(q_nope, keys, nt, preferred_element_type=jnp.float32)
            scores = scores + lax.dot_general(
                q_rope, ropes[:, :ROPE_DIM], nt, preferred_element_type=jnp.float32
            )
            scores = scores * factor
            if masked:
                k_pos = kp_ref[:, pl.ds(start, bk)]
                k_doc = jnp.transpose(ropes.astype(jnp.float32))[ROPE_DIM : ROPE_DIM + 1, :]
                visible = (k_pos <= q_pos) & (k_doc == q_doc)
                scores = jnp.where(visible, scores, jnp.float32(-1e30))
            m_prev = m_sc[...]
            m_new = jnp.maximum(m_prev, jnp.max(scores, axis=1, keepdims=True))
            alpha = jnp.exp(m_prev - m_new)
            weights = jnp.exp(scores - m_new)
            l_sc[...] = alpha * l_sc[...] + jnp.sum(weights, axis=1, keepdims=True)
            acc_sc[...] = alpha * acc_sc[...] + jnp.dot(
                weights.astype(jnp.bfloat16),
                v_ref[pl.ds(start, bk), :],
                preferred_element_type=jnp.float32,
            )
            m_sc[...] = m_new

        def step(t, carry):
            at = number * tiles + t
            active = (
                (kminp_ref[at] <= last_pos)
                & (kmaxd_ref[at] >= first_doc)
                & (kmind_ref[at] <= last_doc)
            )
            full = (
                (kmaxp_ref[at] <= first_pos)
                & (kmind_ref[at] == last_doc)
                & (kmaxd_ref[at] == first_doc)
            )

            @pl.when(active & full)
            def _():
                tile(False, t)

            @pl.when(active & jnp.logical_not(full))
            def _():
                tile(True, t)

            return carry

        return step

    for number, refs in enumerate(set_refs):
        lax.fori_loop(0, tiles, make_step(number, *refs), 0)
    o_ref[...] = (acc_sc[...] / l_sc[...]).astype(o_ref.dtype)


def flash(query_heads, packs, positions, pos_tables, doc_ends, query_base):
    heads_here, rows, _ = query_heads.shape
    count = packs[0].shape[0]
    bq = min(BLOCK_Q, rows)
    bk = BLOCK_K
    q_tiles = rows // bq
    tiles = count // bk
    sets = len(packs)
    assert bq == bk and rows == count
    kminp, kmaxp = pos_tables
    kmind = jnp.concatenate([ends[0] for ends in doc_ends], axis=0)
    kmaxd = jnp.concatenate([ends[1] for ends in doc_ends], axis=0)

    in_specs = [pl.BlockSpec((None, bq, query_heads.shape[2]), lambda h, qt, *_: (h, qt, 0))]
    operands = [query_heads]
    for pack, pos in zip(packs, positions):
        in_specs += [
            pl.BlockSpec((count, LANES), lambda h, qt, *_: (0, h)),
            pl.BlockSpec((count, LANES), lambda h, qt, *_: (0, heads_here + h)),
            pl.BlockSpec((count, LANES), lambda h, qt, *_: (0, 2 * heads_here)),
            pl.BlockSpec((1, count), lambda h, qt, *_: (0, 0)),
        ]
        operands += [pack, pack, pack, pos]

    kernel = functools.partial(
        flash_kernel, sets=sets, tiles=tiles, factor=1.0 / math.sqrt(NOPE_DIM + ROPE_DIM)
    )
    grid_spec = pltpu.PrefetchScalarGridSpec(
        num_scalar_prefetch=5,
        grid=(heads_here, q_tiles),
        in_specs=in_specs,
        out_specs=pl.BlockSpec((bq, LANES), lambda h, qt, *_: (qt, h)),
        scratch_shapes=[
            pltpu.VMEM((bq, 1), jnp.float32),
            pltpu.VMEM((bq, 1), jnp.float32),
            pltpu.VMEM((bq, LANES), jnp.float32),
        ],
    )
    return pl.pallas_call(
        kernel,
        grid_spec=grid_spec,
        out_shape=jax.ShapeDtypeStruct((rows, heads_here * LANES), jnp.bfloat16),
        compiler_params=pltpu.CompilerParams(dimension_semantics=("arbitrary", "arbitrary")),
    )(query_base, kminp, kmaxp, kmind, kmaxd, *operands)


def ring_tables(order):
    count = len(order)
    place = {device: number for number, device in enumerate(order)}
    ahead = count // 2
    behind = count - 1 - ahead
    sources = [list(range(count))]
    for step in range(1, ahead + 1):
        sources.append([order[(place[d] - step) % count] for d in range(count)])
        if step <= behind:
            sources.append([order[(place[d] + step) % count] for d in range(count)])
    source_of = np.zeros((count, count), np.int32)
    slot_of = np.zeros((count, count), np.int32)
    for number, row in enumerate(sources):
        for device, source in enumerate(row):
            source_of[device, number] = source
            slot_of[device, source] = number
    me = lax.axis_index("tp")
    return jnp.asarray(source_of)[me], jnp.asarray(slot_of)[me]


def ring_gather(block, order, early, source_of):
    count = len(order)
    place = {device: number for number, device in enumerate(order)}
    forward = [(order[i], order[(i + 1) % count]) for i in range(count)]
    backward = [(order[(i + 1) % count], order[i]) for i in range(count)]
    ahead = count // 2
    behind = count - 1 - ahead
    arrived = [block]
    moving_f = block
    moving_b = block
    for step in range(1, ahead + 1):
        moving_f = lax.ppermute(moving_f, "tp", forward)
        if step <= behind:
            moving_b = lax.ppermute(moving_b, "tp", backward)
        if step == 1:
            moving_f, moving_b, early = lax.optimization_barrier((moving_f, moving_b, early))
        arrived.append(moving_f)
        if step <= behind:
            arrived.append(moving_b)
    rows = block.shape[0]
    placed = jnp.zeros((count * rows, block.shape[1]), block.dtype)
    for number, piece in enumerate(arrived):
        placed = lax.dynamic_update_slice(placed, piece, (source_of[number] * rows, 0))
    return placed, early


def body(queries, latent_rows, doc_ids, key_weight, value_weight, *, order):
    block_rows = queries.shape[0]
    chunk_rows = latent_rows.shape[0]
    chunks = block_rows // chunk_rows
    cycle_size = lax.axis_size("ctx")
    cycle_index = lax.axis_index("ctx")
    heads_here = key_weight.shape[1] // NOPE_DIM
    width = latent_rows.shape[1]
    pad = (-(width + 1)) % LANES
    lane = lax.broadcasted_iota(jnp.int32, (chunk_rows, width + 1 + pad), 1)
    widened = jnp.pad(latent_rows, ((0, 0), (0, 1 + pad)))
    chunk = jnp.where(lane == width, doc_ids.astype(jnp.bfloat16)[:, None], widened)
    source_of, slot_of = ring_tables(order)
    offsets = jnp.arange(block_rows, dtype=jnp.int32)
    positions = []
    for distance in range(cycle_size - 1, 0, -1):
        source = cycle_index - distance
        positions.append(jnp.where(source >= 0, source * block_rows + offsets, FAR))
    positions.append(cycle_index * block_rows + offsets)
    pos_tiles = jnp.concatenate(positions, axis=0).reshape(-1, BLOCK_K)
    pos_tables = (jnp.min(pos_tiles, axis=1), jnp.max(pos_tiles, axis=1))
    query_base = (cycle_index * block_rows).astype(jnp.int32).reshape(1)
    query_heads = jnp.transpose(queries, (1, 0, 2))
    early = (tuple(pos.reshape(1, -1) for pos in positions), pos_tables, query_base, query_heads)
    gathered, early = ring_gather(chunk, order, early, source_of)
    positions, pos_tables, query_base, query_heads = early
    latent_part = gathered[:, :KV_RANK]
    key_heads = jnp.dot(latent_part, key_weight, preferred_element_type=jnp.float32).astype(
        jnp.bfloat16
    )
    value_heads = jnp.dot(latent_part, value_weight, preferred_element_type=jnp.float32).astype(
        jnp.bfloat16
    )
    pack = jnp.concatenate([key_heads, value_heads, gathered[:, KV_RANK:]], axis=1)
    doc_at = 2 * heads_here * NOPE_DIM + ROPE_DIM

    def ends_of(source):
        return (
            source[::BLOCK_K, doc_at].astype(jnp.int32),
            source[BLOCK_K - 1 :: BLOCK_K, doc_at].astype(jnp.int32),
        )

    packs, doc_ends = [], []
    for distance in range(cycle_size - 1, 0, -1):
        route = [(i - distance, i) for i in range(cycle_size) if i - distance >= 0]
        moved = lax.ppermute(pack, "ctx", route)
        packs.append(moved)
        doc_ends.append(ends_of(moved))
    packs.append(pack)
    doc_ends.append(ends_of(pack))
    return flash(query_heads, packs, positions, pos_tables, doc_ends, query_base)


def ring_order(mesh):
    line = list(mesh.devices[(0,) * (mesh.devices.ndim - 1)].reshape(-1))
    try:
        where = {(d.coords[0], d.coords[2]): number for number, d in enumerate(line)}
        xs = sorted({key[0] for key in where})
        zs = sorted({key[1] for key in where})
        order = []
        for turn, x in enumerate(xs):
            for z in zs if turn % 2 == 0 else zs[::-1]:
                order.append(where[(x, z)])
    except (AttributeError, KeyError, IndexError, TypeError):
        return list(range(len(line)))
    if sorted(order) != list(range(len(line))):
        return list(range(len(line)))
    return order


def solution(mesh):
    placed = (
        P(("grp", "ctx"), "tp", None),
        P(("grp", "ctx", "tp"), None),
        P(("grp", "ctx", "tp")),
        P(None, "tp"),
        P(None, "tp"),
    )
    return jax.shard_map(
        functools.partial(body, order=ring_order(mesh)),
        mesh=mesh,
        in_specs=placed,
        out_specs=P(("grp", "ctx"), "tp"),
        check_vma=False,
    )
```

```python
import functools
import math

import jax
import jax.numpy as jnp
import numpy as np
from jax import lax
from jax.experimental import pallas as pl
from jax.experimental.pallas import tpu as pltpu
from jax.sharding import PartitionSpec as P

KV_RANK = 512
ROPE_DIM = 64
NOPE_DIM = 128
LANES = 128
BLOCK_Q = 512
BLOCK_K = 512
FAR = 1 << 30


def flash_kernel(
    qbase_ref, kminp_ref, kmaxp_ref, kmind_ref, kmaxd_ref,
    q_ref, *rest, sets, tiles, factor,
):
    set_refs = [rest[3 * n : 3 * n + 3] for n in range(sets)]
    o_ref = rest[3 * sets]
    qt = pl.program_id(1)
    bq = q_ref.shape[0]
    bk = BLOCK_K
    first_pos = qbase_ref[0] + qt * bq
    last_pos = first_pos + (bq - 1)
    own = (sets - 1) * tiles + qt
    first_doc = kmind_ref[own]
    last_doc = kmaxd_ref[own]
    q = q_ref[...]
    q_nope = q[:, :NOPE_DIM]
    q_rope = q[:, NOPE_DIM:]
    q_pos = first_pos + lax.broadcasted_iota(jnp.int32, (bq, 1), 0)
    q_doc = set_refs[-1][2][pl.ds(pl.multiple_of(qt * bq, bq), bq), :][:, ROPE_DIM : ROPE_DIM + 1].astype(jnp.float32)
    nt = (((1,), (1,)), ((), ()))

    m_sc, l_sc, acc_sc = rest[3 * sets + 1 :]
    m_sc[...] = jnp.full(m_sc.shape, -1e30, jnp.float32)
    l_sc[...] = jnp.zeros(l_sc.shape, jnp.float32)
    acc_sc[...] = jnp.zeros(acc_sc.shape, jnp.float32)

    def make_step(number, k_ref, v_ref, r_ref):
        def tile(masked, t):
            start = pl.multiple_of(t * bk, bk)
            keys = k_ref[pl.ds(start, bk), :]
            ropes = r_ref[pl.ds(start, bk), :]
            scores = lax.dot_general(q_nope, keys, nt, preferred_element_type=jnp.float32)
            scores = scores + lax.dot_general(
                q_rope, ropes[:, :ROPE_DIM], nt, preferred_element_type=jnp.float32
            )
            scores = scores * factor
            if masked:
                k_pos = kminp_ref[number * tiles + t] + lax.broadcasted_iota(jnp.int32, (1, bk), 1)
                k_doc = jnp.transpose(ropes.astype(jnp.float32))[ROPE_DIM : ROPE_DIM + 1, :]
                visible = (k_pos <= q_pos) & (k_doc == q_doc)
                scores = jnp.where(visible, scores, jnp.float32(-1e30))
            m_prev = m_sc[...]
            m_new = jnp.maximum(m_prev, jnp.max(scores, axis=1, keepdims=True))
            alpha = jnp.exp(m_prev - m_new)
            weights = jnp.exp(scores - m_new)
            l_sc[...] = alpha * l_sc[...] + jnp.sum(weights, axis=1, keepdims=True)
            acc_sc[...] = alpha * acc_sc[...] + jnp.dot(
                weights.astype(jnp.bfloat16),
                v_ref[pl.ds(start, bk), :],
                preferred_element_type=jnp.float32,
            )
            m_sc[...] = m_new

        def step(t, carry):
            at = number * tiles + t
            active = (
                (kminp_ref[at] <= last_pos)
                & (kmaxd_ref[at] >= first_doc)
                & (kmind_ref[at] <= last_doc)
            )
            full = (
                (kmaxp_ref[at] <= first_pos)
                & (kmind_ref[at] == last_doc)
                & (kmaxd_ref[at] == first_doc)
            )

            @pl.when(active & full)
            def _():
                tile(False, t)

            @pl.when(active & jnp.logical_not(full))
            def _():
                tile(True, t)

            return carry

        return step

    for number, refs in enumerate(set_refs):
        lax.fori_loop(0, tiles, make_step(number, *refs), 0)
    o_ref[...] = (acc_sc[...] / l_sc[...]).astype(o_ref.dtype)


def flash(query_heads, packs, positions, pos_tables, doc_ends, query_base):
    heads_here, rows, _ = query_heads.shape
    count = packs[0].shape[0]
    bq = min(BLOCK_Q, rows)
    bk = BLOCK_K
    q_tiles = rows // bq
    tiles = count // bk
    sets = len(packs)
    assert bq == bk and rows == count
    kminp, kmaxp = pos_tables
    kmind = jnp.concatenate([ends[0] for ends in doc_ends], axis=0)
    kmaxd = jnp.concatenate([ends[1] for ends in doc_ends], axis=0)

    in_specs = [pl.BlockSpec((None, bq, query_heads.shape[2]), lambda h, qt, *_: (h, qt, 0))]
    operands = [query_heads]
    for pack in packs:
        in_specs += [
            pl.BlockSpec((count, LANES), lambda h, qt, *_: (0, h)),
            pl.BlockSpec((count, LANES), lambda h, qt, *_: (0, heads_here + h)),
            pl.BlockSpec((count, LANES), lambda h, qt, *_: (0, 2 * heads_here)),
        ]
        operands += [pack, pack, pack]

    kernel = functools.partial(
        flash_kernel, sets=sets, tiles=tiles, factor=1.0 / math.sqrt(NOPE_DIM + ROPE_DIM)
    )
    grid_spec = pltpu.PrefetchScalarGridSpec(
        num_scalar_prefetch=5,
        grid=(heads_here, q_tiles),
        in_specs=in_specs,
        out_specs=pl.BlockSpec((bq, LANES), lambda h, qt, *_: (qt, h)),
        scratch_shapes=[
            pltpu.VMEM((bq, 1), jnp.float32),
            pltpu.VMEM((bq, 1), jnp.float32),
            pltpu.VMEM((bq, LANES), jnp.float32),
        ],
    )
    return pl.pallas_call(
        kernel,
        grid_spec=grid_spec,
        out_shape=jax.ShapeDtypeStruct((rows, heads_here * LANES), jnp.bfloat16),
        compiler_params=pltpu.CompilerParams(dimension_semantics=("arbitrary", "arbitrary")),
    )(query_base, kminp, kmaxp, kmind, kmaxd, *operands)


def ring_tables(order):
    count = len(order)
    place = {device: number for number, device in enumerate(order)}
    ahead = count // 2
    behind = count - 1 - ahead
    sources = [list(range(count))]
    for step in range(1, ahead + 1):
        sources.append([order[(place[d] - step) % count] for d in range(count)])
        if step <= behind:
            sources.append([order[(place[d] + step) % count] for d in range(count)])
    source_of = np.zeros((count, count), np.int32)
    slot_of = np.zeros((count, count), np.int32)
    for number, row in enumerate(sources):
        for device, source in enumerate(row):
            source_of[device, number] = source
            slot_of[device, source] = number
    me = lax.axis_index("tp")
    return jnp.asarray(source_of)[me], jnp.asarray(slot_of)[me]


def ring_gather(block, order, early, source_of):
    count = len(order)
    place = {device: number for number, device in enumerate(order)}
    forward = [(order[i], order[(i + 1) % count]) for i in range(count)]
    backward = [(order[(i + 1) % count], order[i]) for i in range(count)]
    ahead = count // 2
    behind = count - 1 - ahead
    arrived = [block]
    moving_f = block
    moving_b = block
    for step in range(1, ahead + 1):
        moving_f = lax.ppermute(moving_f, "tp", forward)
        if step <= behind:
            moving_b = lax.ppermute(moving_b, "tp", backward)
        if step == 1:
            moving_f, moving_b, early = lax.optimization_barrier((moving_f, moving_b, early))
        arrived.append(moving_f)
        if step <= behind:
            arrived.append(moving_b)
    rows = block.shape[0]
    placed = jnp.zeros((count * rows, block.shape[1]), block.dtype)
    for number, piece in enumerate(arrived):
        placed = lax.dynamic_update_slice(placed, piece, (source_of[number] * rows, 0))
    return placed, early


def body(queries, latent_rows, doc_ids, key_weight, value_weight, *, order):
    block_rows = queries.shape[0]
    chunk_rows = latent_rows.shape[0]
    chunks = block_rows // chunk_rows
    cycle_size = lax.axis_size("ctx")
    cycle_index = lax.axis_index("ctx")
    heads_here = key_weight.shape[1] // NOPE_DIM
    width = latent_rows.shape[1]
    pad = (-(width + 1)) % LANES
    lane = lax.broadcasted_iota(jnp.int32, (chunk_rows, width + 1 + pad), 1)
    widened = jnp.pad(latent_rows, ((0, 0), (0, 1 + pad)))
    chunk = jnp.where(lane == width, doc_ids.astype(jnp.bfloat16)[:, None], widened)
    source_of, slot_of = ring_tables(order)
    offsets = jnp.arange(block_rows, dtype=jnp.int32)
    positions = []
    for distance in range(cycle_size - 1, 0, -1):
        source = cycle_index - distance
        positions.append(jnp.where(source >= 0, source * block_rows + offsets, FAR))
    positions.append(cycle_index * block_rows + offsets)
    pos_tiles = jnp.concatenate(positions, axis=0).reshape(-1, BLOCK_K)
    pos_tables = (jnp.min(pos_tiles, axis=1), jnp.max(pos_tiles, axis=1))
    query_base = (cycle_index * block_rows).astype(jnp.int32).reshape(1)
    query_heads = jnp.transpose(queries, (1, 0, 2))
    early = (pos_tables, query_base, query_heads)
    gathered, early = ring_gather(chunk, order, early, source_of)
    pos_tables, query_base, query_heads = early
    latent_part = gathered[:, :KV_RANK]
    key_heads = jnp.dot(latent_part, key_weight, preferred_element_type=jnp.float32).astype(
        jnp.bfloat16
    )
    value_heads = jnp.dot(latent_part, value_weight, preferred_element_type=jnp.float32).astype(
        jnp.bfloat16
    )
    pack = jnp.concatenate([key_heads, value_heads, gathered[:, KV_RANK:]], axis=1)
    doc_at = 2 * heads_here * NOPE_DIM + ROPE_DIM

    def ends_of(source):
        return (
            source[::BLOCK_K, doc_at].astype(jnp.int32),
            source[BLOCK_K - 1 :: BLOCK_K, doc_at].astype(jnp.int32),
        )

    packs, doc_ends = [], []
    for distance in range(cycle_size - 1, 0, -1):
        route = [(i - distance, i) for i in range(cycle_size) if i - distance >= 0]
        moved = lax.ppermute(pack, "ctx", route)
        packs.append(moved)
        doc_ends.append(ends_of(moved))
    packs.append(pack)
    doc_ends.append(ends_of(pack))
    return flash(query_heads, packs, positions, pos_tables, doc_ends, query_base)


def ring_order(mesh):
    line = list(mesh.devices[(0,) * (mesh.devices.ndim - 1)].reshape(-1))
    try:
        where = {(d.coords[0], d.coords[2]): number for number, d in enumerate(line)}
        xs = sorted({key[0] for key in where})
        zs = sorted({key[1] for key in where})
        order = []
        for turn, x in enumerate(xs):
            for z in zs if turn % 2 == 0 else zs[::-1]:
                order.append(where[(x, z)])
    except (AttributeError, KeyError, IndexError, TypeError):
        return list(range(len(line)))
    if sorted(order) != list(range(len(line))):
        return list(range(len(line)))
    return order


def solution(mesh):
    placed = (
        P(("grp", "ctx"), "tp", None),
        P(("grp", "ctx", "tp"), None),
        P(("grp", "ctx", "tp")),
        P(None, "tp"),
        P(None, "tp"),
    )
    return jax.shard_map(
        functools.partial(body, order=ring_order(mesh)),
        mesh=mesh,
        in_specs=placed,
        out_specs=P(("grp", "ctx"), "tp"),
        check_vma=False,
    )
```

```python
import functools
import math

import jax
import jax.numpy as jnp
import numpy as np
from jax import lax
from jax.experimental import pallas as pl
from jax.experimental.pallas import tpu as pltpu
from jax.sharding import PartitionSpec as P

KV_RANK = 512
ROPE_DIM = 64
NOPE_DIM = 128
LANES = 128
BLOCK_Q = 512
BLOCK_K = 512
FAR = 1 << 30


def flash_kernel(
    qbase_ref, kminp_ref, kmaxp_ref, kmind_ref, kmaxd_ref,
    q_ref, *rest, sets, tiles, factor,
):
    set_refs = [rest[4 * n : 4 * n + 4] for n in range(sets)]
    o_ref = rest[4 * sets]
    qt = pl.program_id(1)
    bq = q_ref.shape[0]
    bk = BLOCK_K
    first_pos = qbase_ref[0] + qt * bq
    last_pos = first_pos + (bq - 1)
    own = (sets - 1) * tiles + qt
    first_doc = kmind_ref[own]
    last_doc = kmaxd_ref[own]
    q = q_ref[...]
    q_nope = q[:, :NOPE_DIM]
    q_rope = q[:, NOPE_DIM:]
    q_pos = first_pos + lax.broadcasted_iota(jnp.int32, (bq, 1), 0)
    q_doc = set_refs[-1][2][pl.ds(pl.multiple_of(qt * bq, bq), bq), :][:, ROPE_DIM : ROPE_DIM + 1].astype(jnp.float32)
    nt = (((1,), (1,)), ((), ()))

    m_sc, l_sc, acc_sc = rest[4 * sets + 1 :]
    m_sc[...] = jnp.full(m_sc.shape, -1e30, jnp.float32)
    l_sc[...] = jnp.zeros(l_sc.shape, jnp.float32)
    acc_sc[...] = jnp.zeros(acc_sc.shape, jnp.float32)

    def make_step(number, k_ref, v_ref, r_ref, kp_ref):
        def tile(masked, t):
            start = pl.multiple_of(t * bk, bk)
            keys = k_ref[pl.ds(start, bk), :]
            ropes = r_ref[pl.ds(start, bk), :]
            scores = lax.dot_general(q_nope, keys, nt, preferred_element_type=jnp.float32)
            scores = scores + lax.dot_general(
                q_rope, ropes[:, :ROPE_DIM], nt, preferred_element_type=jnp.float32
            )
            scores = scores * factor
            if masked:
                k_pos = kp_ref[:, pl.ds(start, bk)]
                k_doc = jnp.transpose(ropes.astype(jnp.float32))[ROPE_DIM : ROPE_DIM + 1, :]
                visible = (k_pos <= q_pos) & (k_doc == q_doc)
                scores = jnp.where(visible, scores, jnp.float32(-1e30))
            m_prev = m_sc[...]
            m_new = jnp.maximum(m_prev, jnp.max(scores, axis=1, keepdims=True))
            alpha = jnp.exp(m_prev - m_new)
            weights = jnp.exp(scores - m_new)
            l_sc[...] = alpha * l_sc[...] + jnp.sum(weights, axis=1, keepdims=True)
            acc_sc[...] = alpha * acc_sc[...] + jnp.dot(
                weights.astype(jnp.bfloat16),
                v_ref[pl.ds(start, bk), :],
                preferred_element_type=jnp.float32,
            )
            m_sc[...] = m_new

        def step(t, carry):
            at = number * tiles + t
            active = (
                (kminp_ref[at] <= last_pos)
                & (kmaxd_ref[at] >= first_doc)
                & (kmind_ref[at] <= last_doc)
            )
            full = (
                (kmaxp_ref[at] <= first_pos)
                & (kmind_ref[at] == last_doc)
                & (kmaxd_ref[at] == first_doc)
            )

            @pl.when(active & full)
            def _():
                tile(False, t)

            @pl.when(active & jnp.logical_not(full))
            def _():
                tile(True, t)

            return carry

        return step

    for number, refs in enumerate(set_refs):
        lax.fori_loop(0, tiles, make_step(number, *refs), 0)
    o_ref[...] = (acc_sc[...] / l_sc[...]).astype(o_ref.dtype)


def flash(query_heads, packs, positions, pos_tables, doc_ends, query_base):
    heads_here, rows, _ = query_heads.shape
    count = packs[0].shape[0]
    bq = min(BLOCK_Q, rows)
    bk = BLOCK_K
    q_tiles = rows // bq
    tiles = count // bk
    sets = len(packs)
    assert bq == bk and rows == count
    kminp, kmaxp = pos_tables
    kmind = jnp.concatenate([ends[0] for ends in doc_ends], axis=0)
    kmaxd = jnp.concatenate([ends[1] for ends in doc_ends], axis=0)

    in_specs = [pl.BlockSpec((None, bq, query_heads.shape[2]), lambda h, qt, *_: (h, qt, 0))]
    operands = [query_heads]
    for pack, pos in zip(packs, positions):
        in_specs += [
            pl.BlockSpec((count, LANES), lambda h, qt, *_: (0, h)),
            pl.BlockSpec((count, LANES), lambda h, qt, *_: (0, heads_here + h)),
            pl.BlockSpec((count, LANES), lambda h, qt, *_: (0, 2 * heads_here)),
            pl.BlockSpec((1, count), lambda h, qt, *_: (0, 0)),
        ]
        operands += [pack, pack, pack, pos]

    kernel = functools.partial(
        flash_kernel, sets=sets, tiles=tiles, factor=1.0 / math.sqrt(NOPE_DIM + ROPE_DIM)
    )
    grid_spec = pltpu.PrefetchScalarGridSpec(
        num_scalar_prefetch=5,
        grid=(heads_here, q_tiles),
        in_specs=in_specs,
        out_specs=pl.BlockSpec((bq, LANES), lambda h, qt, *_: (qt, h)),
        scratch_shapes=[
            pltpu.VMEM((bq, 1), jnp.float32),
            pltpu.VMEM((bq, 1), jnp.float32),
            pltpu.VMEM((bq, LANES), jnp.float32),
        ],
    )
    return pl.pallas_call(
        kernel,
        grid_spec=grid_spec,
        out_shape=jax.ShapeDtypeStruct((rows, heads_here * LANES), jnp.bfloat16),
        compiler_params=pltpu.CompilerParams(dimension_semantics=("arbitrary", "arbitrary")),
    )(query_base, kminp, kmaxp, kmind, kmaxd, *operands)


def ring_tables(order):
    count = len(order)
    place = {device: number for number, device in enumerate(order)}
    ahead = count // 2
    behind = count - 1 - ahead
    sources = [list(range(count))]
    for step in range(1, ahead + 1):
        sources.append([order[(place[d] - step) % count] for d in range(count)])
        if step <= behind:
            sources.append([order[(place[d] + step) % count] for d in range(count)])
    source_of = np.zeros((count, count), np.int32)
    slot_of = np.zeros((count, count), np.int32)
    for number, row in enumerate(sources):
        for device, source in enumerate(row):
            source_of[device, number] = source
            slot_of[device, source] = number
    me = lax.axis_index("tp")
    return jnp.asarray(source_of)[me], jnp.asarray(slot_of)[me]


def ring_gather(block, order, early, source_of):
    count = len(order)
    place = {device: number for number, device in enumerate(order)}
    forward = [(order[i], order[(i + 1) % count]) for i in range(count)]
    backward = [(order[(i + 1) % count], order[i]) for i in range(count)]
    ahead = count // 2
    behind = count - 1 - ahead
    arrived = [block]
    moving_f = block
    moving_b = block
    for step in range(1, ahead + 1):
        moving_f = lax.ppermute(moving_f, "tp", forward)
        if step <= behind:
            moving_b = lax.ppermute(moving_b, "tp", backward)
        if step == 1:
            moving_f, moving_b, early = lax.optimization_barrier((moving_f, moving_b, early))
        arrived.append(moving_f)
        if step <= behind:
            arrived.append(moving_b)
    rows = block.shape[0]
    placed = jnp.zeros((count * rows, block.shape[1]), block.dtype)
    for number in list(range(1, len(arrived))) + [0]:
        placed = lax.dynamic_update_slice(placed, arrived[number], (source_of[number] * rows, 0))
    return placed, early


def body(queries, latent_rows, doc_ids, key_weight, value_weight, *, order):
    block_rows = queries.shape[0]
    chunk_rows = latent_rows.shape[0]
    chunks = block_rows // chunk_rows
    cycle_size = lax.axis_size("ctx")
    cycle_index = lax.axis_index("ctx")
    heads_here = key_weight.shape[1] // NOPE_DIM
    width = latent_rows.shape[1]
    pad = (-(width + 1)) % LANES
    doc_column = jnp.concatenate(
        [doc_ids.astype(jnp.bfloat16)[:, None], jnp.zeros((chunk_rows, pad), jnp.bfloat16)],
        axis=1,
    )
    chunk = jnp.concatenate([latent_rows, doc_column], axis=1)
    source_of, slot_of = ring_tables(order)
    offsets = jnp.arange(block_rows, dtype=jnp.int32)
    positions = []
    for distance in range(cycle_size - 1, 0, -1):
        source = cycle_index - distance
        positions.append(jnp.where(source >= 0, source * block_rows + offsets, FAR))
    positions.append(cycle_index * block_rows + offsets)
    pos_tiles = jnp.concatenate(positions, axis=0).reshape(-1, BLOCK_K)
    pos_tables = (jnp.min(pos_tiles, axis=1), jnp.max(pos_tiles, axis=1))
    query_base = (cycle_index * block_rows).astype(jnp.int32).reshape(1)
    query_heads = jnp.transpose(queries, (1, 0, 2))
    early = (tuple(pos.reshape(1, -1) for pos in positions), pos_tables, query_base, query_heads)
    gathered, early = ring_gather(chunk, order, early, source_of)
    positions, pos_tables, query_base, query_heads = early
    latent_part = gathered[:, :KV_RANK]
    key_heads = jnp.dot(latent_part, key_weight, preferred_element_type=jnp.float32).astype(
        jnp.bfloat16
    )
    value_heads = jnp.dot(latent_part, value_weight, preferred_element_type=jnp.float32).astype(
        jnp.bfloat16
    )
    pack = jnp.concatenate([key_heads, value_heads, gathered[:, KV_RANK:]], axis=1)
    doc_at = 2 * heads_here * NOPE_DIM + ROPE_DIM

    def ends_of(source):
        return (
            source[::BLOCK_K, doc_at].astype(jnp.int32),
            source[BLOCK_K - 1 :: BLOCK_K, doc_at].astype(jnp.int32),
        )

    packs, doc_ends = [], []
    for distance in range(cycle_size - 1, 0, -1):
        route = [(i - distance, i) for i in range(cycle_size) if i - distance >= 0]
        moved = lax.ppermute(pack, "ctx", route)
        packs.append(moved)
        doc_ends.append(ends_of(moved))
    packs.append(pack)
    doc_ends.append(ends_of(pack))
    return flash(query_heads, packs, positions, pos_tables, doc_ends, query_base)


def ring_order(mesh):
    line = list(mesh.devices[(0,) * (mesh.devices.ndim - 1)].reshape(-1))
    try:
        where = {(d.coords[0], d.coords[2]): number for number, d in enumerate(line)}
        xs = sorted({key[0] for key in where})
        zs = sorted({key[1] for key in where})
        order = []
        for turn, x in enumerate(xs):
            for z in zs if turn % 2 == 0 else zs[::-1]:
                order.append(where[(x, z)])
    except (AttributeError, KeyError, IndexError, TypeError):
        return list(range(len(line)))
    if sorted(order) != list(range(len(line))):
        return list(range(len(line)))
    return order


def solution(mesh):
    placed = (
        P(("grp", "ctx"), "tp", None),
        P(("grp", "ctx", "tp"), None),
        P(("grp", "ctx", "tp")),
        P(None, "tp"),
        P(None, "tp"),
    )
    return jax.shard_map(
        functools.partial(body, order=ring_order(mesh)),
        mesh=mesh,
        in_specs=placed,
        out_specs=P(("grp", "ctx"), "tp"),
        check_vma=False,
    )
```

```python
import functools
import math

import jax
import jax.numpy as jnp
import numpy as np
from jax import lax
from jax.experimental import pallas as pl
from jax.experimental.pallas import tpu as pltpu
from jax.sharding import PartitionSpec as P

KV_RANK = 512
ROPE_DIM = 64
NOPE_DIM = 128
LANES = 128
BLOCK_Q = 512
BLOCK_K = 512
FAR = 1 << 30


def flash_kernel(
    qbase_ref, kminp_ref, kmaxp_ref, kmind_ref, kmaxd_ref,
    q_ref, *rest, sets, tiles, factor,
):
    set_refs = [rest[4 * n : 4 * n + 4] for n in range(sets)]
    o_ref = rest[4 * sets]
    qt = pl.program_id(1)
    bq = q_ref.shape[0]
    bk = BLOCK_K
    first_pos = qbase_ref[0] + qt * bq
    last_pos = first_pos + (bq - 1)
    own = (sets - 1) * tiles + qt
    first_doc = kmind_ref[own]
    last_doc = kmaxd_ref[own]
    q = q_ref[...]
    q_nope = q[:, :NOPE_DIM]
    q_rope = q[:, NOPE_DIM:]
    q_pos = first_pos + lax.broadcasted_iota(jnp.int32, (bq, 1), 0)
    q_doc = set_refs[-1][2][pl.ds(pl.multiple_of(qt * bq, bq), bq), :][:, ROPE_DIM : ROPE_DIM + 1].astype(jnp.float32)
    nt = (((1,), (1,)), ((), ()))

    m_sc, l_sc, acc_sc = rest[4 * sets + 1 :]
    m_sc[...] = jnp.full(m_sc.shape, -1e30, jnp.float32)
    l_sc[...] = jnp.zeros(l_sc.shape, jnp.float32)
    acc_sc[...] = jnp.zeros(acc_sc.shape, jnp.float32)

    def make_step(number, k_ref, v_ref, r_ref, kp_ref):
        def tile(masked, t):
            start = pl.multiple_of(t * bk, bk)
            keys = k_ref[pl.ds(start, bk), :]
            ropes = r_ref[pl.ds(start, bk), :]
            scores = lax.dot_general(q_nope, keys, nt, preferred_element_type=jnp.float32)
            scores = scores + lax.dot_general(
                q_rope, ropes[:, :ROPE_DIM], nt, preferred_element_type=jnp.float32
            )
            scores = scores * factor
            if masked:
                k_pos = kp_ref[:, pl.ds(start, bk)]
                k_doc = jnp.transpose(ropes.astype(jnp.float32))[ROPE_DIM : ROPE_DIM + 1, :]
                visible = (k_pos <= q_pos) & (k_doc == q_doc)
                scores = jnp.where(visible, scores, jnp.float32(-1e30))
            m_prev = m_sc[...]
            m_new = jnp.maximum(m_prev, jnp.max(scores, axis=1, keepdims=True))
            alpha = jnp.exp(m_prev - m_new)
            weights = jnp.exp(scores - m_new)
            l_sc[...] = alpha * l_sc[...] + jnp.sum(weights, axis=1, keepdims=True)
            acc_sc[...] = alpha * acc_sc[...] + jnp.dot(
                weights.astype(jnp.bfloat16),
                v_ref[pl.ds(start, bk), :],
                preferred_element_type=jnp.float32,
            )
            m_sc[...] = m_new

        def step(t, carry):
            at = number * tiles + t
            active = (
                (kminp_ref[at] <= last_pos)
                & (kmaxd_ref[at] >= first_doc)
                & (kmind_ref[at] <= last_doc)
            )
            full = (
                (kmaxp_ref[at] <= first_pos)
                & (kmind_ref[at] == last_doc)
                & (kmaxd_ref[at] == first_doc)
            )

            @pl.when(active & full)
            def _():
                tile(False, t)

            @pl.when(active & jnp.logical_not(full))
            def _():
                tile(True, t)

            return carry

        return step

    for number, refs in enumerate(set_refs):
        lax.fori_loop(0, tiles, make_step(number, *refs), 0)
    o_ref[...] = (acc_sc[...] / l_sc[...]).astype(o_ref.dtype)


def flash(query_heads, packs, positions, pos_tables, doc_ends, query_base):
    heads_here, rows, _ = query_heads.shape
    count = packs[0].shape[0]
    bq = min(BLOCK_Q, rows)
    bk = BLOCK_K
    q_tiles = rows // bq
    tiles = count // bk
    sets = len(packs)
    assert bq == bk and rows == count
    kminp, kmaxp = pos_tables
    kmind = jnp.concatenate([ends[0] for ends in doc_ends], axis=0)
    kmaxd = jnp.concatenate([ends[1] for ends in doc_ends], axis=0)

    in_specs = [pl.BlockSpec((None, bq, query_heads.shape[2]), lambda h, qt, *_: (h, qt, 0))]
    operands = [query_heads]
    for pack, pos in zip(packs, positions):
        in_specs += [
            pl.BlockSpec((count, LANES), lambda h, qt, *_: (0, h)),
            pl.BlockSpec((count, LANES), lambda h, qt, *_: (0, heads_here + h)),
            pl.BlockSpec((count, LANES), lambda h, qt, *_: (0, 2 * heads_here)),
            pl.BlockSpec((1, count), lambda h, qt, *_: (0, 0)),
        ]
        operands += [pack, pack, pack, pos]

    kernel = functools.partial(
        flash_kernel, sets=sets, tiles=tiles, factor=1.0 / math.sqrt(NOPE_DIM + ROPE_DIM)
    )
    grid_spec = pltpu.PrefetchScalarGridSpec(
        num_scalar_prefetch=5,
        grid=(heads_here, q_tiles),
        in_specs=in_specs,
        out_specs=pl.BlockSpec((bq, LANES), lambda h, qt, *_: (qt, h)),
        scratch_shapes=[
            pltpu.VMEM((bq, 1), jnp.float32),
            pltpu.VMEM((bq, 1), jnp.float32),
            pltpu.VMEM((bq, LANES), jnp.float32),
        ],
    )
    return pl.pallas_call(
        kernel,
        grid_spec=grid_spec,
        out_shape=jax.ShapeDtypeStruct((rows, heads_here * LANES), jnp.bfloat16),
        compiler_params=pltpu.CompilerParams(dimension_semantics=("arbitrary", "arbitrary")),
    )(query_base, kminp, kmaxp, kmind, kmaxd, *operands)


def ring_tables(order):
    count = len(order)
    place = {device: number for number, device in enumerate(order)}
    ahead = count // 2
    behind = count - 1 - ahead
    sources = [list(range(count))]
    for step in range(1, ahead + 1):
        sources.append([order[(place[d] - step) % count] for d in range(count)])
        if step <= behind:
            sources.append([order[(place[d] + step) % count] for d in range(count)])
    source_of = np.zeros((count, count), np.int32)
    slot_of = np.zeros((count, count), np.int32)
    for number, row in enumerate(sources):
        for device, source in enumerate(row):
            source_of[device, number] = source
            slot_of[device, source] = number
    me = lax.axis_index("tp")
    return jnp.asarray(source_of)[me], jnp.asarray(slot_of)[me]


def ring_gather(block, order, early, source_of):
    count = len(order)
    place = {device: number for number, device in enumerate(order)}
    forward = [(order[i], order[(i + 1) % count]) for i in range(count)]
    backward = [(order[(i + 1) % count], order[i]) for i in range(count)]
    ahead = count // 2
    behind = count - 1 - ahead
    arrived = [block]
    moving_f = block
    moving_b = block
    for step in range(1, ahead + 1):
        moving_f = lax.ppermute(moving_f, "tp", forward)
        if step <= behind:
            moving_b = lax.ppermute(moving_b, "tp", backward)
        if step == 1:
            moving_f, moving_b, early = lax.optimization_barrier((moving_f, moving_b, early))
        arrived.append(moving_f)
        if step <= behind:
            arrived.append(moving_b)
    rows = block.shape[0]
    placed = jnp.zeros((count * rows, block.shape[1]), block.dtype)
    for number in [1, 0] + list(range(2, len(arrived))):
        placed = lax.dynamic_update_slice(placed, arrived[number], (source_of[number] * rows, 0))
    return placed, early


def body(queries, latent_rows, doc_ids, key_weight, value_weight, *, order):
    block_rows = queries.shape[0]
    chunk_rows = latent_rows.shape[0]
    chunks = block_rows // chunk_rows
    cycle_size = lax.axis_size("ctx")
    cycle_index = lax.axis_index("ctx")
    heads_here = key_weight.shape[1] // NOPE_DIM
    width = latent_rows.shape[1]
    pad = (-(width + 1)) % LANES
    doc_column = jnp.concatenate(
        [doc_ids.astype(jnp.bfloat16)[:, None], jnp.zeros((chunk_rows, pad), jnp.bfloat16)],
        axis=1,
    )
    chunk = jnp.concatenate([latent_rows, doc_column], axis=1)
    source_of, slot_of = ring_tables(order)
    offsets = jnp.arange(block_rows, dtype=jnp.int32)
    positions = []
    for distance in range(cycle_size - 1, 0, -1):
        source = cycle_index - distance
        positions.append(jnp.where(source >= 0, source * block_rows + offsets, FAR))
    positions.append(cycle_index * block_rows + offsets)
    pos_tiles = jnp.concatenate(positions, axis=0).reshape(-1, BLOCK_K)
    pos_tables = (jnp.min(pos_tiles, axis=1), jnp.max(pos_tiles, axis=1))
    query_base = (cycle_index * block_rows).astype(jnp.int32).reshape(1)
    query_heads = jnp.transpose(queries, (1, 0, 2))
    early = (tuple(pos.reshape(1, -1) for pos in positions), pos_tables, query_base, query_heads)
    gathered, early = ring_gather(chunk, order, early, source_of)
    positions, pos_tables, query_base, query_heads = early
    latent_part = gathered[:, :KV_RANK]
    key_heads = jnp.dot(latent_part, key_weight, preferred_element_type=jnp.float32).astype(
        jnp.bfloat16
    )
    value_heads = jnp.dot(latent_part, value_weight, preferred_element_type=jnp.float32).astype(
        jnp.bfloat16
    )
    pack = jnp.concatenate([key_heads, value_heads, gathered[:, KV_RANK:]], axis=1)
    doc_at = 2 * heads_here * NOPE_DIM + ROPE_DIM

    def ends_of(source):
        return (
            source[::BLOCK_K, doc_at].astype(jnp.int32),
            source[BLOCK_K - 1 :: BLOCK_K, doc_at].astype(jnp.int32),
        )

    packs, doc_ends = [], []
    for distance in range(cycle_size - 1, 0, -1):
        route = [(i - distance, i) for i in range(cycle_size) if i - distance >= 0]
        moved = lax.ppermute(pack, "ctx", route)
        packs.append(moved)
        doc_ends.append(ends_of(moved))
    packs.append(pack)
    doc_ends.append(ends_of(pack))
    return flash(query_heads, packs, positions, pos_tables, doc_ends, query_base)


def ring_order(mesh):
    line = list(mesh.devices[(0,) * (mesh.devices.ndim - 1)].reshape(-1))
    try:
        where = {(d.coords[0], d.coords[2]): number for number, d in enumerate(line)}
        xs = sorted({key[0] for key in where})
        zs = sorted({key[1] for key in where})
        order = []
        for turn, x in enumerate(xs):
            for z in zs if turn % 2 == 0 else zs[::-1]:
                order.append(where[(x, z)])
    except (AttributeError, KeyError, IndexError, TypeError):
        return list(range(len(line)))
    if sorted(order) != list(range(len(line))):
        return list(range(len(line)))
    return order


def solution(mesh):
    placed = (
        P(("grp", "ctx"), "tp", None),
        P(("grp", "ctx", "tp"), None),
        P(("grp", "ctx", "tp")),
        P(None, "tp"),
        P(None, "tp"),
    )
    return jax.shard_map(
        functools.partial(body, order=ring_order(mesh)),
        mesh=mesh,
        in_specs=placed,
        out_specs=P(("grp", "ctx"), "tp"),
        check_vma=False,
    )
```
